128 devices in a mesh: wide: 32 (over x, y, core), narrow: 4 (over z).
Axes of the slice: x: 4, y: 4, z: 4, core: 2. Of those that a mesh axis runs over, the one named last changes fastest.
Arguments:
- raw_samples: bfloat16 [1024, 32, 16384], P(('wide', 'narrow')), as said below
- filter_taps: float32 [64], replicated, may hold values from -0.75 to 0.75
- tile_pairs: int32 [16, 2], replicated, may hold values from 0 to 127, as said below
- tile_owners: int32 [16], replicated, may hold values from 0 to 3, as said below
Outputs:
- correlation_stacks: float32 [32, 64, 512], P('narrow', 'wide')
The draws below stay inside these ranges and needn't reach their ends.
Inputs may be any that keep to these rules, and one draw needn't show every extreme that they name: `raw_samples`: noise samples, scaled per channel and per window. `tile_pairs`: each row is (source block, receiver block), and the two blocks differ. `tile_owners`: each owner has at most 8 tiles, and some owner has exactly 8.
All inputs are finite; a program needn't handle non-finite values.
Results may differ from the reference program's by a relative error of at most 0.0074.
Values may be sent and summed in bfloat16 or wider, within the bound.
No kernel may reach another device: no remote copies, remote signals or barrier semaphores. Data moves between devices by JAX's collectives and lax.ppermute only.
A program may use at most 128 MiB of HBM per device.

```python
import math
import jax
import jax.numpy as jnp
from jax import lax

NFFT = 4096
DECIM = 4
TAPS = 64
NBINS = 1024
SMOOTH = 63
LAGS = 512
BLK = 8
SLOTS = 8
RAW = 16384
CHANNELS = 1024
WINDOWS = 32
NBLK = 128
PAIRS = 64
TILES = 16
OWNERS = 4


def draw_raw_samples(key, part):
    keys = jax.random.split(jax.random.fold_in(key, 3), 3)
    channel_scale = jnp.exp(jax.random.uniform(keys[1], (CHANNELS, 1, 1), jnp.float32, 0.0, math.log(10.0)))
    window_scale = jnp.exp(jax.random.uniform(keys[2], (1, WINDOWS, 1), jnp.float32, 0.0, math.log(3.0)))
    noise = jax.random.normal(keys[0], (CHANNELS, WINDOWS, RAW), jnp.float32)
    return (noise * channel_scale * window_scale).astype(jnp.bfloat16)


def draw_tile_pairs(key, part):
    first_key, second_key = jax.random.split(jax.random.fold_in(key, 7))
    source = jax.random.randint(first_key, (TILES,), 0, NBLK, dtype=jnp.int32)
    offset = jax.random.randint(second_key, (TILES,), 1, NBLK, dtype=jnp.int32)
    return jnp.stack([source, (source + offset) % NBLK], axis=1).astype(jnp.int32)


def draw_tile_owners(key, part):
    keys = jax.random.split(jax.random.fold_in(key, 11), 3)
    busiest = jax.random.randint(keys[0], (), 0, OWNERS, dtype=jnp.int32)
    offsets = jax.random.randint(keys[1], (SLOTS,), 1, OWNERS, dtype=jnp.int32)
    others = (busiest + offsets) % OWNERS
    listed = jnp.concatenate([jnp.full((SLOTS,), busiest, jnp.int32), others.astype(jnp.int32)])
    order = jax.random.permutation(keys[2], TILES)
    return listed[order].astype(jnp.int32)


def centred(own_key, dims, width, bound, kind=jnp.bfloat16):
    return jnp.clip(width * jax.random.normal(own_key, dims, jnp.float32), -bound, bound).astype(kind)


def setup_inputs(seed: int = 0) -> dict:
    arg_keys = jax.random.split(jax.random.key(seed), 5)
    return {
        "raw_samples": draw_raw_samples(jax.random.fold_in(arg_keys[4], 71), 0),
        "filter_taps": centred(arg_keys[1], (TAPS,), TAPS ** -0.5, 0.75, jnp.float32),
        "tile_pairs": draw_tile_pairs(jax.random.fold_in(arg_keys[4], 71), 0),
        "tile_owners": draw_tile_owners(jax.random.fold_in(arg_keys[4], 71), 0),
    }


water_level = 0.2
epsilon = 1e-06

def fir_tables(filter_taps, block_size):
    in_rows = jnp.arange(DECIM * block_size, dtype=jnp.int32)[:, None]
    out_cols = jnp.arange(block_size, dtype=jnp.int32)[None, :]
    this_index = DECIM * out_cols + DECIM - 1 - in_rows
    last_index = this_index + DECIM * block_size
    tap_count = filter_taps.shape[0]

    def taps_at(tap_index):
        inside = (tap_index >= 0) & (tap_index < tap_count)
        values = jnp.take(filter_taps, jnp.clip(tap_index, 0, tap_count - 1))
        return jnp.where(inside, values, jnp.zeros_like(values)).astype(jnp.bfloat16)
    return (taps_at(this_index), taps_at(last_index))

def decimate(samples, filter_taps):
    row_count, row_length = samples.shape
    block_size = min(128, row_length // DECIM)
    this_table, last_table = fir_tables(filter_taps, block_size)
    segments = samples.reshape(-1, DECIM * block_size)
    current = jnp.dot(segments, this_table, preferred_element_type=jnp.float32).reshape(row_count, -1, block_size)
    spilled = jnp.dot(segments, last_table, preferred_element_type=jnp.float32).reshape(row_count, -1, block_size)
    spilled = jnp.pad(spilled[:, :-1], ((0, 0), (1, 0), (0, 0)))
    return (current + spilled).reshape(row_count, -1).astype(jnp.bfloat16)

def dft_table(point_count, bin_count):
    sample_index = jnp.arange(point_count, dtype=jnp.int32)[:, None]
    frequency = 1 + jnp.arange(bin_count, dtype=jnp.int32)[None, :]
    angle = (sample_index * frequency % point_count).astype(jnp.float32) * (2.0 * math.pi / point_count)
    return jnp.concatenate([jnp.cos(angle), -jnp.sin(angle)], axis=1).astype(jnp.bfloat16)

def lag_table(point_count, bin_count, lag_count, window_count):
    frequency = 1 + jnp.arange(bin_count, dtype=jnp.int32)[:, None]
    shifted = jnp.arange(lag_count, dtype=jnp.int32)[None, :] - lag_count // 2 + point_count
    angle = (frequency * shifted % point_count).astype(jnp.float32) * (2.0 * math.pi / point_count)
    weight = 1.0 / math.sqrt(window_count * bin_count)
    return jnp.concatenate([jnp.cos(angle) * weight, -jnp.sin(angle) * weight], axis=0)

def smoother(bin_count, span_width):
    bin_index = jnp.arange(bin_count, dtype=jnp.int32)
    nearby = (jnp.abs(bin_index[:, None] - bin_index[None, :]) <= (span_width - 1) // 2).astype(jnp.float32)
    return nearby / lax.optimization_barrier(jnp.sum(nearby, axis=0, keepdims=True))

def whiten(decimated):
    spectrum = jnp.dot(decimated, dft_table(decimated.shape[1], NBINS), preferred_element_type=jnp.float32)
    real_part = spectrum[:, :NBINS]
    imag_part = spectrum[:, NBINS:]
    magnitude = jnp.sqrt(real_part * real_part + imag_part * imag_part)
    smooth = jnp.dot(magnitude, smoother(NBINS, SMOOTH), precision=lax.Precision.HIGHEST)
    floor_level = water_level * lax.optimization_barrier(jnp.mean(smooth, axis=1, keepdims=True)) + epsilon
    factor = 1.0 / (smooth + floor_level)
    return (spectrum * jnp.concatenate([factor, factor], axis=1)).astype(jnp.bfloat16)

def cross_spectra(source, target):
    highest = lax.Precision.HIGHEST
    src_real = source[..., :NBINS]
    src_imag = source[..., NBINS:]
    dst_real = target[..., :NBINS]
    dst_imag = target[..., NBINS:]
    real_sum = jnp.einsum('wif,wjf->ijf', src_real, dst_real, precision=highest) + jnp.einsum('wif,wjf->ijf', src_imag, dst_imag, precision=highest)
    imag_sum = jnp.einsum('wif,wjf->ijf', src_real, dst_imag, precision=highest) - jnp.einsum('wif,wjf->ijf', src_imag, dst_real, precision=highest)
    pair_count = source.shape[1] * target.shape[1]
    return jnp.concatenate([real_sum.reshape(pair_count, NBINS), imag_sum.reshape(pair_count, NBINS)], axis=1)

def reference(raw_samples, filter_taps, tile_pairs, tile_owners):

    def one_window(window_index):
        samples = lax.dynamic_index_in_dim(raw_samples, window_index, 1, keepdims=False)
        return whiten(decimate(samples, filter_taps))
    spectra = lax.map(one_window, jnp.arange(WINDOWS, dtype=jnp.int32))
    lag_basis = lag_table(NFFT, NBINS, LAGS, WINDOWS)

    def one_tile(tile_row):
        source = lax.dynamic_slice_in_dim(spectra, (tile_row[0] * BLK).astype(jnp.int32), BLK, 1).astype(jnp.float32)
        target = lax.dynamic_slice_in_dim(spectra, (tile_row[1] * BLK).astype(jnp.int32), BLK, 1).astype(jnp.float32)
        return jnp.dot(cross_spectra(source, target), lag_basis, precision=lax.Precision.HIGHEST)
    correlation = lax.map(one_tile, tile_pairs)
    owner_ids = jnp.arange(OWNERS, dtype=jnp.int32)
    owned_by = tile_owners[None, :] == owner_ids[:, None]
    rank_in_owner = jnp.cumsum(owned_by.astype(jnp.int32), axis=1) - 1
    slot_ids = jnp.arange(SLOTS, dtype=jnp.int32)
    select = (owned_by[:, None, :] & (rank_in_owner[:, None, :] == slot_ids[None, :, None])).astype(jnp.float32)
    stacks = jnp.einsum('ost,tpl->ospl', select, correlation, precision=lax.Precision.HIGHEST)
    return stacks.reshape(OWNERS * SLOTS, PAIRS, LAGS)
```

```python
import math

import jax
import jax.numpy as jnp
from jax import lax
from jax.sharding import PartitionSpec as P

NFFT = 4096
DECIM = 4
NBINS = 1024
SMOOTH = 63
LAGS = 512
BLK = 8
SLOTS = 8
TAPS = 64

water_level = 0.2
epsilon = 1e-06


def fir_table(filter_taps, block_size):
    in_rows = jnp.arange(DECIM * block_size, dtype=jnp.int32)[:, None]
    out_cols = jnp.arange(block_size, dtype=jnp.int32)[None, :]
    this_index = DECIM * out_cols + DECIM - 1 - in_rows
    index = jnp.concatenate([this_index, this_index + DECIM * block_size], axis=1)
    taps = filter_taps.astype(jnp.bfloat16)
    table = jnp.zeros(index.shape, jnp.bfloat16)
    for k in range(filter_taps.shape[0]):
        table = jnp.where(index == k, taps[k], table)
    return lax.optimization_barrier(table)


def decimate(samples, filter_taps):
    row_count, row_length = samples.shape
    block_size = min(128, row_length // DECIM)
    table = fir_table(filter_taps, block_size)
    segments = samples.reshape(-1, DECIM * block_size)
    both = jnp.dot(segments, table, preferred_element_type=jnp.float32).reshape(
        row_count, -1, 2 * block_size
    )
    current = both[:, :, :block_size]
    spilled = both[:, :, block_size:]
    spilled = jnp.pad(spilled[:, :-1], ((0, 0), (1, 0), (0, 0)))
    return (current + spilled).reshape(row_count, -1).astype(jnp.bfloat16)


def trig(index, modulus):
    angle = (index % modulus).astype(jnp.float32) * (2.0 * math.pi / modulus)
    return jnp.cos(angle), jnp.sin(angle)


def dft_table_t(point_count, bin_count, group):
    split = 64
    hi = jnp.arange(point_count // split, dtype=jnp.int32)[None, :]
    lo = jnp.arange(split, dtype=jnp.int32)[None, :]
    frequency = 1 + jnp.arange(bin_count, dtype=jnp.int32)[:, None]
    c1, s1 = trig(frequency * hi * split, point_count)
    c2, s2 = trig(frequency * lo, point_count)
    cos_t = c1[:, :, None] * c2[:, None, :] - s1[:, :, None] * s2[:, None, :]
    sin_t = s1[:, :, None] * c2[:, None, :] + c1[:, :, None] * s2[:, None, :]
    slices = bin_count // group
    cos_t = cos_t.reshape(slices, 1, group, point_count)
    sin_t = sin_t.reshape(slices, 1, group, point_count)
    table = jnp.concatenate([cos_t, -sin_t], axis=1)
    return table.reshape(2 * bin_count, point_count).astype(jnp.bfloat16)


def lag_table_p(point_count, bin_count, lag_count, window_count, group):
    split = 64
    frequency = 1 + jnp.arange(bin_count, dtype=jnp.int32)[:, None]
    hi = jnp.arange(lag_count // split, dtype=jnp.int32)[None, :]
    lo = jnp.arange(split, dtype=jnp.int32)[None, :]
    c1, s1 = trig(frequency * (point_count - lag_count // 2 + split * hi), point_count)
    c2, s2 = trig(frequency * lo, point_count)
    cos_l = c1[:, :, None] * c2[:, None, :] - s1[:, :, None] * s2[:, None, :]
    sin_l = s1[:, :, None] * c2[:, None, :] + c1[:, :, None] * s2[:, None, :]
    weight = 1.0 / math.sqrt(window_count * bin_count)
    slices = bin_count // group
    cos_l = cos_l.reshape(slices, 1, group, lag_count) * weight
    sin_l = sin_l.reshape(slices, 1, group, lag_count) * weight
    return jnp.concatenate([cos_l, -sin_l], axis=1).reshape(slices, 2 * group, lag_count)


def smoother(bin_count, span_width):
    bin_index = jnp.arange(bin_count, dtype=jnp.int32)
    nearby = (jnp.abs(bin_index[:, None] - bin_index[None, :]) <= (span_width - 1) // 2).astype(
        jnp.float32
    )
    return nearby / jnp.sum(nearby, axis=0, keepdims=True)


def whiten_t(decimated, slices, group):
    rows = decimated.shape[0]
    basis_t = dft_table_t(decimated.shape[1], NBINS, group)
    spec = lax.dot_general(
        basis_t, decimated, (((1,), (1,)), ((), ())), preferred_element_type=jnp.float32
    ).reshape(slices, 2, group, rows)
    real_part = spec[:, 0].reshape(NBINS, rows)
    imag_part = spec[:, 1].reshape(NBINS, rows)
    magnitude = jnp.sqrt(real_part * real_part + imag_part * imag_part)
    smooth = lax.dot_general(
        smoother(NBINS, SMOOTH),
        magnitude,
        (((0,), (0,)), ((), ())),
        precision=lax.Precision.HIGHEST,
    )
    floor_level = water_level * jnp.mean(smooth, axis=0, keepdims=True) + epsilon
    factor = (1.0 / (smooth + floor_level)).reshape(slices, 1, group, rows)
    return (spec * factor).astype(jnp.bfloat16).reshape(slices, 2 * group, rows)


def on_device(raw_samples, filter_taps, tile_pairs, tile_owners):
    wide_count = lax.axis_size("wide")
    narrow_count = lax.axis_size("narrow")
    devices = wide_count * narrow_count
    chan_dev, window_total, _ = raw_samples.shape
    assert chan_dev == BLK
    group = NBINS // devices
    rows = chan_dev * window_total

    decimated = decimate(raw_samples.reshape(rows, -1), filter_taps)
    whitened = whiten_t(decimated, devices, group)
    spectra = lax.all_to_all(whitened, ("wide", "narrow"), 0, 0, tiled=True)

    source = jnp.take(spectra, tile_pairs[:, 0], axis=0)
    target = jnp.take(spectra, tile_pairs[:, 1], axis=0)
    tiles = tile_pairs.shape[0]
    source = source.reshape(tiles, 2, group, BLK, window_total)
    target = target.reshape(tiles, 2, group, BLK, window_total)
    src_real, src_imag = source[:, 0], source[:, 1]
    dst_real, dst_imag = target[:, 0], target[:, 1]

    def mm(a, b):
        return jnp.einsum("tbiw,tbjw->tbij", a, b, preferred_element_type=jnp.float32)

    real_sum = mm(src_real, dst_real) + mm(src_imag, dst_imag)
    imag_sum = mm(src_real, dst_imag) - mm(src_imag, dst_real)
    cross = jnp.stack([real_sum, imag_sum], axis=1)
    pair_share = BLK * BLK // wide_count
    cross = cross.reshape(tiles, 2 * group, BLK * BLK // pair_share, pair_share)
    cross = jnp.transpose(cross, (0, 2, 3, 1))

    slot_ids = jnp.arange(SLOTS, dtype=jnp.int32)
    owner_ids = jnp.arange(narrow_count, dtype=jnp.int32)
    owned_all = tile_owners[None, :] == owner_ids[:, None]
    rank_all = jnp.cumsum(owned_all.astype(jnp.int32), axis=1) - 1
    select_all = (owned_all[:, None, :] & (rank_all[:, None, :] == slot_ids[None, :, None])).astype(
        jnp.float32
    )
    send = jnp.einsum("nst,twqv->wnsqv", select_all, cross, precision=lax.Precision.HIGHEST)
    send = send.reshape(devices, SLOTS * pair_share * 2 * group)
    arrived = lax.all_to_all(send, ("wide", "narrow"), 0, 0, tiled=True)
    arrived = arrived.reshape(devices, SLOTS, pair_share, 2 * group)
    lag_basis = lag_table_p(NFFT, NBINS, LAGS, window_total, group)
    return jnp.einsum("dsqv,dvl->sql", arrived, lag_basis, precision=lax.Precision.HIGHEST)


def solution(mesh):
    in_specs = (P(("wide", "narrow"), None, None), P(), P(), P())
    out_specs = P("narrow", "wide", None)
    return jax.shard_map(
        on_device, mesh=mesh, in_specs=in_specs, out_specs=out_specs, check_vma=False
    )
```

```python
import math

import jax
import jax.numpy as jnp
from jax import lax
from jax.experimental import pallas as pl
from jax.experimental.pallas import tpu as pltpu
from jax.sharding import PartitionSpec as P

NFFT = 4096
DECIM = 4
NBINS = 1024
SMOOTH = 63
LAGS = 512
BLK = 8
SLOTS = 8
TAPS = 64

water_level = 0.2
epsilon = 1e-06


def fir_table(filter_taps, block_size):
    taps = filter_taps.astype(jnp.bfloat16)
    span = filter_taps.shape[0] // DECIM
    cols = 2 * block_size
    width = cols + 1
    phase = taps.reshape(span, DECIM)[:, ::-1].T
    padded = jnp.pad(phase, ((0, 0), (0, width - span)))
    shifted = jnp.tile(padded, (1, block_size))[:, : block_size * cols]
    shifted = shifted.reshape(DECIM, block_size, cols)
    return jnp.transpose(shifted, (1, 0, 2)).reshape(DECIM * block_size, cols)


def decimate(samples, filter_taps):
    row_count, row_length = samples.shape
    block_size = min(128, row_length // DECIM)
    table = fir_table(filter_taps, block_size)
    segments = samples.reshape(-1, DECIM * block_size)
    both = jnp.dot(segments, table, preferred_element_type=jnp.float32).reshape(
        row_count, -1, 2 * block_size
    )
    current = both[:, :, :block_size]
    spilled = both[:, :, block_size:]
    spilled = jnp.pad(spilled[:, :-1], ((0, 0), (1, 0), (0, 0)))
    return (current + spilled).reshape(row_count, -1).astype(jnp.bfloat16)


def trig(index, modulus):
    angle = (index % modulus).astype(jnp.float32) * (2.0 * math.pi / modulus)
    return jnp.cos(angle), jnp.sin(angle)


LO = 128


def dft_factors(point_count, bin_count, group):
    hi = jnp.arange(point_count // LO, dtype=jnp.int32)[None, :]
    lo = jnp.arange(LO, dtype=jnp.int32)[None, :]
    frequency = 1 + jnp.arange(bin_count, dtype=jnp.int32)[:, None]
    c1, s1 = trig(frequency * hi * LO, point_count)
    c2, s2 = trig(frequency * lo, point_count)
    slices = bin_count // group

    def rows(real_rows, imag_rows):
        width = real_rows.shape[1]
        real_rows = real_rows.reshape(slices, 1, group, width)
        imag_rows = imag_rows.reshape(slices, 1, group, width)
        return jnp.concatenate([real_rows, imag_rows], axis=1).reshape(2 * bin_count, width)

    return rows(c1, -s1), rows(-s1, -c1), rows(c2, c2), rows(s2, s2)


def dft_kernel(p_ref, q_ref, c_ref, s_ref, dec_ref, out_ref, tab_ref):
    c2 = c_ref[...]
    s2 = s_ref[...]
    p_all = p_ref[...]
    q_all = q_ref[...]
    for hi in range(p_ref.shape[1]):
        value = p_all[:, hi : hi + 1] * c2 + q_all[:, hi : hi + 1] * s2
        tab_ref[:, hi * LO : (hi + 1) * LO] = value.astype(jnp.bfloat16)
    out_ref[...] = lax.dot_general(
        tab_ref[...], dec_ref[...], (((1,), (1,)), ((), ())), preferred_element_type=jnp.float32
    )


def dft_t(decimated, group, block_rows=256):
    rows, points = decimated.shape
    p, q, c, s = dft_factors(points, NBINS, group)
    out_rows = p.shape[0]
    hi_count = p.shape[1]
    return pl.pallas_call(
        dft_kernel,
        grid=(out_rows // block_rows,),
        in_specs=[
            pl.BlockSpec((block_rows, hi_count), lambda i: (i, 0)),
            pl.BlockSpec((block_rows, hi_count), lambda i: (i, 0)),
            pl.BlockSpec((block_rows, LO), lambda i: (i, 0)),
            pl.BlockSpec((block_rows, LO), lambda i: (i, 0)),
            pl.BlockSpec((rows, points), lambda i: (0, 0)),
        ],
        out_specs=pl.BlockSpec((block_rows, rows), lambda i: (i, 0)),
        out_shape=jax.ShapeDtypeStruct((out_rows, rows), jnp.float32),
        scratch_shapes=[pltpu.VMEM((block_rows, points), jnp.bfloat16)],
    )(p, q, c, s, decimated)


def lag_transform(cross, point_count, lag_count, window_count):
    split = 64
    pairs, _, bin_count = cross.shape
    frequency = 1 + jnp.arange(bin_count, dtype=jnp.int32)
    hi = jnp.arange(lag_count // split, dtype=jnp.int32)[:, None]
    lo = jnp.arange(split, dtype=jnp.int32)[None, :]
    ca, sa = trig(frequency[None, :] * (point_count - lag_count // 2 + split * hi), point_count)
    cb, sb = trig(frequency[:, None] * lo, point_count)
    weight = 1.0 / math.sqrt(window_count * bin_count)
    xr = cross[:, 0][:, None, :]
    xi = cross[:, 1][:, None, :]
    u = xr * ca[None] - xi * sa[None]
    v = xr * sa[None] + xi * ca[None]
    uv = jnp.concatenate([u, v], axis=2).reshape(pairs * (lag_count // split), 2 * bin_count)
    table = jnp.concatenate([cb, -sb], axis=0) * weight
    out = jnp.dot(uv, table, precision=lax.Precision.HIGHEST)
    return out.reshape(pairs, lag_count)


def smoother(bin_count, span_width):
    bin_index = jnp.arange(bin_count, dtype=jnp.int32)
    nearby = (jnp.abs(bin_index[:, None] - bin_index[None, :]) <= (span_width - 1) // 2).astype(
        jnp.float32
    )
    return nearby / jnp.sum(nearby, axis=0, keepdims=True)


def whiten_t(decimated, slices, group):
    rows = decimated.shape[0]
    spec = dft_t(decimated, group).reshape(slices, 2, group, rows)
    real_part = spec[:, 0].reshape(NBINS, rows)
    imag_part = spec[:, 1].reshape(NBINS, rows)
    magnitude = jnp.sqrt(real_part * real_part + imag_part * imag_part)
    smooth = lax.dot_general(
        smoother(NBINS, SMOOTH),
        magnitude,
        (((0,), (0,)), ((), ())),
        precision=lax.Precision.HIGHEST,
    )
    floor_level = water_level * jnp.mean(smooth, axis=0, keepdims=True) + epsilon
    factor = (1.0 / (smooth + floor_level)).reshape(slices, 1, group, rows)
    return (spec * factor).astype(jnp.bfloat16).reshape(slices, 2 * group, rows)


def on_device(raw_samples, filter_taps, tile_pairs, tile_owners):
    wide_count = lax.axis_size("wide")
    narrow_count = lax.axis_size("narrow")
    devices = wide_count * narrow_count
    chan_dev, window_total, _ = raw_samples.shape
    assert chan_dev == BLK
    group = NBINS // devices
    rows = chan_dev * window_total

    decimated = decimate(raw_samples.reshape(rows, -1), filter_taps)
    whitened = whiten_t(decimated, devices, group)
    spectra = lax.all_to_all(whitened, ("wide", "narrow"), 0, 0, tiled=True)

    source = jnp.take(spectra, tile_pairs[:, 0], axis=0)
    target = jnp.take(spectra, tile_pairs[:, 1], axis=0)
    tiles = tile_pairs.shape[0]
    source = source.reshape(tiles, 2, group, BLK, window_total)
    target = target.reshape(tiles, 2, group, BLK, window_total)
    src_real, src_imag = source[:, 0], source[:, 1]
    dst_real, dst_imag = target[:, 0], target[:, 1]

    def mm(a, b):
        return jnp.einsum("tbiw,tbjw->tbij", a, b, preferred_element_type=jnp.float32)

    real_sum = mm(src_real, dst_real) + mm(src_imag, dst_imag)
    imag_sum = mm(src_real, dst_imag) - mm(src_imag, dst_real)
    cross = jnp.stack([real_sum, imag_sum], axis=1)
    pair_share = BLK * BLK // wide_count
    cross = cross.reshape(tiles, 2 * group, BLK * BLK // pair_share, pair_share)
    cross = jnp.transpose(cross, (0, 2, 3, 1))

    slot_ids = jnp.arange(SLOTS, dtype=jnp.int32)
    owner_ids = jnp.arange(narrow_count, dtype=jnp.int32)
    owned_all = tile_owners[None, :] == owner_ids[:, None]
    rank_all = jnp.cumsum(owned_all.astype(jnp.int32), axis=1) - 1
    select_all = (owned_all[:, None, :] & (rank_all[:, None, :] == slot_ids[None, :, None])).astype(
        jnp.float32
    )
    send = jnp.einsum("nst,twqv->wnsqv", select_all, cross, precision=lax.Precision.HIGHEST)
    send = send.reshape(devices, SLOTS * pair_share * 2 * group)
    arrived = lax.all_to_all(send, ("wide", "narrow"), 0, 0, tiled=True)
    arrived = arrived.reshape(devices, SLOTS * pair_share, 2, group)
    arrived = jnp.transpose(arrived, (1, 2, 0, 3)).reshape(SLOTS * pair_share, 2, NBINS)
    stacked = lag_transform(arrived, NFFT, LAGS, window_total)
    return stacked.reshape(SLOTS, pair_share, LAGS)


def solution(mesh):
    in_specs = (P(("wide", "narrow"), None, None), P(), P(), P())
    out_specs = P("narrow", "wide", None)
    return jax.shard_map(
        on_device, mesh=mesh, in_specs=in_specs, out_specs=out_specs, check_vma=False
    )
```

```python
import math

import jax
import jax.numpy as jnp
from jax import lax
from jax.experimental import pallas as pl
from jax.experimental.pallas import tpu as pltpu
from jax.sharding import PartitionSpec as P

NFFT = 4096
DECIM = 4
NBINS = 1024
SMOOTH = 63
LAGS = 512
BLK = 8
SLOTS = 8
TAPS = 64

water_level = 0.2
epsilon = 1e-06


def fir_table(filter_taps, block_size):
    taps = filter_taps.astype(jnp.bfloat16)
    span = filter_taps.shape[0] // DECIM
    cols = 2 * block_size
    width = cols + 1
    phase = taps.reshape(span, DECIM)[:, ::-1].T
    padded = jnp.pad(phase, ((0, 0), (0, width - span)))
    shifted = jnp.tile(padded, (1, block_size))[:, : block_size * cols]
    shifted = shifted.reshape(DECIM, block_size, cols)
    return jnp.transpose(shifted, (1, 0, 2)).reshape(DECIM * block_size, cols)


def decim_kernel(x_ref, t_ref, o_ref, carry_ref):
    @pl.when(pl.program_id(0) == 0)
    def _():
        carry_ref[...] = jnp.zeros_like(carry_ref)

    table = t_ref[...]
    channels, windows, width = x_ref.shape
    segment = table.shape[0]
    block = table.shape[1] // 2
    for g in range(width // segment):
        x = x_ref[:, :, g * segment : (g + 1) * segment].reshape(channels * windows, segment)
        both = jnp.dot(x, table, preferred_element_type=jnp.float32)
        o_ref[:, g * block : (g + 1) * block] = (both[:, :block] + carry_ref[...]).astype(
            jnp.bfloat16
        )
        carry_ref[...] = both[:, block:]


def decimate(samples, filter_taps, chunk=2048):
    channels, windows, row_length = samples.shape
    block_size = min(128, row_length // DECIM)
    table = fir_table(filter_taps, block_size)
    rows = channels * windows
    return pl.pallas_call(
        decim_kernel,
        grid=(row_length // chunk,),
        in_specs=[
            pl.BlockSpec((channels, windows, chunk), lambda j: (0, 0, j)),
            pl.BlockSpec(table.shape, lambda j: (0, 0)),
        ],
        out_specs=pl.BlockSpec((rows, chunk // DECIM), lambda j: (0, j)),
        out_shape=jax.ShapeDtypeStruct((rows, row_length // DECIM), jnp.bfloat16),
        scratch_shapes=[pltpu.VMEM((rows, block_size), jnp.float32)],
    )(samples, table)


def trig(index, modulus):
    angle = (index % modulus).astype(jnp.float32) * (2.0 * math.pi / modulus)
    return jnp.cos(angle), jnp.sin(angle)


LO = 128


def dft_factors(point_count, bin_count, group):
    hi = jnp.arange(point_count // LO, dtype=jnp.int32)[None, :]
    lo = jnp.arange(LO, dtype=jnp.int32)[None, :]
    frequency = 1 + jnp.arange(bin_count, dtype=jnp.int32)[:, None]
    c1, s1 = trig(frequency * hi * LO, point_count)
    c2, s2 = trig(frequency * lo, point_count)
    slices = bin_count // group

    def rows(real_rows, imag_rows):
        width = real_rows.shape[1]
        real_rows = real_rows.reshape(slices, 1, group, width)
        imag_rows = imag_rows.reshape(slices, 1, group, width)
        return jnp.concatenate([real_rows, imag_rows], axis=1).reshape(2 * bin_count, width)

    return rows(c1, -s1), rows(-s1, -c1), rows(c2, c2), rows(s2, s2)


def dft_kernel(p_ref, q_ref, c_ref, s_ref, dec_ref, out_ref, tab_ref):
    c2 = c_ref[...]
    s2 = s_ref[...]
    p_all = p_ref[...]
    q_all = q_ref[...]
    for hi in range(p_ref.shape[1]):
        value = p_all[:, hi : hi + 1] * c2 + q_all[:, hi : hi + 1] * s2
        tab_ref[:, hi * LO : (hi + 1) * LO] = value.astype(jnp.bfloat16)
    out_ref[...] = lax.dot_general(
        tab_ref[...], dec_ref[...], (((1,), (1,)), ((), ())), preferred_element_type=jnp.float32
    )


def dft_t(decimated, group, block_rows=256):
    rows, points = decimated.shape
    p, q, c, s = dft_factors(points, NBINS, group)
    out_rows = p.shape[0]
    hi_count = p.shape[1]
    return pl.pallas_call(
        dft_kernel,
        grid=(out_rows // block_rows,),
        in_specs=[
            pl.BlockSpec((block_rows, hi_count), lambda i: (i, 0)),
            pl.BlockSpec((block_rows, hi_count), lambda i: (i, 0)),
            pl.BlockSpec((block_rows, LO), lambda i: (i, 0)),
            pl.BlockSpec((block_rows, LO), lambda i: (i, 0)),
            pl.BlockSpec((rows, points), lambda i: (0, 0)),
        ],
        out_specs=pl.BlockSpec((block_rows, rows), lambda i: (i, 0)),
        out_shape=jax.ShapeDtypeStruct((out_rows, rows), jnp.float32),
        scratch_shapes=[pltpu.VMEM((block_rows, points), jnp.bfloat16)],
    )(p, q, c, s, decimated)


def lag_transform(cross, point_count, lag_count, window_count):
    split = 64
    pairs, _, bin_count = cross.shape
    frequency = 1 + jnp.arange(bin_count, dtype=jnp.int32)
    hi = jnp.arange(lag_count // split, dtype=jnp.int32)[:, None]
    lo = jnp.arange(split, dtype=jnp.int32)[None, :]
    ca, sa = trig(frequency[None, :] * (point_count - lag_count // 2 + split * hi), point_count)
    cb, sb = trig(frequency[:, None] * lo, point_count)
    weight = 1.0 / math.sqrt(window_count * bin_count)
    xr = cross[:, 0][:, None, :]
    xi = cross[:, 1][:, None, :]
    u = xr * ca[None] - xi * sa[None]
    v = xr * sa[None] + xi * ca[None]
    uv = jnp.concatenate([u, v], axis=2).reshape(pairs * (lag_count // split), 2 * bin_count)
    table = jnp.concatenate([cb, -sb], axis=0) * weight
    out = jnp.dot(uv, table, precision=lax.Precision.HIGHEST)
    return out.reshape(pairs, lag_count)


def smoother(bin_count, span_width):
    bin_index = jnp.arange(bin_count, dtype=jnp.int32)
    nearby = (jnp.abs(bin_index[:, None] - bin_index[None, :]) <= (span_width - 1) // 2).astype(
        jnp.float32
    )
    return nearby / jnp.sum(nearby, axis=0, keepdims=True)


def whiten_t(decimated, slices, group):
    rows = decimated.shape[0]
    spec = dft_t(decimated, group).reshape(slices, 2, group, rows)
    real_part = spec[:, 0].reshape(NBINS, rows)
    imag_part = spec[:, 1].reshape(NBINS, rows)
    magnitude = jnp.sqrt(real_part * real_part + imag_part * imag_part)
    smooth = lax.dot_general(
        smoother(NBINS, SMOOTH),
        magnitude,
        (((0,), (0,)), ((), ())),
        precision=lax.Precision.HIGHEST,
    )
    floor_level = water_level * jnp.mean(smooth, axis=0, keepdims=True) + epsilon
    factor = (1.0 / (smooth + floor_level)).reshape(slices, 1, group, rows)
    return (spec * factor).astype(jnp.bfloat16).reshape(slices, 2 * group, rows)


def on_device(raw_samples, filter_taps, tile_pairs, tile_owners):
    wide_count = lax.axis_size("wide")
    narrow_count = lax.axis_size("narrow")
    devices = wide_count * narrow_count
    chan_dev, window_total, _ = raw_samples.shape
    assert chan_dev == BLK
    group = NBINS // devices
    rows = chan_dev * window_total

    decimated = decimate(raw_samples, filter_taps)
    whitened = whiten_t(decimated, devices, group)
    spectra = lax.all_to_all(whitened, ("wide", "narrow"), 0, 0, tiled=True)

    source = jnp.take(spectra, tile_pairs[:, 0], axis=0)
    target = jnp.take(spectra, tile_pairs[:, 1], axis=0)
    tiles = tile_pairs.shape[0]
    source = source.reshape(tiles, 2, group, BLK, window_total)
    target = target.reshape(tiles, 2, group, BLK, window_total)
    src_real, src_imag = source[:, 0], source[:, 1]
    dst_real, dst_imag = target[:, 0], target[:, 1]

    def mm(a, b):
        return jnp.einsum("tbiw,tbjw->tbij", a, b, preferred_element_type=jnp.float32)

    real_sum = mm(src_real, dst_real) + mm(src_imag, dst_imag)
    imag_sum = mm(src_real, dst_imag) - mm(src_imag, dst_real)
    cross = jnp.stack([real_sum, imag_sum], axis=1)
    pair_share = BLK * BLK // wide_count
    cross = cross.reshape(tiles, 2 * group, BLK * BLK // pair_share, pair_share)
    cross = jnp.transpose(cross, (0, 2, 3, 1))

    slot_ids = jnp.arange(SLOTS, dtype=jnp.int32)
    owner_ids = jnp.arange(narrow_count, dtype=jnp.int32)
    owned_all = tile_owners[None, :] == owner_ids[:, None]
    rank_all = jnp.cumsum(owned_all.astype(jnp.int32), axis=1) - 1
    select_all = (owned_all[:, None, :] & (rank_all[:, None, :] == slot_ids[None, :, None])).astype(
        jnp.float32
    )
    send = jnp.einsum("nst,twqv->wnsqv", select_all, cross, precision=lax.Precision.HIGHEST)
    send = send.reshape(devices, SLOTS * pair_share * 2 * group)
    arrived = lax.all_to_all(send, ("wide", "narrow"), 0, 0, tiled=True)
    arrived = arrived.reshape(devices, SLOTS * pair_share, 2, group)
    arrived = jnp.transpose(arrived, (1, 2, 0, 3)).reshape(SLOTS * pair_share, 2, NBINS)
    stacked = lag_transform(arrived, NFFT, LAGS, window_total)
    return stacked.reshape(SLOTS, pair_share, LAGS)


def solution(mesh):
    in_specs = (P(("wide", "narrow"), None, None), P(), P(), P())
    out_specs = P("narrow", "wide", None)
    return jax.shard_map(
        on_device, mesh=mesh, in_specs=in_specs, out_specs=out_specs, check_vma=False
    )
```

```python
import math

import jax
import jax.numpy as jnp
from jax import lax
from jax.experimental import pallas as pl
from jax.experimental.pallas import tpu as pltpu
from jax.sharding import PartitionSpec as P

NFFT = 4096
DECIM = 4
NBINS = 1024
SMOOTH = 63
LAGS = 512
BLK = 8
SLOTS = 8
TAPS = 64

water_level = 0.2
epsilon = 1e-06


def fir_table(filter_taps, block_size):
    taps = filter_taps.astype(jnp.bfloat16)
    span = filter_taps.shape[0] // DECIM
    cols = 2 * block_size
    width = cols + 1
    phase = taps.reshape(span, DECIM)[:, ::-1].T
    padded = jnp.pad(phase, ((0, 0), (0, width - span)))
    shifted = jnp.tile(padded, (1, block_size))[:, : block_size * cols]
    shifted = shifted.reshape(DECIM, block_size, cols)
    return jnp.transpose(shifted, (1, 0, 2)).reshape(DECIM * block_size, cols)


def decim_kernel(x_ref, t_ref, o_ref, carry_ref):
    @pl.when(pl.program_id(0) == 0)
    def _():
        carry_ref[...] = jnp.zeros_like(carry_ref)

    table = t_ref[...]
    channels, windows, width = x_ref.shape
    segment = table.shape[0]
    block = table.shape[1] // 2
    for g in range(width // segment):
        x = x_ref[:, :, g * segment : (g + 1) * segment].reshape(channels * windows, segment)
        both = jnp.dot(x, table, preferred_element_type=jnp.float32)
        o_ref[:, g * block : (g + 1) * block] = (both[:, :block] + carry_ref[...]).astype(
            jnp.bfloat16
        )
        carry_ref[...] = both[:, block:]


def decimate(samples, filter_taps, chunk=2048):
    channels, windows, row_length = samples.shape
    block_size = min(128, row_length // DECIM)
    table = fir_table(filter_taps, block_size)
    rows = channels * windows
    return pl.pallas_call(
        decim_kernel,
        grid=(row_length // chunk,),
        in_specs=[
            pl.BlockSpec((channels, windows, chunk), lambda j: (0, 0, j)),
            pl.BlockSpec(table.shape, lambda j: (0, 0)),
        ],
        out_specs=pl.BlockSpec((rows, chunk // DECIM), lambda j: (0, j)),
        out_shape=jax.ShapeDtypeStruct((rows, row_length // DECIM), jnp.bfloat16),
        scratch_shapes=[pltpu.VMEM((rows, block_size), jnp.float32)],
    )(samples, table)


def trig(index, modulus):
    angle = (index % modulus).astype(jnp.float32) * (2.0 * math.pi / modulus)
    return jnp.cos(angle), jnp.sin(angle)


LO = 128


def dft_factors(point_count, bin_count):
    hi = jnp.arange(point_count // LO, dtype=jnp.int32)[:, None]
    lo = jnp.arange(LO, dtype=jnp.int32)[:, None]
    frequency = 1 + jnp.arange(bin_count, dtype=jnp.int32)[None, :]
    c1, s1 = trig(frequency * hi * LO, point_count)
    c2, s2 = trig(frequency * lo, point_count)

    def cat(real_cols, imag_cols):
        return jnp.concatenate([real_cols, imag_cols], axis=1)

    return cat(c1, -s1), cat(-s1, -c1), cat(c2, c2), cat(s2, s2)


def dft_kernel(p_ref, q_ref, c_ref, s_ref, dec_ref, out_ref, tab_ref):
    c2 = c_ref[...]
    s2 = s_ref[...]
    for hi in range(p_ref.shape[0]):
        value = p_ref[hi : hi + 1, :] * c2 + q_ref[hi : hi + 1, :] * s2
        tab_ref[hi * LO : (hi + 1) * LO, :] = value.astype(jnp.bfloat16)
    out_ref[...] = jnp.dot(dec_ref[...], tab_ref[...], preferred_element_type=jnp.float32)


def dft(decimated, block_cols=512):
    rows, points = decimated.shape
    p, q, c, s = dft_factors(points, NBINS)
    cols = p.shape[1]
    hi_count = p.shape[0]
    return pl.pallas_call(
        dft_kernel,
        grid=(cols // block_cols,),
        in_specs=[
            pl.BlockSpec((hi_count, block_cols), lambda i: (0, i)),
            pl.BlockSpec((hi_count, block_cols), lambda i: (0, i)),
            pl.BlockSpec((LO, block_cols), lambda i: (0, i)),
            pl.BlockSpec((LO, block_cols), lambda i: (0, i)),
            pl.BlockSpec((rows, points), lambda i: (0, 0)),
        ],
        out_specs=pl.BlockSpec((rows, block_cols), lambda i: (0, i)),
        out_shape=jax.ShapeDtypeStruct((rows, cols), jnp.float32),
        scratch_shapes=[pltpu.VMEM((points, block_cols), jnp.bfloat16)],
    )(p, q, c, s, decimated)


def lag_transform(cross, point_count, lag_count, window_count):
    split = 64
    pairs, _, bin_count = cross.shape
    frequency = 1 + jnp.arange(bin_count, dtype=jnp.int32)
    hi = jnp.arange(lag_count // split, dtype=jnp.int32)[:, None]
    lo = jnp.arange(split, dtype=jnp.int32)[None, :]
    ca, sa = trig(frequency[None, :] * (point_count - lag_count // 2 + split * hi), point_count)
    cb, sb = trig(frequency[:, None] * lo, point_count)
    weight = 1.0 / math.sqrt(window_count * bin_count)
    xr = cross[:, 0][:, None, :]
    xi = cross[:, 1][:, None, :]
    u = xr * ca[None] - xi * sa[None]
    v = xr * sa[None] + xi * ca[None]
    uv = jnp.concatenate([u, v], axis=2).reshape(pairs * (lag_count // split), 2 * bin_count)
    table = jnp.concatenate([cb, -sb], axis=0) * weight
    out = jnp.dot(uv, table, precision=lax.Precision.HIGHEST)
    return out.reshape(pairs, lag_count)


def smoother(bin_count, span_width):
    bin_index = jnp.arange(bin_count, dtype=jnp.int32)
    nearby = (jnp.abs(bin_index[:, None] - bin_index[None, :]) <= (span_width - 1) // 2).astype(
        jnp.float32
    )
    return nearby / jnp.sum(nearby, axis=0, keepdims=True)


def whiten(decimated, slices, group):
    rows = decimated.shape[0]
    spectrum = dft(decimated)
    real_part = spectrum[:, :NBINS]
    imag_part = spectrum[:, NBINS:]
    magnitude = jnp.sqrt(real_part * real_part + imag_part * imag_part)
    smooth = jnp.dot(magnitude, smoother(NBINS, SMOOTH), precision=lax.Precision.HIGHEST)
    floor_level = water_level * jnp.mean(smooth, axis=1, keepdims=True) + epsilon
    factor = 1.0 / (smooth + floor_level)
    whitened = (spectrum * jnp.concatenate([factor, factor], axis=1)).astype(jnp.bfloat16)
    whitened = jnp.transpose(whitened.reshape(rows, 2, slices, group), (2, 1, 3, 0))
    return whitened.reshape(slices, 2 * group, rows)


def on_device(raw_samples, filter_taps, tile_pairs, tile_owners):
    wide_count = lax.axis_size("wide")
    narrow_count = lax.axis_size("narrow")
    devices = wide_count * narrow_count
    chan_dev, window_total, _ = raw_samples.shape
    assert chan_dev == BLK
    group = NBINS // devices
    rows = chan_dev * window_total

    decimated = decimate(raw_samples, filter_taps)
    whitened = whiten(decimated, devices, group)
    spectra = lax.all_to_all(whitened, ("wide", "narrow"), 0, 0, tiled=True)

    source = jnp.take(spectra, tile_pairs[:, 0], axis=0)
    target = jnp.take(spectra, tile_pairs[:, 1], axis=0)
    tiles = tile_pairs.shape[0]
    source = source.reshape(tiles, 2, group, BLK, window_total)
    target = target.reshape(tiles, 2, group, BLK, window_total)
    src_real, src_imag = source[:, 0], source[:, 1]
    dst_real, dst_imag = target[:, 0], target[:, 1]

    def mm(a, b):
        return jnp.einsum("tbiw,tbjw->tbij", a, b, preferred_element_type=jnp.float32)

    real_sum = mm(src_real, dst_real) + mm(src_imag, dst_imag)
    imag_sum = mm(src_real, dst_imag) - mm(src_imag, dst_real)
    cross = jnp.stack([real_sum, imag_sum], axis=1)
    pair_share = BLK * BLK // wide_count
    cross = cross.reshape(tiles, 2 * group, BLK * BLK // pair_share, pair_share)
    cross = jnp.transpose(cross, (0, 2, 3, 1))

    slot_ids = jnp.arange(SLOTS, dtype=jnp.int32)
    owner_ids = jnp.arange(narrow_count, dtype=jnp.int32)
    owned_all = tile_owners[None, :] == owner_ids[:, None]
    rank_all = jnp.cumsum(owned_all.astype(jnp.int32), axis=1) - 1
    select_all = (owned_all[:, None, :] & (rank_all[:, None, :] == slot_ids[None, :, None])).astype(
        jnp.float32
    )
    send = jnp.einsum("nst,twqv->wnsqv", select_all, cross, precision=lax.Precision.HIGHEST)
    send = send.reshape(devices, SLOTS * pair_share * 2 * group)
    arrived = lax.all_to_all(send, ("wide", "narrow"), 0, 0, tiled=True)
    arrived = arrived.reshape(devices, SLOTS * pair_share, 2, group)
    arrived = jnp.transpose(arrived, (1, 2, 0, 3)).reshape(SLOTS * pair_share, 2, NBINS)
    stacked = lag_transform(arrived, NFFT, LAGS, window_total)
    return stacked.reshape(SLOTS, pair_share, LAGS)


def solution(mesh):
    in_specs = (P(("wide", "narrow"), None, None), P(), P(), P())
    out_specs = P("narrow", "wide", None)
    return jax.shard_map(
        on_device, mesh=mesh, in_specs=in_specs, out_specs=out_specs, check_vma=False
    )
```

```python
import functools
import math

import numpy as np

import jax
import jax.numpy as jnp
from jax import lax
from jax.experimental import pallas as pl
from jax.experimental.pallas import tpu as pltpu
from jax.sharding import PartitionSpec as P

NFFT = 4096
DECIM = 4
NBINS = 1024
SMOOTH = 63
LAGS = 512
BLK = 8
SLOTS = 8
TAPS = 64

water_level = 0.2
epsilon = 1e-06


def fir_table(filter_taps, block_size):
    taps = filter_taps.astype(jnp.bfloat16)
    span = filter_taps.shape[0] // DECIM
    cols = 2 * block_size
    width = cols + 1
    phase = taps.reshape(span, DECIM)[:, ::-1].T
    padded = jnp.pad(phase, ((0, 0), (0, width - span)))
    shifted = jnp.tile(padded, (1, block_size))[:, : block_size * cols]
    shifted = shifted.reshape(DECIM, block_size, cols)
    return jnp.transpose(shifted, (1, 0, 2)).reshape(DECIM * block_size, cols)


def decim_kernel(x_ref, t_ref, o_ref, carry_ref):
    @pl.when(pl.program_id(0) == 0)
    def _():
        carry_ref[...] = jnp.zeros_like(carry_ref)

    table = t_ref[...]
    channels, windows, width = x_ref.shape
    segment = table.shape[0]
    block = table.shape[1] // 2
    for g in range(width // segment):
        x = x_ref[:, :, g * segment : (g + 1) * segment].reshape(channels * windows, segment)
        both = jnp.dot(x, table, preferred_element_type=jnp.float32)
        o_ref[:, g * block : (g + 1) * block] = (both[:, :block] + carry_ref[...]).astype(
            jnp.bfloat16
        )
        carry_ref[...] = both[:, block:]


def decimate(samples, filter_taps, chunk=2048):
    channels, windows, row_length = samples.shape
    block_size = min(128, row_length // DECIM)
    table = fir_table(filter_taps, block_size)
    rows = channels * windows
    return pl.pallas_call(
        decim_kernel,
        grid=(row_length // chunk,),
        in_specs=[
            pl.BlockSpec((channels, windows, chunk), lambda j: (0, 0, j)),
            pl.BlockSpec(table.shape, lambda j: (0, 0)),
        ],
        out_specs=pl.BlockSpec((rows, chunk // DECIM), lambda j: (0, j)),
        out_shape=jax.ShapeDtypeStruct((rows, row_length // DECIM), jnp.bfloat16),
        scratch_shapes=[pltpu.VMEM((rows, block_size), jnp.float32)],
    )(samples, table)


def trig(index, modulus):
    angle = (index % modulus).astype(jnp.float32) * (2.0 * math.pi / modulus)
    return jnp.cos(angle), jnp.sin(angle)


LO = 128


def dft_factors(point_count, bin_count):
    frequency = 1 + np.arange(bin_count, dtype=np.int64)[None, :]
    hi = np.arange(point_count // LO, dtype=np.int64)[:, None]
    lo = np.arange(LO, dtype=np.int64)[:, None]
    angle_hi = (frequency * hi * LO % point_count) * (2.0 * np.pi / point_count)
    angle_lo = (frequency * lo % point_count) * (2.0 * np.pi / point_count)
    c1, s1 = np.cos(angle_hi), np.sin(angle_hi)
    c2, s2 = np.cos(angle_lo), np.sin(angle_lo)
    return [jnp.asarray(t.astype(np.float32)) for t in (c1, s1, c2, s2)]


def dft_kernel(c1_ref, s1_ref, c2_ref, s2_ref, dec_ref, out_ref, tab_ref, *, halves):
    real = pl.program_id(0) < halves
    c1 = c1_ref[...]
    s1 = s1_ref[...]
    p = jnp.where(real, c1, -s1)
    q = jnp.where(real, -s1, -c1)
    c2 = c2_ref[...]
    s2 = s2_ref[...]
    for hi in range(p.shape[0]):
        value = p[hi : hi + 1, :] * c2 + q[hi : hi + 1, :] * s2
        tab_ref[hi * LO : (hi + 1) * LO, :] = value.astype(jnp.bfloat16)
    out_ref[...] = jnp.dot(dec_ref[...], tab_ref[...], preferred_element_type=jnp.float32)


def dft(decimated, block_cols=512):
    rows, points = decimated.shape
    c1, s1, c2, s2 = dft_factors(points, NBINS)
    hi_count = c1.shape[0]
    halves = NBINS // block_cols
    return pl.pallas_call(
        functools.partial(dft_kernel, halves=halves),
        grid=(2 * halves,),
        in_specs=[
            pl.BlockSpec((hi_count, block_cols), lambda i: (0, i % halves)),
            pl.BlockSpec((hi_count, block_cols), lambda i: (0, i % halves)),
            pl.BlockSpec((LO, block_cols), lambda i: (0, i % halves)),
            pl.BlockSpec((LO, block_cols), lambda i: (0, i % halves)),
            pl.BlockSpec((rows, points), lambda i: (0, 0)),
        ],
        out_specs=pl.BlockSpec((rows, block_cols), lambda i: (0, i)),
        out_shape=jax.ShapeDtypeStruct((rows, 2 * NBINS), jnp.float32),
        scratch_shapes=[pltpu.VMEM((points, block_cols), jnp.bfloat16)],
    )(c1, s1, c2, s2, decimated)


def lag_transform(cross, point_count, lag_count, window_count):
    split = 64
    pairs, _, bin_count = cross.shape
    frequency = 1 + jnp.arange(bin_count, dtype=jnp.int32)
    hi = jnp.arange(lag_count // split, dtype=jnp.int32)[:, None]
    lo = jnp.arange(split, dtype=jnp.int32)[None, :]
    ca, sa = trig(frequency[None, :] * (point_count - lag_count // 2 + split * hi), point_count)
    cb, sb = trig(frequency[:, None] * lo, point_count)
    weight = 1.0 / math.sqrt(window_count * bin_count)
    xr = cross[:, 0][:, None, :]
    xi = cross[:, 1][:, None, :]
    u = xr * ca[None] - xi * sa[None]
    v = xr * sa[None] + xi * ca[None]
    uv = jnp.concatenate([u, v], axis=2).reshape(pairs * (lag_count // split), 2 * bin_count)
    table = jnp.concatenate([cb, -sb], axis=0) * weight
    out = jnp.dot(uv, table, precision=lax.Precision.HIGHEST)
    return out.reshape(pairs, lag_count)


def smoother(bin_count, span_width):
    bin_index = jnp.arange(bin_count, dtype=jnp.int32)
    nearby = (jnp.abs(bin_index[:, None] - bin_index[None, :]) <= (span_width - 1) // 2).astype(
        jnp.float32
    )
    return nearby / jnp.sum(nearby, axis=0, keepdims=True)


def whiten(decimated, slices, group):
    rows = decimated.shape[0]
    spectrum = dft(decimated)
    real_part = spectrum[:, :NBINS]
    imag_part = spectrum[:, NBINS:]
    magnitude = jnp.sqrt(real_part * real_part + imag_part * imag_part)
    smooth = jnp.dot(magnitude, smoother(NBINS, SMOOTH), precision=lax.Precision.HIGH)
    floor_level = water_level * jnp.mean(smooth, axis=1, keepdims=True) + epsilon
    factor = 1.0 / (smooth + floor_level)
    whitened = (spectrum * jnp.concatenate([factor, factor], axis=1)).astype(jnp.bfloat16)
    whitened = jnp.transpose(whitened.reshape(rows, 2, slices, group), (2, 1, 3, 0))
    return whitened.reshape(slices, 2 * group, rows)


def on_device(raw_samples, filter_taps, tile_pairs, tile_owners):
    wide_count = lax.axis_size("wide")
    narrow_count = lax.axis_size("narrow")
    devices = wide_count * narrow_count
    chan_dev, window_total, _ = raw_samples.shape
    assert chan_dev == BLK
    group = NBINS // devices
    rows = chan_dev * window_total

    decimated = decimate(raw_samples, filter_taps)
    whitened = whiten(decimated, devices, group)
    spectra = lax.all_to_all(whitened, ("wide", "narrow"), 0, 0, tiled=True)

    source = jnp.take(spectra, tile_pairs[:, 0], axis=0)
    target = jnp.take(spectra, tile_pairs[:, 1], axis=0)
    tiles = tile_pairs.shape[0]
    source = source.reshape(tiles, 2, group, BLK, window_total)
    target = target.reshape(tiles, 2, group, BLK, window_total)
    src_real, src_imag = source[:, 0], source[:, 1]
    dst_real, dst_imag = target[:, 0], target[:, 1]

    def mm(a, b):
        return jnp.einsum("tbiw,tbjw->tbij", a, b, preferred_element_type=jnp.float32)

    real_sum = mm(src_real, dst_real) + mm(src_imag, dst_imag)
    imag_sum = mm(src_real, dst_imag) - mm(src_imag, dst_real)
    cross = jnp.stack([real_sum, imag_sum], axis=1).reshape(tiles, -1)

    slot_ids = jnp.arange(SLOTS, dtype=jnp.int32)
    owner_ids = jnp.arange(narrow_count, dtype=jnp.int32)
    owned_all = tile_owners[None, :] == owner_ids[:, None]
    rank_all = jnp.cumsum(owned_all.astype(jnp.int32), axis=1) - 1
    select_all = (owned_all[:, None, :] & (rank_all[:, None, :] == slot_ids[None, :, None])).astype(
        jnp.float32
    )
    slotted = jnp.dot(
        select_all.reshape(narrow_count * SLOTS, tiles), cross, precision=lax.Precision.HIGHEST
    )
    pair_share = BLK * BLK // wide_count
    slotted = slotted.reshape(
        narrow_count, SLOTS, 2, group, BLK, BLK // pair_share, pair_share
    )
    send = jnp.transpose(slotted, (4, 5, 0, 1, 2, 3, 6))
    send = send.reshape(devices, SLOTS * 2 * group * pair_share)
    arrived = lax.all_to_all(send, ("wide", "narrow"), 0, 0, tiled=True)
    arrived = arrived.reshape(devices, SLOTS, 2, group, pair_share)
    arrived = jnp.transpose(arrived, (1, 4, 2, 0, 3)).reshape(SLOTS * pair_share, 2, NBINS)
    stacked = lag_transform(arrived, NFFT, LAGS, window_total)
    return stacked.reshape(SLOTS, pair_share, LAGS)


def solution(mesh):
    in_specs = (P(("wide", "narrow"), None, None), P(), P(), P())
    out_specs = P("narrow", "wide", None)
    return jax.shard_map(
        on_device, mesh=mesh, in_specs=in_specs, out_specs=out_specs, check_vma=False
    )
```

```python
import functools
import math

import numpy as np

import jax
import jax.numpy as jnp
from jax import lax
from jax.experimental import pallas as pl
from jax.experimental.pallas import tpu as pltpu
from jax.sharding import PartitionSpec as P

NFFT = 4096
DECIM = 4
NBINS = 1024
SMOOTH = 63
LAGS = 512
BLK = 8
SLOTS = 8
TAPS = 64

water_level = 0.2
epsilon = 1e-06


def fir_table(filter_taps, block_size):
    taps = filter_taps.astype(jnp.bfloat16)
    span = filter_taps.shape[0] // DECIM
    cols = 2 * block_size
    width = cols + 1
    phase = taps.reshape(span, DECIM)[:, ::-1].T
    padded = jnp.pad(phase, ((0, 0), (0, width - span)))
    shifted = jnp.tile(padded, (1, block_size))[:, : block_size * cols]
    shifted = shifted.reshape(DECIM, block_size, cols)
    return jnp.transpose(shifted, (1, 0, 2)).reshape(DECIM * block_size, cols)


def decim_kernel(x_ref, t_ref, o_ref, carry_ref):
    @pl.when(pl.program_id(0) == 0)
    def _():
        carry_ref[...] = jnp.zeros_like(carry_ref)

    table = t_ref[...]
    channels, windows, width = x_ref.shape
    segment = table.shape[0]
    block = table.shape[1] // 2
    for g in range(width // segment):
        x = x_ref[:, :, g * segment : (g + 1) * segment].reshape(channels * windows, segment)
        both = jnp.dot(x, table, preferred_element_type=jnp.float32)
        o_ref[:, g * block : (g + 1) * block] = (both[:, :block] + carry_ref[...]).astype(
            jnp.bfloat16
        )
        carry_ref[...] = both[:, block:]


def decimate(samples, filter_taps, chunk=2048):
    channels, windows, row_length = samples.shape
    block_size = min(128, row_length // DECIM)
    table = fir_table(filter_taps, block_size)
    rows = channels * windows
    return pl.pallas_call(
        decim_kernel,
        grid=(row_length // chunk,),
        in_specs=[
            pl.BlockSpec((channels, windows, chunk), lambda j: (0, 0, j)),
            pl.BlockSpec(table.shape, lambda j: (0, 0)),
        ],
        out_specs=pl.BlockSpec((rows, chunk // DECIM), lambda j: (0, j)),
        out_shape=jax.ShapeDtypeStruct((rows, row_length // DECIM), jnp.bfloat16),
        scratch_shapes=[pltpu.VMEM((rows, block_size), jnp.float32)],
    )(samples, table)


def trig(index, modulus):
    angle = (index % modulus).astype(jnp.float32) * (2.0 * math.pi / modulus)
    return jnp.cos(angle), jnp.sin(angle)


LO = 128


def dft_factors(point_count, bin_count):
    frequency = 1 + np.arange(bin_count, dtype=np.int64)[None, :]
    hi = np.arange(point_count // LO, dtype=np.int64)[:, None]
    lo = np.arange(LO, dtype=np.int64)[:, None]
    angle_hi = (frequency * hi * LO % point_count) * (2.0 * np.pi / point_count)
    angle_lo = (frequency * lo % point_count) * (2.0 * np.pi / point_count)
    c1, s1 = np.cos(angle_hi), np.sin(angle_hi)
    c2, s2 = np.cos(angle_lo), np.sin(angle_lo)
    return [jnp.asarray(t.astype(np.float32)) for t in (c1, s1, c2, s2)]


def dft_kernel(c1_ref, s1_ref, c2_ref, s2_ref, dec_ref, out_ref, tab_ref, *, halves):
    real = pl.program_id(0) < halves
    c1 = c1_ref[...]
    s1 = s1_ref[...]
    p = jnp.where(real, c1, -s1)
    q = jnp.where(real, -s1, -c1)
    c2 = c2_ref[...]
    s2 = s2_ref[...]
    for hi in range(p.shape[0]):
        value = p[hi : hi + 1, :] * c2 + q[hi : hi + 1, :] * s2
        tab_ref[hi * LO : (hi + 1) * LO, :] = value.astype(jnp.bfloat16)
    out_ref[...] = jnp.dot(dec_ref[...], tab_ref[...], preferred_element_type=jnp.float32)


def dft(decimated, block_cols=512):
    rows, points = decimated.shape
    c1, s1, c2, s2 = dft_factors(points, NBINS)
    hi_count = c1.shape[0]
    halves = NBINS // block_cols
    return pl.pallas_call(
        functools.partial(dft_kernel, halves=halves),
        grid=(2 * halves,),
        in_specs=[
            pl.BlockSpec((hi_count, block_cols), lambda i: (0, i % halves)),
            pl.BlockSpec((hi_count, block_cols), lambda i: (0, i % halves)),
            pl.BlockSpec((LO, block_cols), lambda i: (0, i % halves)),
            pl.BlockSpec((LO, block_cols), lambda i: (0, i % halves)),
            pl.BlockSpec((rows, points), lambda i: (0, 0)),
        ],
        out_specs=pl.BlockSpec((rows, block_cols), lambda i: (0, i)),
        out_shape=jax.ShapeDtypeStruct((rows, 2 * NBINS), jnp.float32),
        scratch_shapes=[pltpu.VMEM((points, block_cols), jnp.bfloat16)],
    )(c1, s1, c2, s2, decimated)


def lag_transform(cross, point_count, lag_count, window_count):
    split = 64
    pairs, _, bin_count = cross.shape
    frequency = 1 + jnp.arange(bin_count, dtype=jnp.int32)
    hi = jnp.arange(lag_count // split, dtype=jnp.int32)[:, None]
    lo = jnp.arange(split, dtype=jnp.int32)[None, :]
    ca, sa = trig(frequency[None, :] * (point_count - lag_count // 2 + split * hi), point_count)
    cb, sb = trig(frequency[:, None] * lo, point_count)
    weight = 1.0 / math.sqrt(window_count * bin_count)
    xr = cross[:, 0][:, None, :]
    xi = cross[:, 1][:, None, :]
    u = xr * ca[None] - xi * sa[None]
    v = xr * sa[None] + xi * ca[None]
    uv = jnp.concatenate([u, v], axis=2).reshape(pairs * (lag_count // split), 2 * bin_count)
    table = jnp.concatenate([cb, -sb], axis=0) * weight
    out = jnp.dot(uv, table, precision=lax.Precision.HIGHEST)
    return out.reshape(pairs, lag_count)


def smoother(bin_count, span_width):
    bin_index = jnp.arange(bin_count, dtype=jnp.int32)
    nearby = (jnp.abs(bin_index[:, None] - bin_index[None, :]) <= (span_width - 1) // 2).astype(
        jnp.float32
    )
    return nearby / jnp.sum(nearby, axis=0, keepdims=True)


def whiten(decimated, slices, group):
    rows = decimated.shape[0]
    spectrum = dft(decimated)
    real_part = spectrum[:, :NBINS]
    imag_part = spectrum[:, NBINS:]
    magnitude = jnp.sqrt(real_part * real_part + imag_part * imag_part)
    smooth = jnp.dot(magnitude, smoother(NBINS, SMOOTH), precision=lax.Precision.HIGH)
    floor_level = water_level * jnp.mean(smooth, axis=1, keepdims=True) + epsilon
    factor = 1.0 / (smooth + floor_level)
    whitened = (spectrum * jnp.concatenate([factor, factor], axis=1)).astype(jnp.bfloat16)
    whitened = jnp.transpose(whitened.reshape(rows, 2, slices, group), (2, 1, 3, 0))
    return whitened.reshape(slices, 2 * group, rows)


def on_device(raw_samples, filter_taps, tile_pairs, tile_owners):
    wide_count = lax.axis_size("wide")
    narrow_count = lax.axis_size("narrow")
    devices = wide_count * narrow_count
    chan_dev, window_total, _ = raw_samples.shape
    assert chan_dev == BLK
    group = NBINS // devices
    rows = chan_dev * window_total

    decimated = decimate(raw_samples, filter_taps)
    whitened = whiten(decimated, devices, group)
    spectra = lax.all_to_all(whitened, ("wide", "narrow"), 0, 0, tiled=True)

    source = jnp.take(spectra, tile_pairs[:, 0], axis=0)
    target = jnp.take(spectra, tile_pairs[:, 1], axis=0)
    tiles = tile_pairs.shape[0]
    source = source.reshape(tiles, 2, group, BLK, window_total)
    target = target.reshape(tiles, 2, group, BLK, window_total)
    src_real, src_imag = source[:, 0], source[:, 1]
    dst_real, dst_imag = target[:, 0], target[:, 1]

    def mm(a, b):
        return jnp.einsum("tbiw,tbjw->tbij", a, b, preferred_element_type=jnp.float32)

    real_sum = mm(src_real, dst_real) + mm(src_imag, dst_imag)
    imag_sum = mm(src_real, dst_imag) - mm(src_imag, dst_real)
    cross = jnp.stack([real_sum, imag_sum], axis=1)
    pair_share = BLK * BLK // wide_count
    cross = cross.reshape(tiles, 2 * group, BLK * BLK // pair_share, pair_share)
    cross = jnp.transpose(cross, (0, 2, 3, 1))

    slot_ids = jnp.arange(SLOTS, dtype=jnp.int32)
    owner_ids = jnp.arange(narrow_count, dtype=jnp.int32)
    owned_all = tile_owners[None, :] == owner_ids[:, None]
    rank_all = jnp.cumsum(owned_all.astype(jnp.int32), axis=1) - 1
    select_all = (owned_all[:, None, :] & (rank_all[:, None, :] == slot_ids[None, :, None])).astype(
        jnp.float32
    )
    send = jnp.einsum("nst,twqv->wnsqv", select_all, cross, precision=lax.Precision.HIGHEST)
    send = send.reshape(devices, SLOTS * pair_share * 2 * group)
    arrived = lax.all_to_all(send, ("wide", "narrow"), 0, 0, tiled=True)
    arrived = arrived.reshape(devices, SLOTS * pair_share, 2, group)
    arrived = jnp.transpose(arrived, (1, 2, 0, 3)).reshape(SLOTS * pair_share, 2, NBINS)
    stacked = lag_transform(arrived, NFFT, LAGS, window_total)
    return stacked.reshape(SLOTS, pair_share, LAGS)


def solution(mesh):
    in_specs = (P(("wide", "narrow"), None, None), P(), P(), P())
    out_specs = P("narrow", "wide", None)
    return jax.shard_map(
        on_device, mesh=mesh, in_specs=in_specs, out_specs=out_specs, check_vma=False
    )
```

```python
import functools
import math

import numpy as np

import jax
import jax.numpy as jnp
from jax import lax
from jax.experimental import pallas as pl
from jax.experimental.pallas import tpu as pltpu
from jax.sharding import PartitionSpec as P

NFFT = 4096
DECIM = 4
NBINS = 1024
SMOOTH = 63
LAGS = 512
BLK = 8
SLOTS = 8
TAPS = 64

water_level = 0.2
epsilon = 1e-06


def fir_table(filter_taps, block_size):
    taps = filter_taps.astype(jnp.bfloat16)
    span = filter_taps.shape[0] // DECIM
    cols = 2 * block_size
    width = cols + 1
    phase = taps.reshape(span, DECIM)[:, ::-1].T
    padded = jnp.pad(phase, ((0, 0), (0, width - span)))
    shifted = jnp.tile(padded, (1, block_size))[:, : block_size * cols]
    shifted = shifted.reshape(DECIM, block_size, cols)
    return jnp.transpose(shifted, (1, 0, 2)).reshape(DECIM * block_size, cols)


def decim_kernel(x_ref, t_ref, o_ref, carry_ref):
    @pl.when(pl.program_id(0) == 0)
    def _():
        carry_ref[...] = jnp.zeros_like(carry_ref)

    table = t_ref[...]
    channels, windows, width = x_ref.shape
    segment = table.shape[0]
    block = table.shape[1] // 2
    for g in range(width // segment):
        x = x_ref[:, :, g * segment : (g + 1) * segment].reshape(channels * windows, segment)
        both = jnp.dot(x, table, preferred_element_type=jnp.float32)
        o_ref[:, g * block : (g + 1) * block] = (both[:, :block] + carry_ref[...]).astype(
            jnp.bfloat16
        )
        carry_ref[...] = both[:, block:]


def decimate(samples, filter_taps, chunk=8192):
    channels, windows, row_length = samples.shape
    block_size = min(128, row_length // DECIM)
    table = fir_table(filter_taps, block_size)
    rows = channels * windows
    return pl.pallas_call(
        decim_kernel,
        grid=(row_length // chunk,),
        in_specs=[
            pl.BlockSpec((channels, windows, chunk), lambda j: (0, 0, j)),
            pl.BlockSpec(table.shape, lambda j: (0, 0)),
        ],
        out_specs=pl.BlockSpec((rows, chunk // DECIM), lambda j: (0, j)),
        out_shape=jax.ShapeDtypeStruct((rows, row_length // DECIM), jnp.bfloat16),
        scratch_shapes=[pltpu.VMEM((rows, block_size), jnp.float32)],
    )(samples, table)


def trig(index, modulus):
    angle = (index % modulus).astype(jnp.float32) * (2.0 * math.pi / modulus)
    return jnp.cos(angle), jnp.sin(angle)


LO = 128


def dft_factors(point_count, bin_count):
    frequency = 1 + np.arange(bin_count, dtype=np.int64)[None, :]
    hi = np.arange(point_count // LO, dtype=np.int64)[:, None]
    lo = np.arange(LO, dtype=np.int64)[:, None]
    angle_hi = (frequency * hi * LO % point_count) * (2.0 * np.pi / point_count)
    angle_lo = (frequency * lo % point_count) * (2.0 * np.pi / point_count)
    c1, s1 = np.cos(angle_hi), np.sin(angle_hi)
    c2, s2 = np.cos(angle_lo), np.sin(angle_lo)
    return [jnp.asarray(t.astype(np.float32)) for t in (c1, s1, c2, s2)]


def dft_kernel(c1_ref, s1_ref, c2_ref, s2_ref, dec_ref, out_ref, tab_ref, *, halves):
    real = pl.program_id(0) < halves
    c1 = c1_ref[...]
    s1 = s1_ref[...]
    p = jnp.where(real, c1, -s1)
    q = jnp.where(real, -s1, -c1)
    c2 = c2_ref[...]
    s2 = s2_ref[...]
    for hi in range(p.shape[0]):
        value = p[hi : hi + 1, :] * c2 + q[hi : hi + 1, :] * s2
        tab_ref[hi * LO : (hi + 1) * LO, :] = value.astype(jnp.bfloat16)
    out_ref[...] = jnp.dot(dec_ref[...], tab_ref[...], preferred_element_type=jnp.float32)


def dft(decimated, block_cols=512):
    rows, points = decimated.shape
    c1, s1, c2, s2 = dft_factors(points, NBINS)
    hi_count = c1.shape[0]
    halves = NBINS // block_cols
    return pl.pallas_call(
        functools.partial(dft_kernel, halves=halves),
        grid=(2 * halves,),
        in_specs=[
            pl.BlockSpec((hi_count, block_cols), lambda i: (0, i % halves)),
            pl.BlockSpec((hi_count, block_cols), lambda i: (0, i % halves)),
            pl.BlockSpec((LO, block_cols), lambda i: (0, i % halves)),
            pl.BlockSpec((LO, block_cols), lambda i: (0, i % halves)),
            pl.BlockSpec((rows, points), lambda i: (0, 0)),
        ],
        out_specs=pl.BlockSpec((rows, block_cols), lambda i: (0, i)),
        out_shape=jax.ShapeDtypeStruct((rows, 2 * NBINS), jnp.float32),
        scratch_shapes=[pltpu.VMEM((points, block_cols), jnp.bfloat16)],
    )(c1, s1, c2, s2, decimated)


def lag_transform(cross, point_count, lag_count, window_count):
    split = 64
    pairs, _, bin_count = cross.shape
    frequency = 1 + jnp.arange(bin_count, dtype=jnp.int32)
    hi = jnp.arange(lag_count // split, dtype=jnp.int32)[:, None]
    lo = jnp.arange(split, dtype=jnp.int32)[None, :]
    ca, sa = trig(frequency[None, :] * (point_count - lag_count // 2 + split * hi), point_count)
    cb, sb = trig(frequency[:, None] * lo, point_count)
    weight = 1.0 / math.sqrt(window_count * bin_count)
    xr = cross[:, 0][:, None, :]
    xi = cross[:, 1][:, None, :]
    u = xr * ca[None] - xi * sa[None]
    v = xr * sa[None] + xi * ca[None]
    uv = jnp.concatenate([u, v], axis=2).reshape(pairs * (lag_count // split), 2 * bin_count)
    table = jnp.concatenate([cb, -sb], axis=0) * weight
    out = jnp.dot(uv, table, precision=lax.Precision.HIGHEST)
    return out.reshape(pairs, lag_count)


def smoother(bin_count, span_width):
    bin_index = jnp.arange(bin_count, dtype=jnp.int32)
    nearby = (jnp.abs(bin_index[:, None] - bin_index[None, :]) <= (span_width - 1) // 2).astype(
        jnp.float32
    )
    return nearby / jnp.sum(nearby, axis=0, keepdims=True)


def whiten(decimated, slices, group):
    rows = decimated.shape[0]
    spectrum = dft(decimated)
    real_part = spectrum[:, :NBINS]
    imag_part = spectrum[:, NBINS:]
    magnitude = jnp.sqrt(real_part * real_part + imag_part * imag_part)
    smooth = jnp.dot(magnitude, smoother(NBINS, SMOOTH), precision=lax.Precision.HIGH)
    floor_level = water_level * jnp.mean(smooth, axis=1, keepdims=True) + epsilon
    factor = 1.0 / (smooth + floor_level)
    whitened = (spectrum * jnp.concatenate([factor, factor], axis=1)).astype(jnp.bfloat16)
    whitened = jnp.transpose(whitened.reshape(rows, 2, slices, group), (2, 1, 3, 0))
    return whitened.reshape(slices, 2 * group, rows)


def on_device(raw_samples, filter_taps, tile_pairs, tile_owners):
    wide_count = lax.axis_size("wide")
    narrow_count = lax.axis_size("narrow")
    devices = wide_count * narrow_count
    chan_dev, window_total, _ = raw_samples.shape
    assert chan_dev == BLK
    group = NBINS // devices
    rows = chan_dev * window_total

    decimated = decimate(raw_samples, filter_taps)
    whitened = whiten(decimated, devices, group)
    spectra = lax.all_to_all(whitened, ("wide", "narrow"), 0, 0, tiled=True)

    source = jnp.take(spectra, tile_pairs[:, 0], axis=0)
    target = jnp.take(spectra, tile_pairs[:, 1], axis=0)
    tiles = tile_pairs.shape[0]
    source = source.reshape(tiles, 2, group, BLK, window_total)
    target = target.reshape(tiles, 2, group, BLK, window_total)
    src_real, src_imag = source[:, 0], source[:, 1]
    dst_real, dst_imag = target[:, 0], target[:, 1]

    def mm(a, b):
        return jnp.einsum("tbiw,tbjw->tbij", a, b, preferred_element_type=jnp.float32)

    real_sum = mm(src_real, dst_real) + mm(src_imag, dst_imag)
    imag_sum = mm(src_real, dst_imag) - mm(src_imag, dst_real)
    cross = jnp.stack([real_sum, imag_sum], axis=1)
    pair_share = BLK * BLK // wide_count
    cross = cross.reshape(tiles, 2 * group, BLK * BLK // pair_share, pair_share)
    cross = jnp.transpose(cross, (0, 2, 3, 1))

    slot_ids = jnp.arange(SLOTS, dtype=jnp.int32)
    owner_ids = jnp.arange(narrow_count, dtype=jnp.int32)
    owned_all = tile_owners[None, :] == owner_ids[:, None]
    rank_all = jnp.cumsum(owned_all.astype(jnp.int32), axis=1) - 1
    select_all = (owned_all[:, None, :] & (rank_all[:, None, :] == slot_ids[None, :, None])).astype(
        jnp.float32
    )
    send = jnp.einsum("nst,twqv->wnsqv", select_all, cross, precision=lax.Precision.HIGHEST)
    send = send.reshape(devices, SLOTS * pair_share * 2 * group)
    arrived = lax.all_to_all(send, ("wide", "narrow"), 0, 0, tiled=True)
    arrived = arrived.reshape(devices, SLOTS * pair_share, 2, group)
    arrived = jnp.transpose(arrived, (1, 2, 0, 3)).reshape(SLOTS * pair_share, 2, NBINS)
    stacked = lag_transform(arrived, NFFT, LAGS, window_total)
    return stacked.reshape(SLOTS, pair_share, LAGS)


def solution(mesh):
    in_specs = (P(("wide", "narrow"), None, None), P(), P(), P())
    out_specs = P("narrow", "wide", None)
    return jax.shard_map(
        on_device, mesh=mesh, in_specs=in_specs, out_specs=out_specs, check_vma=False
    )
```

```python
import functools
import math

import numpy as np

import jax
import jax.numpy as jnp
from jax import lax
from jax.experimental import pallas as pl
from jax.experimental.pallas import tpu as pltpu
from jax.sharding import PartitionSpec as P

NFFT = 4096
DECIM = 4
NBINS = 1024
SMOOTH = 63
LAGS = 512
BLK = 8
SLOTS = 8
TAPS = 64

water_level = 0.2
epsilon = 1e-06


def fir_table(filter_taps, block_size):
    taps = filter_taps.astype(jnp.bfloat16)
    span = filter_taps.shape[0] // DECIM
    cols = 2 * block_size
    width = cols + 1
    phase = taps.reshape(span, DECIM)[:, ::-1].T
    padded = jnp.pad(phase, ((0, 0), (0, width - span)))
    shifted = jnp.tile(padded, (1, block_size))[:, : block_size * cols]
    shifted = shifted.reshape(DECIM, block_size, cols)
    return jnp.transpose(shifted, (1, 0, 2)).reshape(DECIM * block_size, cols)


def decim_kernel(x_ref, t_ref, o_ref, carry_ref):
    @pl.when(pl.program_id(0) == 0)
    def _():
        carry_ref[...] = jnp.zeros_like(carry_ref)

    table = t_ref[...]
    channels, windows, width = x_ref.shape
    segment = table.shape[0]
    block = table.shape[1] // 2
    for g in range(width // segment):
        x = x_ref[:, :, g * segment : (g + 1) * segment].reshape(channels * windows, segment)
        both = jnp.dot(x, table, preferred_element_type=jnp.float32)
        o_ref[:, g * block : (g + 1) * block] = (both[:, :block] + carry_ref[...]).astype(
            jnp.bfloat16
        )
        carry_ref[...] = both[:, block:]


def decimate(samples, filter_taps, chunk=8192):
    channels, windows, row_length = samples.shape
    block_size = min(128, row_length // DECIM)
    table = fir_table(filter_taps, block_size)
    rows = channels * windows
    return pl.pallas_call(
        decim_kernel,
        grid=(row_length // chunk,),
        in_specs=[
            pl.BlockSpec((channels, windows, chunk), lambda j: (0, 0, j)),
            pl.BlockSpec(table.shape, lambda j: (0, 0)),
        ],
        out_specs=pl.BlockSpec((rows, chunk // DECIM), lambda j: (0, j)),
        out_shape=jax.ShapeDtypeStruct((rows, row_length // DECIM), jnp.bfloat16),
        scratch_shapes=[pltpu.VMEM((rows, block_size), jnp.float32)],
    )(samples, table)


def trig(index, modulus):
    angle = (index % modulus).astype(jnp.float32) * (2.0 * math.pi / modulus)
    return jnp.cos(angle), jnp.sin(angle)


LO = 128


def dft_factors(point_count, bin_count):
    frequency = 1 + np.arange(bin_count, dtype=np.int64)[None, :]
    hi = np.arange(point_count // LO, dtype=np.int64)[:, None]
    lo = np.arange(LO, dtype=np.int64)[:, None]
    angle_hi = (frequency * hi * LO % point_count) * (2.0 * np.pi / point_count)
    angle_lo = (frequency * lo % point_count) * (2.0 * np.pi / point_count)
    c1, s1 = np.cos(angle_hi), np.sin(angle_hi)
    c2, s2 = np.cos(angle_lo), np.sin(angle_lo)
    return [jnp.asarray(t.astype(np.float32)) for t in (c1, s1, c2, s2)]


def dft_kernel(c1_ref, s1_ref, c2_ref, s2_ref, dec_ref, out_ref, tab_ref, *, halves):
    real = pl.program_id(0) < halves
    c1 = c1_ref[...]
    s1 = s1_ref[...]
    p = jnp.where(real, c1, -s1)
    q = jnp.where(real, -s1, -c1)
    c2 = c2_ref[...]
    s2 = s2_ref[...]
    for hi in range(p.shape[0]):
        value = p[hi : hi + 1, :] * c2 + q[hi : hi + 1, :] * s2
        tab_ref[hi * LO : (hi + 1) * LO, :] = value.astype(jnp.bfloat16)
    out_ref[...] = jnp.dot(dec_ref[...], tab_ref[...], preferred_element_type=jnp.float32)


def dft(decimated, block_cols=512):
    rows, points = decimated.shape
    c1, s1, c2, s2 = dft_factors(points, NBINS)
    hi_count = c1.shape[0]
    halves = NBINS // block_cols
    return pl.pallas_call(
        functools.partial(dft_kernel, halves=halves),
        grid=(2 * halves,),
        in_specs=[
            pl.BlockSpec((hi_count, block_cols), lambda i: (0, i % halves)),
            pl.BlockSpec((hi_count, block_cols), lambda i: (0, i % halves)),
            pl.BlockSpec((LO, block_cols), lambda i: (0, i % halves)),
            pl.BlockSpec((LO, block_cols), lambda i: (0, i % halves)),
            pl.BlockSpec((rows, points), lambda i: (0, 0)),
        ],
        out_specs=pl.BlockSpec((rows, block_cols), lambda i: (0, i)),
        out_shape=jax.ShapeDtypeStruct((rows, 2 * NBINS), jnp.float32),
        scratch_shapes=[pltpu.VMEM((points, block_cols), jnp.bfloat16)],
    )(c1, s1, c2, s2, decimated)


def lag_transform(cross, point_count, lag_count, window_count):
    split = 64
    pairs, _, bin_count = cross.shape
    frequency = 1 + jnp.arange(bin_count, dtype=jnp.int32)
    hi = jnp.arange(lag_count // split, dtype=jnp.int32)[:, None]
    lo = jnp.arange(split, dtype=jnp.int32)[None, :]
    ca, sa = trig(frequency[None, :] * (point_count - lag_count // 2 + split * hi), point_count)
    cb, sb = trig(frequency[:, None] * lo, point_count)
    weight = 1.0 / math.sqrt(window_count * bin_count)
    xr = cross[:, 0][:, None, :]
    xi = cross[:, 1][:, None, :]
    u = xr * ca[None] - xi * sa[None]
    v = xr * sa[None] + xi * ca[None]
    uv = jnp.concatenate([u, v], axis=2).reshape(pairs * (lag_count // split), 2 * bin_count)
    table = jnp.concatenate([cb, -sb], axis=0) * weight
    out = jnp.dot(uv, table, precision=lax.Precision.HIGHEST)
    return out.reshape(pairs, lag_count)


def smoother(bin_count, span_width):
    bin_index = jnp.arange(bin_count, dtype=jnp.int32)
    nearby = (jnp.abs(bin_index[:, None] - bin_index[None, :]) <= (span_width - 1) // 2).astype(
        jnp.float32
    )
    return nearby / jnp.sum(nearby, axis=0, keepdims=True)


def whiten(decimated, slices, group):
    rows = decimated.shape[0]
    spectrum = dft(decimated)
    real_part = spectrum[:, :NBINS]
    imag_part = spectrum[:, NBINS:]
    magnitude = jnp.sqrt(real_part * real_part + imag_part * imag_part)
    smooth = jnp.dot(magnitude, smoother(NBINS, SMOOTH), precision=lax.Precision.HIGH)
    floor_level = water_level * jnp.mean(smooth, axis=1, keepdims=True) + epsilon
    factor = 1.0 / (smooth + floor_level)
    whitened = (spectrum * jnp.concatenate([factor, factor], axis=1)).astype(jnp.bfloat16)
    whitened = jnp.transpose(whitened.reshape(rows, 2, slices, group), (2, 1, 3, 0))
    return whitened.reshape(slices, 2 * group, rows)


def on_device(raw_samples, filter_taps, tile_pairs, tile_owners):
    wide_count = lax.axis_size("wide")
    narrow_count = lax.axis_size("narrow")
    devices = wide_count * narrow_count
    chan_dev, window_total, _ = raw_samples.shape
    assert chan_dev == BLK
    group = NBINS // devices
    rows = chan_dev * window_total

    decimated = decimate(raw_samples, filter_taps)
    whitened = whiten(decimated, devices, group)
    spectra = lax.all_to_all(whitened, ("wide", "narrow"), 0, 0, tiled=True)

    tiles = tile_pairs.shape[0]
    slot_ids = jnp.arange(SLOTS, dtype=jnp.int32)
    owner_ids = jnp.arange(narrow_count, dtype=jnp.int32)
    owned_all = tile_owners[None, :] == owner_ids[:, None]
    rank_all = jnp.cumsum(owned_all.astype(jnp.int32), axis=1) - 1
    select_all = owned_all[:, None, :] & (rank_all[:, None, :] == slot_ids[None, :, None])
    slot_tile = jnp.sum(select_all * jnp.arange(tiles, dtype=jnp.int32), axis=2).reshape(-1)
    live = jnp.any(select_all, axis=2).astype(jnp.float32)
    slot_pairs = jnp.take(tile_pairs, slot_tile, axis=0)
    shape = (narrow_count, SLOTS, 2, group, BLK, window_total)
    source = jnp.take(spectra, slot_pairs[:, 0], axis=0).reshape(shape)
    target = jnp.take(spectra, slot_pairs[:, 1], axis=0).reshape(shape)
    src_real, src_imag = source[:, :, 0], source[:, :, 1]
    dst_real, dst_imag = target[:, :, 0], target[:, :, 1]

    def mm(a, b):
        return jnp.einsum("nsbiw,nsbjw->nijsb", a, b, preferred_element_type=jnp.float32)

    real_sum = mm(src_real, dst_real) + mm(src_imag, dst_imag)
    imag_sum = mm(src_real, dst_imag) - mm(src_imag, dst_real)
    cross = jnp.stack([real_sum, imag_sum], axis=4) * live[:, None, None, :, None, None]
    pair_share = BLK * BLK // wide_count
    send = cross.reshape(devices, pair_share * SLOTS * 2 * group)
    arrived = lax.all_to_all(send, ("narrow", "wide"), 0, 0, tiled=True)
    arrived = arrived.reshape(narrow_count, wide_count, pair_share, SLOTS, 2, group)
    arrived = jnp.transpose(arrived, (3, 2, 4, 1, 0, 5)).reshape(SLOTS * pair_share, 2, NBINS)
    stacked = lag_transform(arrived, NFFT, LAGS, window_total)
    return stacked.reshape(SLOTS, pair_share, LAGS)


def solution(mesh):
    in_specs = (P(("wide", "narrow"), None, None), P(), P(), P())
    out_specs = P("narrow", "wide", None)
    return jax.shard_map(
        on_device, mesh=mesh, in_specs=in_specs, out_specs=out_specs, check_vma=False
    )
```

```python
import functools
import math

import numpy as np

import jax
import jax.numpy as jnp
from jax import lax
from jax.experimental import pallas as pl
from jax.experimental.pallas import tpu as pltpu
from jax.sharding import PartitionSpec as P

NFFT = 4096
DECIM = 4
NBINS = 1024
SMOOTH = 63
LAGS = 512
BLK = 8
SLOTS = 8
TAPS = 64

water_level = 0.2
epsilon = 1e-06


def fir_table(filter_taps, block_size):
    taps = filter_taps.astype(jnp.bfloat16)
    span = filter_taps.shape[0] // DECIM
    cols = 2 * block_size
    width = cols + 1
    phase = taps.reshape(span, DECIM)[:, ::-1].T
    padded = jnp.pad(phase, ((0, 0), (0, width - span)))
    shifted = jnp.tile(padded, (1, block_size))[:, : block_size * cols]
    shifted = shifted.reshape(DECIM, block_size, cols)
    return jnp.transpose(shifted, (1, 0, 2)).reshape(DECIM * block_size, cols)


def decim_kernel(x_ref, t_ref, o_ref, carry_ref):
    @pl.when(pl.program_id(0) == 0)
    def _():
        carry_ref[...] = jnp.zeros_like(carry_ref)

    table = t_ref[...]
    channels, windows, width = x_ref.shape
    segment = table.shape[0]
    block = table.shape[1] // 2
    for g in range(width // segment):
        x = x_ref[:, :, g * segment : (g + 1) * segment].reshape(channels * windows, segment)
        both = jnp.dot(x, table, preferred_element_type=jnp.float32)
        o_ref[:, g * block : (g + 1) * block] = (both[:, :block] + carry_ref[...]).astype(
            jnp.bfloat16
        )
        carry_ref[...] = both[:, block:]


def decimate(samples, filter_taps, chunk=8192):
    channels, windows, row_length = samples.shape
    block_size = min(128, row_length // DECIM)
    table = fir_table(filter_taps, block_size)
    rows = channels * windows
    return pl.pallas_call(
        decim_kernel,
        grid=(row_length // chunk,),
        in_specs=[
            pl.BlockSpec((channels, windows, chunk), lambda j: (0, 0, j)),
            pl.BlockSpec(table.shape, lambda j: (0, 0)),
        ],
        out_specs=pl.BlockSpec((rows, chunk // DECIM), lambda j: (0, j)),
        out_shape=jax.ShapeDtypeStruct((rows, row_length // DECIM), jnp.bfloat16),
        scratch_shapes=[pltpu.VMEM((rows, block_size), jnp.float32)],
    )(samples, table)


def trig(index, modulus):
    angle = (index % modulus).astype(jnp.float32) * (2.0 * math.pi / modulus)
    return jnp.cos(angle), jnp.sin(angle)


LO = 128


def dft_factors(point_count, bin_count):
    frequency = 1 + np.arange(bin_count, dtype=np.int64)[None, :]
    hi = np.arange(point_count // LO, dtype=np.int64)[:, None]
    lo = np.arange(LO, dtype=np.int64)[:, None]
    angle_hi = (frequency * hi * LO % point_count) * (2.0 * np.pi / point_count)
    angle_lo = (frequency * lo % point_count) * (2.0 * np.pi / point_count)
    c1, s1 = np.cos(angle_hi), np.sin(angle_hi)
    c2, s2 = np.cos(angle_lo), np.sin(angle_lo)
    return [jnp.asarray(t.astype(np.float32)) for t in (c1, s1, c2, s2)]


def dft_kernel(c1_ref, s1_ref, c2_ref, s2_ref, dec_ref, out_ref, tab_ref, *, halves):
    real = pl.program_id(0) < halves
    c1 = c1_ref[...]
    s1 = s1_ref[...]
    p = jnp.where(real, c1, -s1)
    q = jnp.where(real, -s1, -c1)
    c2 = c2_ref[...]
    s2 = s2_ref[...]
    for hi in range(p.shape[0]):
        value = p[hi : hi + 1, :] * c2 + q[hi : hi + 1, :] * s2
        tab_ref[hi * LO : (hi + 1) * LO, :] = value.astype(jnp.bfloat16)
    out_ref[...] = jnp.dot(dec_ref[...], tab_ref[...], preferred_element_type=jnp.float32)


def dft(decimated, block_cols=512):
    rows, points = decimated.shape
    c1, s1, c2, s2 = dft_factors(points, NBINS)
    hi_count = c1.shape[0]
    halves = NBINS // block_cols
    return pl.pallas_call(
        functools.partial(dft_kernel, halves=halves),
        grid=(2 * halves,),
        in_specs=[
            pl.BlockSpec((hi_count, block_cols), lambda i: (0, i % halves)),
            pl.BlockSpec((hi_count, block_cols), lambda i: (0, i % halves)),
            pl.BlockSpec((LO, block_cols), lambda i: (0, i % halves)),
            pl.BlockSpec((LO, block_cols), lambda i: (0, i % halves)),
            pl.BlockSpec((rows, points), lambda i: (0, 0)),
        ],
        out_specs=pl.BlockSpec((rows, block_cols), lambda i: (0, i)),
        out_shape=jax.ShapeDtypeStruct((rows, 2 * NBINS), jnp.float32),
        scratch_shapes=[pltpu.VMEM((points, block_cols), jnp.bfloat16)],
    )(c1, s1, c2, s2, decimated)


def lag_transform(cross, point_count, lag_count, window_count):
    split = 64
    pairs, _, bin_count = cross.shape
    frequency = 1 + jnp.arange(bin_count, dtype=jnp.int32)
    hi = jnp.arange(lag_count // split, dtype=jnp.int32)[:, None]
    lo = jnp.arange(split, dtype=jnp.int32)[None, :]
    ca, sa = trig(frequency[None, :] * (point_count - lag_count // 2 + split * hi), point_count)
    cb, sb = trig(frequency[:, None] * lo, point_count)
    weight = 1.0 / math.sqrt(window_count * bin_count)
    xr = cross[:, 0][:, None, :]
    xi = cross[:, 1][:, None, :]
    u = xr * ca[None] - xi * sa[None]
    v = xr * sa[None] + xi * ca[None]
    uv = jnp.concatenate([u, v], axis=2).reshape(pairs * (lag_count // split), 2 * bin_count)
    table = jnp.concatenate([cb, -sb], axis=0) * weight
    out = jnp.dot(uv, table, precision=lax.Precision.HIGHEST)
    return out.reshape(pairs, lag_count)


def smoother(bin_count, span_width):
    bin_index = jnp.arange(bin_count, dtype=jnp.int32)
    nearby = (jnp.abs(bin_index[:, None] - bin_index[None, :]) <= (span_width - 1) // 2).astype(
        jnp.float32
    )
    return nearby / jnp.sum(nearby, axis=0, keepdims=True)


def fused_kernel(x_ref, t_ref, c1_ref, s1_ref, c2_ref, s2_ref, out_ref, carry_ref, dec_ref, tab_ref,
                 *, dec_steps, halves):
    i = pl.program_id(0)

    @pl.when(i == 0)
    def _():
        carry_ref[...] = jnp.zeros_like(carry_ref)

    @pl.when(i < dec_steps)
    def _():
        table = t_ref[...]
        channels, windows, width = x_ref.shape
        segment = table.shape[0]
        block = table.shape[1] // 2
        per_step = width // segment
        for g in range(per_step):
            x = x_ref[:, :, g * segment : (g + 1) * segment].reshape(channels * windows, segment)
            both = jnp.dot(x, table, preferred_element_type=jnp.float32)
            col = pl.multiple_of((i * per_step + g) * block, block)
            dec_ref[:, pl.ds(col, block)] = (both[:, :block] + carry_ref[...]).astype(jnp.bfloat16)
            carry_ref[...] = both[:, block:]

    @pl.when(i >= dec_steps)
    def _():
        real = i - dec_steps < halves
        c1 = c1_ref[...]
        s1 = s1_ref[...]
        p = jnp.where(real, c1, -s1)
        q = jnp.where(real, -s1, -c1)
        c2 = c2_ref[...]
        s2 = s2_ref[...]
        for hi in range(p.shape[0]):
            value = p[hi : hi + 1, :] * c2 + q[hi : hi + 1, :] * s2
            tab_ref[hi * LO : (hi + 1) * LO, :] = value.astype(jnp.bfloat16)
        out_ref[...] = jnp.dot(dec_ref[...], tab_ref[...], preferred_element_type=jnp.float32)


def decimate_dft(samples, filter_taps, chunk=8192, block_cols=512):
    channels, windows, row_length = samples.shape
    block_size = min(128, row_length // DECIM)
    table = fir_table(filter_taps, block_size)
    rows = channels * windows
    points = row_length // DECIM
    c1, s1, c2, s2 = dft_factors(points, NBINS)
    hi_count = c1.shape[0]
    halves = NBINS // block_cols
    dec_steps = row_length // chunk

    def raw_map(i):
        return (0, 0, jnp.minimum(i, dec_steps - 1))

    def factor_map(i):
        return (0, jnp.maximum(i - dec_steps, 0) % halves)

    def out_map(i):
        return (0, jnp.maximum(i - dec_steps, 0))

    return pl.pallas_call(
        functools.partial(fused_kernel, dec_steps=dec_steps, halves=halves),
        grid=(dec_steps + 2 * halves,),
        in_specs=[
            pl.BlockSpec((channels, windows, chunk), raw_map),
            pl.BlockSpec(table.shape, lambda i: (0, 0)),
            pl.BlockSpec((hi_count, block_cols), factor_map),
            pl.BlockSpec((hi_count, block_cols), factor_map),
            pl.BlockSpec((LO, block_cols), factor_map),
            pl.BlockSpec((LO, block_cols), factor_map),
        ],
        out_specs=pl.BlockSpec((rows, block_cols), out_map),
        out_shape=jax.ShapeDtypeStruct((rows, 2 * NBINS), jnp.float32),
        scratch_shapes=[
            pltpu.VMEM((rows, block_size), jnp.float32),
            pltpu.VMEM((rows, points), jnp.bfloat16),
            pltpu.VMEM((points, block_cols), jnp.bfloat16),
        ],
    )(samples, table, c1, s1, c2, s2)


def whiten(spectrum, slices, group):
    rows = spectrum.shape[0]
    real_part = spectrum[:, :NBINS]
    imag_part = spectrum[:, NBINS:]
    magnitude = jnp.sqrt(real_part * real_part + imag_part * imag_part)
    smooth = jnp.dot(magnitude, smoother(NBINS, SMOOTH), precision=lax.Precision.HIGH)
    floor_level = water_level * jnp.mean(smooth, axis=1, keepdims=True) + epsilon
    factor = 1.0 / (smooth + floor_level)
    whitened = (spectrum * jnp.concatenate([factor, factor], axis=1)).astype(jnp.bfloat16)
    whitened = jnp.transpose(whitened.reshape(rows, 2, slices, group), (2, 1, 3, 0))
    return whitened.reshape(slices, 2 * group, rows)


def on_device(raw_samples, filter_taps, tile_pairs, tile_owners):
    wide_count = lax.axis_size("wide")
    narrow_count = lax.axis_size("narrow")
    devices = wide_count * narrow_count
    chan_dev, window_total, _ = raw_samples.shape
    assert chan_dev == BLK
    group = NBINS // devices
    rows = chan_dev * window_total

    whitened = whiten(decimate_dft(raw_samples, filter_taps), devices, group)
    spectra = lax.all_to_all(whitened, ("wide", "narrow"), 0, 0, tiled=True)

    source = jnp.take(spectra, tile_pairs[:, 0], axis=0)
    target = jnp.take(spectra, tile_pairs[:, 1], axis=0)
    tiles = tile_pairs.shape[0]
    source = source.reshape(tiles, 2, group, BLK, window_total)
    target = target.reshape(tiles, 2, group, BLK, window_total)
    src_real, src_imag = source[:, 0], source[:, 1]
    dst_real, dst_imag = target[:, 0], target[:, 1]

    def mm(a, b):
        return jnp.einsum("tbiw,tbjw->tbij", a, b, preferred_element_type=jnp.float32)

    real_sum = mm(src_real, dst_real) + mm(src_imag, dst_imag)
    imag_sum = mm(src_real, dst_imag) - mm(src_imag, dst_real)
    cross = jnp.stack([real_sum, imag_sum], axis=1)
    pair_share = BLK * BLK // wide_count
    cross = cross.reshape(tiles, 2 * group, BLK * BLK // pair_share, pair_share)
    cross = jnp.transpose(cross, (0, 2, 3, 1))

    slot_ids = jnp.arange(SLOTS, dtype=jnp.int32)
    owner_ids = jnp.arange(narrow_count, dtype=jnp.int32)
    owned_all = tile_owners[None, :] == owner_ids[:, None]
    rank_all = jnp.cumsum(owned_all.astype(jnp.int32), axis=1) - 1
    select_all = (owned_all[:, None, :] & (rank_all[:, None, :] == slot_ids[None, :, None])).astype(
        jnp.float32
    )
    send = jnp.einsum("nst,twqv->wnsqv", select_all, cross, precision=lax.Precision.HIGHEST)
    send = send.reshape(devices, SLOTS * pair_share * 2 * group)
    arrived = lax.all_to_all(send, ("wide", "narrow"), 0, 0, tiled=True)
    arrived = arrived.reshape(devices, SLOTS * pair_share, 2, group)
    arrived = jnp.transpose(arrived, (1, 2, 0, 3)).reshape(SLOTS * pair_share, 2, NBINS)
    stacked = lag_transform(arrived, NFFT, LAGS, window_total)
    return stacked.reshape(SLOTS, pair_share, LAGS)


def solution(mesh):
    in_specs = (P(("wide", "narrow"), None, None), P(), P(), P())
    out_specs = P("narrow", "wide", None)
    return jax.shard_map(
        on_device, mesh=mesh, in_specs=in_specs, out_specs=out_specs, check_vma=False
    )
```

```python
import functools
import math

import numpy as np

import jax
import jax.numpy as jnp
from jax import lax
from jax.experimental import pallas as pl
from jax.experimental.pallas import tpu as pltpu
from jax.sharding import PartitionSpec as P

NFFT = 4096
DECIM = 4
NBINS = 1024
SMOOTH = 63
LAGS = 512
BLK = 8
SLOTS = 8
TAPS = 64

water_level = 0.2
epsilon = 1e-06


def fir_table(filter_taps, block_size):
    taps = filter_taps.astype(jnp.bfloat16)
    span = filter_taps.shape[0] // DECIM
    cols = 2 * block_size
    width = cols + 1
    phase = taps.reshape(span, DECIM)[:, ::-1].T
    padded = jnp.pad(phase, ((0, 0), (0, width - span)))
    shifted = jnp.tile(padded, (1, block_size))[:, : block_size * cols]
    shifted = shifted.reshape(DECIM, block_size, cols)
    return jnp.transpose(shifted, (1, 0, 2)).reshape(DECIM * block_size, cols)


def decim_kernel(x_ref, t_ref, o_ref, carry_ref):
    @pl.when(pl.program_id(0) == 0)
    def _():
        carry_ref[...] = jnp.zeros_like(carry_ref)

    table = t_ref[...]
    channels, windows, width = x_ref.shape
    segment = table.shape[0]
    block = table.shape[1] // 2
    for g in range(width // segment):
        x = x_ref[:, :, g * segment : (g + 1) * segment].reshape(channels * windows, segment)
        both = jnp.dot(x, table, preferred_element_type=jnp.float32)
        o_ref[:, g * block : (g + 1) * block] = (both[:, :block] + carry_ref[...]).astype(
            jnp.bfloat16
        )
        carry_ref[...] = both[:, block:]


def decimate(samples, filter_taps, chunk=8192):
    channels, windows, row_length = samples.shape
    block_size = min(128, row_length // DECIM)
    table = fir_table(filter_taps, block_size)
    rows = channels * windows
    return pl.pallas_call(
        decim_kernel,
        grid=(row_length // chunk,),
        in_specs=[
            pl.BlockSpec((channels, windows, chunk), lambda j: (0, 0, j)),
            pl.BlockSpec(table.shape, lambda j: (0, 0)),
        ],
        out_specs=pl.BlockSpec((rows, chunk // DECIM), lambda j: (0, j)),
        out_shape=jax.ShapeDtypeStruct((rows, row_length // DECIM), jnp.bfloat16),
        scratch_shapes=[pltpu.VMEM((rows, block_size), jnp.float32)],
    )(samples, table)


def trig(index, modulus):
    angle = (index % modulus).astype(jnp.float32) * (2.0 * math.pi / modulus)
    return jnp.cos(angle), jnp.sin(angle)


LO = 128


def dft_factors(point_count, bin_count):
    frequency = 1 + np.arange(bin_count, dtype=np.int64)[None, :]
    hi = np.arange(point_count // LO, dtype=np.int64)[:, None]
    lo = np.arange(LO, dtype=np.int64)[:, None]
    angle_hi = (frequency * hi * LO % point_count) * (2.0 * np.pi / point_count)
    angle_lo = (frequency * lo % point_count) * (2.0 * np.pi / point_count)
    c1, s1 = np.cos(angle_hi), np.sin(angle_hi)
    c2, s2 = np.cos(angle_lo), np.sin(angle_lo)
    return [jnp.asarray(t.astype(np.float32)) for t in (c1, s1, c2, s2)]


def dft_kernel(c1_ref, s1_ref, c2_ref, s2_ref, dec_ref, out_ref, tab_ref, *, halves):
    real = pl.program_id(0) < halves
    c1 = c1_ref[...]
    s1 = s1_ref[...]
    p = jnp.where(real, c1, -s1)
    q = jnp.where(real, -s1, -c1)
    c2 = c2_ref[...]
    s2 = s2_ref[...]
    for hi in range(p.shape[0]):
        value = p[hi : hi + 1, :] * c2 + q[hi : hi + 1, :] * s2
        tab_ref[hi * LO : (hi + 1) * LO, :] = value.astype(jnp.bfloat16)
    out_ref[...] = jnp.dot(dec_ref[...], tab_ref[...], preferred_element_type=jnp.float32)


def dft(decimated, block_cols=512):
    rows, points = decimated.shape
    c1, s1, c2, s2 = dft_factors(points, NBINS)
    hi_count = c1.shape[0]
    halves = NBINS // block_cols
    return pl.pallas_call(
        functools.partial(dft_kernel, halves=halves),
        grid=(2 * halves,),
        in_specs=[
            pl.BlockSpec((hi_count, block_cols), lambda i: (0, i % halves)),
            pl.BlockSpec((hi_count, block_cols), lambda i: (0, i % halves)),
            pl.BlockSpec((LO, block_cols), lambda i: (0, i % halves)),
            pl.BlockSpec((LO, block_cols), lambda i: (0, i % halves)),
            pl.BlockSpec((rows, points), lambda i: (0, 0)),
        ],
        out_specs=pl.BlockSpec((rows, block_cols), lambda i: (0, i)),
        out_shape=jax.ShapeDtypeStruct((rows, 2 * NBINS), jnp.float32),
        scratch_shapes=[pltpu.VMEM((points, block_cols), jnp.bfloat16)],
    )(c1, s1, c2, s2, decimated)


def lag_transform(cross, point_count, lag_count, window_count):
    split = 64
    pairs, _, bin_count = cross.shape
    frequency = 1 + jnp.arange(bin_count, dtype=jnp.int32)
    hi = jnp.arange(lag_count // split, dtype=jnp.int32)[:, None]
    lo = jnp.arange(split, dtype=jnp.int32)[None, :]
    ca, sa = trig(frequency[None, :] * (point_count - lag_count // 2 + split * hi), point_count)
    cb, sb = trig(frequency[:, None] * lo, point_count)
    weight = 1.0 / math.sqrt(window_count * bin_count)
    xr = cross[:, 0][:, None, :]
    xi = cross[:, 1][:, None, :]
    u = xr * ca[None] - xi * sa[None]
    v = xr * sa[None] + xi * ca[None]
    uv = jnp.concatenate([u, v], axis=2).reshape(pairs * (lag_count // split), 2 * bin_count)
    table = jnp.concatenate([cb, -sb], axis=0) * weight
    out = jnp.dot(uv, table, precision=lax.Precision.HIGHEST)
    return out.reshape(pairs, lag_count)


def smoother(bin_count, span_width):
    bin_index = jnp.arange(bin_count, dtype=jnp.int32)
    nearby = (jnp.abs(bin_index[:, None] - bin_index[None, :]) <= (span_width - 1) // 2).astype(
        jnp.float32
    )
    return nearby / jnp.sum(nearby, axis=0, keepdims=True)


def fused_kernel(taps_ref, x_ref, c1_ref, s1_ref, c2_ref, s2_ref, out_ref, carry_ref, fir_ref, dec_ref,
                 tab_ref, *, dec_steps, halves):
    i = pl.program_id(0)

    @pl.when(i == 0)
    def _():
        carry_ref[...] = jnp.zeros_like(carry_ref)
        shape = fir_ref.shape
        row = lax.broadcasted_iota(jnp.int32, shape, 0)
        phase = row % DECIM
        offset = lax.broadcasted_iota(jnp.int32, shape, 1) - row // DECIM
        table = jnp.zeros(shape, jnp.float32)
        for m in range(taps_ref.shape[0] // DECIM):
            value = jnp.full(shape, taps_ref[DECIM * m], jnp.float32)
            for b in range(DECIM - 1):
                value = jnp.where(phase == b, taps_ref[DECIM * m + DECIM - 1 - b], value)
            table = jnp.where(offset == m, value, table)
        fir_ref[...] = table.astype(jnp.bfloat16)

    @pl.when(i < dec_steps)
    def _():
        table = fir_ref[...]
        channels, windows, width = x_ref.shape
        segment = table.shape[0]
        block = table.shape[1] // 2
        per_step = width // segment
        for g in range(per_step):
            x = x_ref[:, :, g * segment : (g + 1) * segment].reshape(channels * windows, segment)
            both = jnp.dot(x, table, preferred_element_type=jnp.float32)
            col = pl.multiple_of((i * per_step + g) * block, block)
            dec_ref[:, pl.ds(col, block)] = (both[:, :block] + carry_ref[...]).astype(jnp.bfloat16)
            carry_ref[...] = both[:, block:]

    @pl.when(i >= dec_steps)
    def _():
        real = i - dec_steps < halves
        c1 = c1_ref[...]
        s1 = s1_ref[...]
        p = jnp.where(real, c1, -s1)
        q = jnp.where(real, -s1, -c1)
        c2 = c2_ref[...]
        s2 = s2_ref[...]
        for hi in range(p.shape[0]):
            value = p[hi : hi + 1, :] * c2 + q[hi : hi + 1, :] * s2
            tab_ref[hi * LO : (hi + 1) * LO, :] = value.astype(jnp.bfloat16)
        out_ref[...] = jnp.dot(dec_ref[...], tab_ref[...], preferred_element_type=jnp.float32)


def decimate_dft(samples, filter_taps, chunk=8192, block_cols=512):
    channels, windows, row_length = samples.shape
    block_size = min(128, row_length // DECIM)
    rows = channels * windows
    points = row_length // DECIM
    c1, s1, c2, s2 = dft_factors(points, NBINS)
    hi_count = c1.shape[0]
    halves = NBINS // block_cols
    dec_steps = row_length // chunk

    def raw_map(i):
        return (0, 0, jnp.minimum(i, dec_steps - 1))

    def factor_map(i):
        return (0, jnp.maximum(i - dec_steps, 0) % halves)

    def out_map(i):
        return (0, jnp.maximum(i - dec_steps, 0))

    return pl.pallas_call(
        functools.partial(fused_kernel, dec_steps=dec_steps, halves=halves),
        grid=(dec_steps + 2 * halves,),
        in_specs=[
            pl.BlockSpec(memory_space=pltpu.SMEM),
            pl.BlockSpec((channels, windows, chunk), raw_map),
            pl.BlockSpec((hi_count, block_cols), factor_map),
            pl.BlockSpec((hi_count, block_cols), factor_map),
            pl.BlockSpec((LO, block_cols), factor_map),
            pl.BlockSpec((LO, block_cols), factor_map),
        ],
        out_specs=pl.BlockSpec((rows, block_cols), out_map),
        out_shape=jax.ShapeDtypeStruct((rows, 2 * NBINS), jnp.float32),
        scratch_shapes=[
            pltpu.VMEM((rows, block_size), jnp.float32),
            pltpu.VMEM((DECIM * block_size, 2 * block_size), jnp.bfloat16),
            pltpu.VMEM((rows, points), jnp.bfloat16),
            pltpu.VMEM((points, block_cols), jnp.bfloat16),
        ],
    )(filter_taps, samples, c1, s1, c2, s2)


def whiten(spectrum, slices, group):
    rows = spectrum.shape[0]
    real_part = spectrum[:, :NBINS]
    imag_part = spectrum[:, NBINS:]
    magnitude = jnp.sqrt(real_part * real_part + imag_part * imag_part)
    smooth = jnp.dot(magnitude, smoother(NBINS, SMOOTH), precision=lax.Precision.HIGH)
    floor_level = water_level * jnp.mean(smooth, axis=1, keepdims=True) + epsilon
    factor = 1.0 / (smooth + floor_level)
    whitened = (spectrum * jnp.concatenate([factor, factor], axis=1)).astype(jnp.bfloat16)
    whitened = jnp.transpose(whitened.reshape(rows, 2, slices, group), (2, 1, 3, 0))
    return whitened.reshape(slices, 2 * group, rows)


def on_device(raw_samples, filter_taps, tile_pairs, tile_owners):
    wide_count = lax.axis_size("wide")
    narrow_count = lax.axis_size("narrow")
    devices = wide_count * narrow_count
    chan_dev, window_total, _ = raw_samples.shape
    assert chan_dev == BLK
    group = NBINS // devices
    rows = chan_dev * window_total

    whitened = whiten(decimate_dft(raw_samples, filter_taps), devices, group)
    spectra = lax.all_to_all(whitened, ("wide", "narrow"), 0, 0, tiled=True)

    source = jnp.take(spectra, tile_pairs[:, 0], axis=0)
    target = jnp.take(spectra, tile_pairs[:, 1], axis=0)
    tiles = tile_pairs.shape[0]
    source = source.reshape(tiles, 2, group, BLK, window_total)
    target = target.reshape(tiles, 2, group, BLK, window_total)
    src_real, src_imag = source[:, 0], source[:, 1]
    dst_real, dst_imag = target[:, 0], target[:, 1]

    def mm(a, b):
        return jnp.einsum("tbiw,tbjw->tbij", a, b, preferred_element_type=jnp.float32)

    real_sum = mm(src_real, dst_real) + mm(src_imag, dst_imag)
    imag_sum = mm(src_real, dst_imag) - mm(src_imag, dst_real)
    cross = jnp.stack([real_sum, imag_sum], axis=1)
    pair_share = BLK * BLK // wide_count
    cross = cross.reshape(tiles, 2 * group, BLK * BLK // pair_share, pair_share)
    cross = jnp.transpose(cross, (0, 2, 3, 1))

    slot_ids = jnp.arange(SLOTS, dtype=jnp.int32)
    owner_ids = jnp.arange(narrow_count, dtype=jnp.int32)
    owned_all = tile_owners[None, :] == owner_ids[:, None]
    rank_all = jnp.cumsum(owned_all.astype(jnp.int32), axis=1) - 1
    select_all = (owned_all[:, None, :] & (rank_all[:, None, :] == slot_ids[None, :, None])).astype(
        jnp.float32
    )
    send = jnp.einsum("nst,twqv->wnsqv", select_all, cross, precision=lax.Precision.HIGHEST)
    send = send.reshape(devices, SLOTS * pair_share * 2 * group)
    arrived = lax.all_to_all(send, ("wide", "narrow"), 0, 0, tiled=True)
    arrived = arrived.reshape(devices, SLOTS * pair_share, 2, group)
    arrived = jnp.transpose(arrived, (1, 2, 0, 3)).reshape(SLOTS * pair_share, 2, NBINS)
    stacked = lag_transform(arrived, NFFT, LAGS, window_total)
    return stacked.reshape(SLOTS, pair_share, LAGS)


def solution(mesh):
    in_specs = (P(("wide", "narrow"), None, None), P(), P(), P())
    out_specs = P("narrow", "wide", None)
    return jax.shard_map(
        on_device, mesh=mesh, in_specs=in_specs, out_specs=out_specs, check_vma=False
    )
```

```python
import functools
import math

import numpy as np

import jax
import jax.numpy as jnp
from jax import lax
from jax.experimental import pallas as pl
from jax.experimental.pallas import tpu as pltpu
from jax.sharding import PartitionSpec as P

NFFT = 4096
DECIM = 4
NBINS = 1024
SMOOTH = 63
LAGS = 512
BLK = 8
SLOTS = 8
TAPS = 64

water_level = 0.2
epsilon = 1e-06


def fir_table(filter_taps, block_size):
    taps = filter_taps.astype(jnp.bfloat16)
    span = filter_taps.shape[0] // DECIM
    cols = 2 * block_size
    width = cols + 1
    phase = taps.reshape(span, DECIM)[:, ::-1].T
    padded = jnp.pad(phase, ((0, 0), (0, width - span)))
    shifted = jnp.tile(padded, (1, block_size))[:, : block_size * cols]
    shifted = shifted.reshape(DECIM, block_size, cols)
    return jnp.transpose(shifted, (1, 0, 2)).reshape(DECIM * block_size, cols)


def decim_kernel(x_ref, t_ref, o_ref, carry_ref):
    @pl.when(pl.program_id(0) == 0)
    def _():
        carry_ref[...] = jnp.zeros_like(carry_ref)

    table = t_ref[...]
    channels, windows, width = x_ref.shape
    segment = table.shape[0]
    block = table.shape[1] // 2
    for g in range(width // segment):
        x = x_ref[:, :, g * segment : (g + 1) * segment].reshape(channels * windows, segment)
        both = jnp.dot(x, table, preferred_element_type=jnp.float32)
        o_ref[:, g * block : (g + 1) * block] = (both[:, :block] + carry_ref[...]).astype(
            jnp.bfloat16
        )
        carry_ref[...] = both[:, block:]


def decimate(samples, filter_taps, chunk=8192):
    channels, windows, row_length = samples.shape
    block_size = min(128, row_length // DECIM)
    table = fir_table(filter_taps, block_size)
    rows = channels * windows
    return pl.pallas_call(
        decim_kernel,
        grid=(row_length // chunk,),
        in_specs=[
            pl.BlockSpec((channels, windows, chunk), lambda j: (0, 0, j)),
            pl.BlockSpec(table.shape, lambda j: (0, 0)),
        ],
        out_specs=pl.BlockSpec((rows, chunk // DECIM), lambda j: (0, j)),
        out_shape=jax.ShapeDtypeStruct((rows, row_length // DECIM), jnp.bfloat16),
        scratch_shapes=[pltpu.VMEM((rows, block_size), jnp.float32)],
    )(samples, table)


def trig(index, modulus):
    angle = (index % modulus).astype(jnp.float32) * (2.0 * math.pi / modulus)
    return jnp.cos(angle), jnp.sin(angle)


LO = 128


def dft_factors(point_count, bin_count):
    frequency = 1 + np.arange(bin_count, dtype=np.int64)[None, :]
    hi = np.arange(point_count // LO, dtype=np.int64)[:, None]
    lo = np.arange(LO, dtype=np.int64)[:, None]
    angle_hi = (frequency * hi * LO % point_count) * (2.0 * np.pi / point_count)
    angle_lo = (frequency * lo % point_count) * (2.0 * np.pi / point_count)
    c1, s1 = np.cos(angle_hi), np.sin(angle_hi)
    c2, s2 = np.cos(angle_lo), np.sin(angle_lo)
    return [jnp.asarray(t.astype(np.float32)) for t in (c1, s1, c2, s2)]


def dft_kernel(c1_ref, s1_ref, c2_ref, s2_ref, dec_ref, out_ref, tab_ref, *, halves):
    real = pl.program_id(0) < halves
    c1 = c1_ref[...]
    s1 = s1_ref[...]
    p = jnp.where(real, c1, -s1)
    q = jnp.where(real, -s1, -c1)
    c2 = c2_ref[...]
    s2 = s2_ref[...]
    for hi in range(p.shape[0]):
        value = p[hi : hi + 1, :] * c2 + q[hi : hi + 1, :] * s2
        tab_ref[hi * LO : (hi + 1) * LO, :] = value.astype(jnp.bfloat16)
    out_ref[...] = jnp.dot(dec_ref[...], tab_ref[...], preferred_element_type=jnp.float32)


def dft(decimated, block_cols=512):
    rows, points = decimated.shape
    c1, s1, c2, s2 = dft_factors(points, NBINS)
    hi_count = c1.shape[0]
    halves = NBINS // block_cols
    return pl.pallas_call(
        functools.partial(dft_kernel, halves=halves),
        grid=(2 * halves,),
        in_specs=[
            pl.BlockSpec((hi_count, block_cols), lambda i: (0, i % halves)),
            pl.BlockSpec((hi_count, block_cols), lambda i: (0, i % halves)),
            pl.BlockSpec((LO, block_cols), lambda i: (0, i % halves)),
            pl.BlockSpec((LO, block_cols), lambda i: (0, i % halves)),
            pl.BlockSpec((rows, points), lambda i: (0, 0)),
        ],
        out_specs=pl.BlockSpec((rows, block_cols), lambda i: (0, i)),
        out_shape=jax.ShapeDtypeStruct((rows, 2 * NBINS), jnp.float32),
        scratch_shapes=[pltpu.VMEM((points, block_cols), jnp.bfloat16)],
    )(c1, s1, c2, s2, decimated)


def lag_transform(cross, point_count, lag_count, window_count):
    split = 64
    pairs, _, bin_count = cross.shape
    frequency = 1 + jnp.arange(bin_count, dtype=jnp.int32)
    hi = jnp.arange(lag_count // split, dtype=jnp.int32)[:, None]
    lo = jnp.arange(split, dtype=jnp.int32)[None, :]
    ca, sa = trig(frequency[None, :] * (point_count - lag_count // 2 + split * hi), point_count)
    cb, sb = trig(frequency[:, None] * lo, point_count)
    weight = 1.0 / math.sqrt(window_count * bin_count)
    xr = cross[:, 0][:, None, :]
    xi = cross[:, 1][:, None, :]
    u = xr * ca[None] - xi * sa[None]
    v = xr * sa[None] + xi * ca[None]
    uv = jnp.concatenate([u, v], axis=2).reshape(pairs * (lag_count // split), 2 * bin_count)
    table = jnp.concatenate([cb, -sb], axis=0) * weight
    out = jnp.dot(uv, table, precision=lax.Precision.HIGHEST)
    return out.reshape(pairs, lag_count)


def window_sums(bin_count, span_width):
    bin_index = jnp.arange(bin_count, dtype=jnp.int32)
    nearby = jnp.abs(bin_index[:, None] - bin_index[None, :]) <= (span_width - 1) // 2
    count = jnp.sum(nearby.astype(jnp.float32), axis=0, keepdims=True)
    return nearby.astype(jnp.bfloat16), count


def smoother(bin_count, span_width):
    bin_index = jnp.arange(bin_count, dtype=jnp.int32)
    nearby = (jnp.abs(bin_index[:, None] - bin_index[None, :]) <= (span_width - 1) // 2).astype(
        jnp.float32
    )
    return nearby / jnp.sum(nearby, axis=0, keepdims=True)


def fused_kernel(taps_ref, x_ref, c1_ref, s1_ref, c2_ref, s2_ref, out_ref, carry_ref, fir_ref, dec_ref,
                 tab_ref, *, dec_steps, halves):
    i = pl.program_id(0)

    @pl.when(i == 0)
    def _():
        carry_ref[...] = jnp.zeros_like(carry_ref)
        shape = fir_ref.shape
        row = lax.broadcasted_iota(jnp.int32, shape, 0)
        phase = row % DECIM
        offset = lax.broadcasted_iota(jnp.int32, shape, 1) - row // DECIM
        table = jnp.zeros(shape, jnp.float32)
        for m in range(taps_ref.shape[0] // DECIM):
            value = jnp.full(shape, taps_ref[DECIM * m], jnp.float32)
            for b in range(DECIM - 1):
                value = jnp.where(phase == b, taps_ref[DECIM * m + DECIM - 1 - b], value)
            table = jnp.where(offset == m, value, table)
        fir_ref[...] = table.astype(jnp.bfloat16)

    @pl.when(i < dec_steps)
    def _():
        table = fir_ref[...]
        channels, windows, width = x_ref.shape
        segment = table.shape[0]
        block = table.shape[1] // 2
        per_step = width // segment
        for g in range(per_step):
            x = x_ref[:, :, g * segment : (g + 1) * segment].reshape(channels * windows, segment)
            both = jnp.dot(x, table, preferred_element_type=jnp.float32)
            col = pl.multiple_of((i * per_step + g) * block, block)
            dec_ref[:, pl.ds(col, block)] = (both[:, :block] + carry_ref[...]).astype(jnp.bfloat16)
            carry_ref[...] = both[:, block:]

    @pl.when(i >= dec_steps)
    def _():
        real = i - dec_steps < halves
        c1 = c1_ref[...]
        s1 = s1_ref[...]
        p = jnp.where(real, c1, -s1)
        q = jnp.where(real, -s1, -c1)
        c2 = c2_ref[...]
        s2 = s2_ref[...]
        for hi in range(p.shape[0]):
            value = p[hi : hi + 1, :] * c2 + q[hi : hi + 1, :] * s2
            tab_ref[hi * LO : (hi + 1) * LO, :] = value.astype(jnp.bfloat16)
        out_ref[...] = jnp.dot(dec_ref[...], tab_ref[...], preferred_element_type=jnp.float32)


def decimate_dft(samples, filter_taps, chunk=8192, block_cols=512):
    channels, windows, row_length = samples.shape
    block_size = min(128, row_length // DECIM)
    rows = channels * windows
    points = row_length // DECIM
    c1, s1, c2, s2 = dft_factors(points, NBINS)
    hi_count = c1.shape[0]
    halves = NBINS // block_cols
    dec_steps = row_length // chunk

    def raw_map(i):
        return (0, 0, jnp.minimum(i, dec_steps - 1))

    def factor_map(i):
        return (0, jnp.maximum(i - dec_steps, 0) % halves)

    def out_map(i):
        return (0, jnp.maximum(i - dec_steps, 0))

    return pl.pallas_call(
        functools.partial(fused_kernel, dec_steps=dec_steps, halves=halves),
        grid=(dec_steps + 2 * halves,),
        in_specs=[
            pl.BlockSpec(memory_space=pltpu.SMEM),
            pl.BlockSpec((channels, windows, chunk), raw_map),
            pl.BlockSpec((hi_count, block_cols), factor_map),
            pl.BlockSpec((hi_count, block_cols), factor_map),
            pl.BlockSpec((LO, block_cols), factor_map),
            pl.BlockSpec((LO, block_cols), factor_map),
        ],
        out_specs=pl.BlockSpec((rows, block_cols), out_map),
        out_shape=jax.ShapeDtypeStruct((rows, 2 * NBINS), jnp.float32),
        scratch_shapes=[
            pltpu.VMEM((rows, block_size), jnp.float32),
            pltpu.VMEM((DECIM * block_size, 2 * block_size), jnp.bfloat16),
            pltpu.VMEM((rows, points), jnp.bfloat16),
            pltpu.VMEM((points, block_cols), jnp.bfloat16),
        ],
    )(filter_taps, samples, c1, s1, c2, s2)


def whiten(spectrum, slices, group):
    rows = spectrum.shape[0]
    real_part = spectrum[:, :NBINS]
    imag_part = spectrum[:, NBINS:]
    magnitude = jnp.sqrt(real_part * real_part + imag_part * imag_part)
    nearby, count = window_sums(NBINS, SMOOTH)
    mag_hi = magnitude.astype(jnp.bfloat16)
    mag_lo = (magnitude - mag_hi.astype(jnp.float32)).astype(jnp.bfloat16)
    summed = jnp.dot(mag_hi, nearby, preferred_element_type=jnp.float32) + jnp.dot(
        mag_lo, nearby, preferred_element_type=jnp.float32
    )
    smooth = summed / count
    floor_level = water_level * jnp.mean(smooth, axis=1, keepdims=True) + epsilon
    factor = 1.0 / (smooth + floor_level)
    whitened = (spectrum * jnp.concatenate([factor, factor], axis=1)).astype(jnp.bfloat16)
    whitened = jnp.transpose(whitened.reshape(rows, 2, slices, group), (2, 1, 3, 0))
    return whitened.reshape(slices, 2 * group, rows)


def on_device(raw_samples, filter_taps, tile_pairs, tile_owners):
    wide_count = lax.axis_size("wide")
    narrow_count = lax.axis_size("narrow")
    devices = wide_count * narrow_count
    chan_dev, window_total, _ = raw_samples.shape
    assert chan_dev == BLK
    group = NBINS // devices
    rows = chan_dev * window_total

    whitened = whiten(decimate_dft(raw_samples, filter_taps), devices, group)
    spectra = lax.all_to_all(whitened, ("wide", "narrow"), 0, 0, tiled=True)

    source = jnp.take(spectra, tile_pairs[:, 0], axis=0)
    target = jnp.take(spectra, tile_pairs[:, 1], axis=0)
    tiles = tile_pairs.shape[0]
    source = source.reshape(tiles, 2, group, BLK, window_total)
    target = target.reshape(tiles, 2, group, BLK, window_total)
    src_real, src_imag = source[:, 0], source[:, 1]
    dst_real, dst_imag = target[:, 0], target[:, 1]

    def mm(a, b):
        return jnp.einsum("tbiw,tbjw->tbij", a, b, preferred_element_type=jnp.float32)

    real_sum = mm(src_real, dst_real) + mm(src_imag, dst_imag)
    imag_sum = mm(src_real, dst_imag) - mm(src_imag, dst_real)
    cross = jnp.stack([real_sum, imag_sum], axis=1)
    pair_share = BLK * BLK // wide_count
    cross = cross.reshape(tiles, 2 * group, BLK * BLK // pair_share, pair_share)
    cross = jnp.transpose(cross, (0, 2, 3, 1))

    slot_ids = jnp.arange(SLOTS, dtype=jnp.int32)
    owner_ids = jnp.arange(narrow_count, dtype=jnp.int32)
    owned_all = tile_owners[None, :] == owner_ids[:, None]
    rank_all = jnp.cumsum(owned_all.astype(jnp.int32), axis=1) - 1
    select_all = (owned_all[:, None, :] & (rank_all[:, None, :] == slot_ids[None, :, None])).astype(
        jnp.float32
    )
    send = jnp.einsum("nst,twqv->wnsqv", select_all, cross, precision=lax.Precision.HIGHEST)
    send = send.reshape(devices, SLOTS * pair_share * 2 * group)
    arrived = lax.all_to_all(send, ("wide", "narrow"), 0, 0, tiled=True)
    arrived = arrived.reshape(devices, SLOTS * pair_share, 2, group)
    arrived = jnp.transpose(arrived, (1, 2, 0, 3)).reshape(SLOTS * pair_share, 2, NBINS)
    stacked = lag_transform(arrived, NFFT, LAGS, window_total)
    return stacked.reshape(SLOTS, pair_share, LAGS)


def solution(mesh):
    in_specs = (P(("wide", "narrow"), None, None), P(), P(), P())
    out_specs = P("narrow", "wide", None)
    return jax.shard_map(
        on_device, mesh=mesh, in_specs=in_specs, out_specs=out_specs, check_vma=False
    )
```

```python
import functools
import math

import numpy as np

import jax
import jax.numpy as jnp
from jax import lax
from jax.experimental import pallas as pl
from jax.experimental.pallas import tpu as pltpu
from jax.sharding import PartitionSpec as P

NFFT = 4096
DECIM = 4
NBINS = 1024
SMOOTH = 63
LAGS = 512
BLK = 8
SLOTS = 8
TAPS = 64

water_level = 0.2
epsilon = 1e-06


def fir_table(filter_taps, block_size):
    taps = filter_taps.astype(jnp.bfloat16)
    span = filter_taps.shape[0] // DECIM
    cols = 2 * block_size
    width = cols + 1
    phase = taps.reshape(span, DECIM)[:, ::-1].T
    padded = jnp.pad(phase, ((0, 0), (0, width - span)))
    shifted = jnp.tile(padded, (1, block_size))[:, : block_size * cols]
    shifted = shifted.reshape(DECIM, block_size, cols)
    return jnp.transpose(shifted, (1, 0, 2)).reshape(DECIM * block_size, cols)


def decim_kernel(x_ref, t_ref, o_ref, carry_ref):
    @pl.when(pl.program_id(0) == 0)
    def _():
        carry_ref[...] = jnp.zeros_like(carry_ref)

    table = t_ref[...]
    channels, windows, width = x_ref.shape
    segment = table.shape[0]
    block = table.shape[1] // 2
    for g in range(width // segment):
        x = x_ref[:, :, g * segment : (g + 1) * segment].reshape(channels * windows, segment)
        both = jnp.dot(x, table, preferred_element_type=jnp.float32)
        o_ref[:, g * block : (g + 1) * block] = (both[:, :block] + carry_ref[...]).astype(
            jnp.bfloat16
        )
        carry_ref[...] = both[:, block:]


def decimate(samples, filter_taps, chunk=8192):
    channels, windows, row_length = samples.shape
    block_size = min(128, row_length // DECIM)
    table = fir_table(filter_taps, block_size)
    rows = channels * windows
    return pl.pallas_call(
        decim_kernel,
        grid=(row_length // chunk,),
        in_specs=[
            pl.BlockSpec((channels, windows, chunk), lambda j: (0, 0, j)),
            pl.BlockSpec(table.shape, lambda j: (0, 0)),
        ],
        out_specs=pl.BlockSpec((rows, chunk // DECIM), lambda j: (0, j)),
        out_shape=jax.ShapeDtypeStruct((rows, row_length // DECIM), jnp.bfloat16),
        scratch_shapes=[pltpu.VMEM((rows, block_size), jnp.float32)],
    )(samples, table)


def trig(index, modulus):
    angle = (index % modulus).astype(jnp.float32) * (2.0 * math.pi / modulus)
    return jnp.cos(angle), jnp.sin(angle)


LO = 128


def dft_factors(point_count, bin_count):
    frequency = 1 + np.arange(bin_count, dtype=np.int64)[None, :]
    hi = np.arange(point_count // LO, dtype=np.int64)[:, None]
    lo = np.arange(LO, dtype=np.int64)[:, None]
    angle_hi = (frequency * hi * LO % point_count) * (2.0 * np.pi / point_count)
    angle_lo = (frequency * lo % point_count) * (2.0 * np.pi / point_count)
    c1, s1 = np.cos(angle_hi), np.sin(angle_hi)
    c2, s2 = np.cos(angle_lo), np.sin(angle_lo)
    return [jnp.asarray(t.astype(np.float32)) for t in (c1, s1, c2, s2)]


def dft_kernel(c1_ref, s1_ref, c2_ref, s2_ref, dec_ref, out_ref, tab_ref, *, halves):
    real = pl.program_id(0) < halves
    c1 = c1_ref[...]
    s1 = s1_ref[...]
    p = jnp.where(real, c1, -s1)
    q = jnp.where(real, -s1, -c1)
    c2 = c2_ref[...]
    s2 = s2_ref[...]
    for hi in range(p.shape[0]):
        value = p[hi : hi + 1, :] * c2 + q[hi : hi + 1, :] * s2
        tab_ref[hi * LO : (hi + 1) * LO, :] = value.astype(jnp.bfloat16)
    out_ref[...] = jnp.dot(dec_ref[...], tab_ref[...], preferred_element_type=jnp.float32)


def dft(decimated, block_cols=512):
    rows, points = decimated.shape
    c1, s1, c2, s2 = dft_factors(points, NBINS)
    hi_count = c1.shape[0]
    halves = NBINS // block_cols
    return pl.pallas_call(
        functools.partial(dft_kernel, halves=halves),
        grid=(2 * halves,),
        in_specs=[
            pl.BlockSpec((hi_count, block_cols), lambda i: (0, i % halves)),
            pl.BlockSpec((hi_count, block_cols), lambda i: (0, i % halves)),
            pl.BlockSpec((LO, block_cols), lambda i: (0, i % halves)),
            pl.BlockSpec((LO, block_cols), lambda i: (0, i % halves)),
            pl.BlockSpec((rows, points), lambda i: (0, 0)),
        ],
        out_specs=pl.BlockSpec((rows, block_cols), lambda i: (0, i)),
        out_shape=jax.ShapeDtypeStruct((rows, 2 * NBINS), jnp.float32),
        scratch_shapes=[pltpu.VMEM((points, block_cols), jnp.bfloat16)],
    )(c1, s1, c2, s2, decimated)


def lag_transform(cross, point_count, lag_count, window_count):
    split = 64
    pairs, _, bin_count = cross.shape
    frequency = 1 + jnp.arange(bin_count, dtype=jnp.int32)
    hi = jnp.arange(lag_count // split, dtype=jnp.int32)[:, None]
    lo = jnp.arange(split, dtype=jnp.int32)[None, :]
    ca, sa = trig(frequency[None, :] * (point_count - lag_count // 2 + split * hi), point_count)
    cb, sb = trig(frequency[:, None] * lo, point_count)
    weight = 1.0 / math.sqrt(window_count * bin_count)
    xr = cross[:, 0][:, None, :]
    xi = cross[:, 1][:, None, :]
    u = xr * ca[None] - xi * sa[None]
    v = xr * sa[None] + xi * ca[None]
    uv = jnp.concatenate([u, v], axis=2).reshape(pairs * (lag_count // split), 2 * bin_count)
    table = jnp.concatenate([cb, -sb], axis=0) * weight
    out = jnp.dot(uv, table, precision=lax.Precision.HIGHEST)
    return out.reshape(pairs, lag_count)


def smoother(bin_count, span_width):
    bin_index = jnp.arange(bin_count, dtype=jnp.int32)
    nearby = (jnp.abs(bin_index[:, None] - bin_index[None, :]) <= (span_width - 1) // 2).astype(
        jnp.float32
    )
    return nearby / jnp.sum(nearby, axis=0, keepdims=True)


def fused_kernel(taps_ref, x_ref, c1_ref, s1_ref, c2_ref, s2_ref, out_ref, carry_ref, fir_ref, dec_ref,
                 tab_ref, *, dec_steps, halves, sub_cols):
    i = pl.program_id(0)

    @pl.when(i == 0)
    def _():
        carry_ref[...] = jnp.zeros_like(carry_ref)
        shape = fir_ref.shape
        row = lax.broadcasted_iota(jnp.int32, shape, 0)
        phase = row % DECIM
        offset = lax.broadcasted_iota(jnp.int32, shape, 1) - row // DECIM
        table = jnp.zeros(shape, jnp.float32)
        for m in range(taps_ref.shape[0] // DECIM):
            value = jnp.full(shape, taps_ref[DECIM * m], jnp.float32)
            for b in range(DECIM - 1):
                value = jnp.where(phase == b, taps_ref[DECIM * m + DECIM - 1 - b], value)
            table = jnp.where(offset == m, value, table)
        fir_ref[...] = table.astype(jnp.bfloat16)

    @pl.when(i < dec_steps)
    def _():
        table = fir_ref[...]
        channels, windows, width = x_ref.shape
        segment = table.shape[0]
        block = table.shape[1] // 2
        per_step = width // segment
        for g in range(per_step):
            x = x_ref[:, :, g * segment : (g + 1) * segment].reshape(channels * windows, segment)
            both = jnp.dot(x, table, preferred_element_type=jnp.float32)
            col = pl.multiple_of((i * per_step + g) * block, block)
            dec_ref[:, pl.ds(col, block)] = (both[:, :block] + carry_ref[...]).astype(jnp.bfloat16)
            carry_ref[...] = both[:, block:]

    @pl.when(i >= dec_steps)
    def _():
        real = i - dec_steps < halves
        for start in range(0, tab_ref.shape[1], sub_cols):
            cols = slice(start, start + sub_cols)
            c1 = c1_ref[:, cols]
            s1 = s1_ref[:, cols]
            p = jnp.where(real, c1, -s1)
            q = jnp.where(real, -s1, -c1)
            c2 = c2_ref[:, cols]
            s2 = s2_ref[:, cols]
            for hi in range(p.shape[0]):
                value = p[hi : hi + 1, :] * c2 + q[hi : hi + 1, :] * s2
                tab_ref[hi * LO : (hi + 1) * LO, cols] = value.astype(jnp.bfloat16)
            out_ref[:, cols] = jnp.dot(
                dec_ref[...], tab_ref[:, cols], preferred_element_type=jnp.float32
            )


def decimate_dft(samples, filter_taps, chunk=8192, block_cols=512):
    channels, windows, row_length = samples.shape
    block_size = min(128, row_length // DECIM)
    rows = channels * windows
    points = row_length // DECIM
    c1, s1, c2, s2 = dft_factors(points, NBINS)
    hi_count = c1.shape[0]
    halves = NBINS // block_cols
    dec_steps = row_length // chunk

    def raw_map(i):
        return (0, 0, jnp.minimum(i, dec_steps - 1))

    def factor_map(i):
        return (0, jnp.maximum(i - dec_steps, 0) % halves)

    def out_map(i):
        return (0, jnp.maximum(i - dec_steps, 0))

    return pl.pallas_call(
        functools.partial(fused_kernel, dec_steps=dec_steps, halves=halves, sub_cols=256),
        grid=(dec_steps + 2 * halves,),
        in_specs=[
            pl.BlockSpec(memory_space=pltpu.SMEM),
            pl.BlockSpec((channels, windows, chunk), raw_map),
            pl.BlockSpec((hi_count, block_cols), factor_map),
            pl.BlockSpec((hi_count, block_cols), factor_map),
            pl.BlockSpec((LO, block_cols), factor_map),
            pl.BlockSpec((LO, block_cols), factor_map),
        ],
        out_specs=pl.BlockSpec((rows, block_cols), out_map),
        out_shape=jax.ShapeDtypeStruct((rows, 2 * NBINS), jnp.float32),
        scratch_shapes=[
            pltpu.VMEM((rows, block_size), jnp.float32),
            pltpu.VMEM((DECIM * block_size, 2 * block_size), jnp.bfloat16),
            pltpu.VMEM((rows, points), jnp.bfloat16),
            pltpu.VMEM((points, block_cols), jnp.bfloat16),
        ],
    )(filter_taps, samples, c1, s1, c2, s2)


def whiten(spectrum, slices, group):
    rows = spectrum.shape[0]
    real_part = spectrum[:, :NBINS]
    imag_part = spectrum[:, NBINS:]
    magnitude = jnp.sqrt(real_part * real_part + imag_part * imag_part)
    smooth = jnp.dot(magnitude, smoother(NBINS, SMOOTH), precision=lax.Precision.HIGH)
    floor_level = water_level * jnp.mean(smooth, axis=1, keepdims=True) + epsilon
    factor = 1.0 / (smooth + floor_level)
    whitened = (spectrum * jnp.concatenate([factor, factor], axis=1)).astype(jnp.bfloat16)
    whitened = jnp.transpose(whitened.reshape(rows, 2, slices, group), (2, 1, 3, 0))
    return whitened.reshape(slices, 2 * group, rows)


def on_device(raw_samples, filter_taps, tile_pairs, tile_owners):
    wide_count = lax.axis_size("wide")
    narrow_count = lax.axis_size("narrow")
    devices = wide_count * narrow_count
    chan_dev, window_total, _ = raw_samples.shape
    assert chan_dev == BLK
    group = NBINS // devices
    rows = chan_dev * window_total

    whitened = whiten(decimate_dft(raw_samples, filter_taps), devices, group)
    spectra = lax.all_to_all(whitened, ("wide", "narrow"), 0, 0, tiled=True)

    source = jnp.take(spectra, tile_pairs[:, 0], axis=0)
    target = jnp.take(spectra, tile_pairs[:, 1], axis=0)
    tiles = tile_pairs.shape[0]
    source = source.reshape(tiles, 2, group, BLK, window_total)
    target = target.reshape(tiles, 2, group, BLK, window_total)
    src_real, src_imag = source[:, 0], source[:, 1]
    dst_real, dst_imag = target[:, 0], target[:, 1]

    def mm(a, b):
        return jnp.einsum("tbiw,tbjw->tbij", a, b, preferred_element_type=jnp.float32)

    real_sum = mm(src_real, dst_real) + mm(src_imag, dst_imag)
    imag_sum = mm(src_real, dst_imag) - mm(src_imag, dst_real)
    cross = jnp.stack([real_sum, imag_sum], axis=1)
    pair_share = BLK * BLK // wide_count
    cross = cross.reshape(tiles, 2 * group, BLK * BLK // pair_share, pair_share)
    cross = jnp.transpose(cross, (0, 2, 3, 1))

    slot_ids = jnp.arange(SLOTS, dtype=jnp.int32)
    owner_ids = jnp.arange(narrow_count, dtype=jnp.int32)
    owned_all = tile_owners[None, :] == owner_ids[:, None]
    rank_all = jnp.cumsum(owned_all.astype(jnp.int32), axis=1) - 1
    select_all = (owned_all[:, None, :] & (rank_all[:, None, :] == slot_ids[None, :, None])).astype(
        jnp.float32
    )
    send = jnp.einsum("nst,twqv->wnsqv", select_all, cross, precision=lax.Precision.HIGHEST)
    send = send.reshape(devices, SLOTS * pair_share * 2 * group)
    arrived = lax.all_to_all(send, ("wide", "narrow"), 0, 0, tiled=True)
    arrived = arrived.reshape(devices, SLOTS * pair_share, 2, group)
    arrived = jnp.transpose(arrived, (1, 2, 0, 3)).reshape(SLOTS * pair_share, 2, NBINS)
    stacked = lag_transform(arrived, NFFT, LAGS, window_total)
    return stacked.reshape(SLOTS, pair_share, LAGS)


def solution(mesh):
    in_specs = (P(("wide", "narrow"), None, None), P(), P(), P())
    out_specs = P("narrow", "wide", None)
    return jax.shard_map(
        on_device, mesh=mesh, in_specs=in_specs, out_specs=out_specs, check_vma=False
    )
```

```python
import functools
import math

import numpy as np

import jax
import jax.numpy as jnp
from jax import lax
from jax.experimental import pallas as pl
from jax.experimental.pallas import tpu as pltpu
from jax.sharding import PartitionSpec as P

NFFT = 4096
DECIM = 4
NBINS = 1024
SMOOTH = 63
LAGS = 512
BLK = 8
SLOTS = 8
TAPS = 64

water_level = 0.2
epsilon = 1e-06


def fir_table(filter_taps, block_size):
    taps = filter_taps.astype(jnp.bfloat16)
    span = filter_taps.shape[0] // DECIM
    cols = 2 * block_size
    width = cols + 1
    phase = taps.reshape(span, DECIM)[:, ::-1].T
    padded = jnp.pad(phase, ((0, 0), (0, width - span)))
    shifted = jnp.tile(padded, (1, block_size))[:, : block_size * cols]
    shifted = shifted.reshape(DECIM, block_size, cols)
    return jnp.transpose(shifted, (1, 0, 2)).reshape(DECIM * block_size, cols)


def decim_kernel(x_ref, t_ref, o_ref, carry_ref):
    @pl.when(pl.program_id(0) == 0)
    def _():
        carry_ref[...] = jnp.zeros_like(carry_ref)

    table = t_ref[...]
    channels, windows, width = x_ref.shape
    segment = table.shape[0]
    block = table.shape[1] // 2
    for g in range(width // segment):
        x = x_ref[:, :, g * segment : (g + 1) * segment].reshape(channels * windows, segment)
        both = jnp.dot(x, table, preferred_element_type=jnp.float32)
        o_ref[:, g * block : (g + 1) * block] = (both[:, :block] + carry_ref[...]).astype(
            jnp.bfloat16
        )
        carry_ref[...] = both[:, block:]


def decimate(samples, filter_taps, chunk=8192):
    channels, windows, row_length = samples.shape
    block_size = min(128, row_length // DECIM)
    table = fir_table(filter_taps, block_size)
    rows = channels * windows
    return pl.pallas_call(
        decim_kernel,
        grid=(row_length // chunk,),
        in_specs=[
            pl.BlockSpec((channels, windows, chunk), lambda j: (0, 0, j)),
            pl.BlockSpec(table.shape, lambda j: (0, 0)),
        ],
        out_specs=pl.BlockSpec((rows, chunk // DECIM), lambda j: (0, j)),
        out_shape=jax.ShapeDtypeStruct((rows, row_length // DECIM), jnp.bfloat16),
        scratch_shapes=[pltpu.VMEM((rows, block_size), jnp.float32)],
    )(samples, table)


def trig(index, modulus):
    angle = (index % modulus).astype(jnp.float32) * (2.0 * math.pi / modulus)
    return jnp.cos(angle), jnp.sin(angle)


LO = 128


def dft_factors(point_count, bin_count):
    frequency = 1 + np.arange(bin_count, dtype=np.int64)[None, :]
    hi = np.arange(point_count // LO, dtype=np.int64)[:, None]
    lo = np.arange(LO, dtype=np.int64)[:, None]
    angle_hi = (frequency * hi * LO % point_count) * (2.0 * np.pi / point_count)
    angle_lo = (frequency * lo % point_count) * (2.0 * np.pi / point_count)
    c1, s1 = np.cos(angle_hi), np.sin(angle_hi)
    c2, s2 = np.cos(angle_lo), np.sin(angle_lo)
    return [jnp.asarray(t.astype(np.float32)) for t in (c1, s1, c2, s2)]


def dft_kernel(c1_ref, s1_ref, c2_ref, s2_ref, dec_ref, out_ref, tab_ref, *, halves):
    real = pl.program_id(0) < halves
    c1 = c1_ref[...]
    s1 = s1_ref[...]
    p = jnp.where(real, c1, -s1)
    q = jnp.where(real, -s1, -c1)
    c2 = c2_ref[...]
    s2 = s2_ref[...]
    for hi in range(p.shape[0]):
        value = p[hi : hi + 1, :] * c2 + q[hi : hi + 1, :] * s2
        tab_ref[hi * LO : (hi + 1) * LO, :] = value.astype(jnp.bfloat16)
    out_ref[...] = jnp.dot(dec_ref[...], tab_ref[...], preferred_element_type=jnp.float32)


def dft(decimated, block_cols=512):
    rows, points = decimated.shape
    c1, s1, c2, s2 = dft_factors(points, NBINS)
    hi_count = c1.shape[0]
    halves = NBINS // block_cols
    return pl.pallas_call(
        functools.partial(dft_kernel, halves=halves),
        grid=(2 * halves,),
        in_specs=[
            pl.BlockSpec((hi_count, block_cols), lambda i: (0, i % halves)),
            pl.BlockSpec((hi_count, block_cols), lambda i: (0, i % halves)),
            pl.BlockSpec((LO, block_cols), lambda i: (0, i % halves)),
            pl.BlockSpec((LO, block_cols), lambda i: (0, i % halves)),
            pl.BlockSpec((rows, points), lambda i: (0, 0)),
        ],
        out_specs=pl.BlockSpec((rows, block_cols), lambda i: (0, i)),
        out_shape=jax.ShapeDtypeStruct((rows, 2 * NBINS), jnp.float32),
        scratch_shapes=[pltpu.VMEM((points, block_cols), jnp.bfloat16)],
    )(c1, s1, c2, s2, decimated)


def lag_transform(cross, point_count, lag_count, window_count):
    split = 64
    pairs, _, bin_count = cross.shape
    frequency = 1 + jnp.arange(bin_count, dtype=jnp.int32)
    hi = jnp.arange(lag_count // split, dtype=jnp.int32)[:, None]
    lo = jnp.arange(split, dtype=jnp.int32)[None, :]
    ca, sa = trig(frequency[None, :] * (point_count - lag_count // 2 + split * hi), point_count)
    cb, sb = trig(frequency[:, None] * lo, point_count)
    weight = 1.0 / math.sqrt(window_count * bin_count)
    xr = cross[:, 0][:, None, :]
    xi = cross[:, 1][:, None, :]
    u = xr * ca[None] - xi * sa[None]
    v = xr * sa[None] + xi * ca[None]
    uv = jnp.concatenate([u, v], axis=2).reshape(pairs * (lag_count // split), 2 * bin_count)
    table = jnp.concatenate([cb, -sb], axis=0) * weight
    out = jnp.dot(uv, table, precision=lax.Precision.HIGHEST)
    return out.reshape(pairs, lag_count)


def smoother(bin_count, span_width):
    bin_index = jnp.arange(bin_count, dtype=jnp.int32)
    nearby = (jnp.abs(bin_index[:, None] - bin_index[None, :]) <= (span_width - 1) // 2).astype(
        jnp.float32
    )
    return nearby / jnp.sum(nearby, axis=0, keepdims=True)


def fused_kernel(taps_ref, x_ref, c1_ref, s1_ref, c2_ref, s2_ref, out_ref, carry_ref, fir_ref, dec_ref,
                 tab_ref, *, dec_steps, halves, sub_cols):
    i = pl.program_id(0)

    @pl.when(i == 0)
    def _():
        carry_ref[...] = jnp.zeros_like(carry_ref)
        shape = fir_ref.shape
        row = lax.broadcasted_iota(jnp.int32, shape, 0)
        phase = row % DECIM
        offset = lax.broadcasted_iota(jnp.int32, shape, 1) - row // DECIM
        table = jnp.zeros(shape, jnp.float32)
        for m in range(taps_ref.shape[0] // DECIM):
            value = jnp.full(shape, taps_ref[DECIM * m], jnp.float32)
            for b in range(DECIM - 1):
                value = jnp.where(phase == b, taps_ref[DECIM * m + DECIM - 1 - b], value)
            table = jnp.where(offset == m, value, table)
        fir_ref[...] = table.astype(jnp.bfloat16)

    @pl.when(i < dec_steps)
    def _():
        table = fir_ref[...]
        channels, windows, width = x_ref.shape
        segment = table.shape[0]
        block = table.shape[1] // 2
        per_step = width // segment
        for g in range(per_step):
            x = x_ref[:, :, g * segment : (g + 1) * segment].reshape(channels * windows, segment)
            both = jnp.dot(x, table, preferred_element_type=jnp.float32)
            col = pl.multiple_of((i * per_step + g) * block, block)
            dec_ref[:, pl.ds(col, block)] = (both[:, :block] + carry_ref[...]).astype(jnp.bfloat16)
            carry_ref[...] = both[:, block:]

    @pl.when(i >= dec_steps)
    def _():
        real = i - dec_steps < halves
        for start in range(0, tab_ref.shape[1], sub_cols):
            cols = slice(start, start + sub_cols)
            c1 = c1_ref[:, cols]
            s1 = s1_ref[:, cols]
            p = jnp.where(real, c1, -s1)
            q = jnp.where(real, -s1, -c1)
            c2 = c2_ref[:, cols]
            s2 = s2_ref[:, cols]
            for hi in range(p.shape[0]):
                value = p[hi : hi + 1, :] * c2 + q[hi : hi + 1, :] * s2
                tab_ref[hi * LO : (hi + 1) * LO, cols] = value.astype(jnp.bfloat16)
            out_ref[:, cols] = jnp.dot(
                dec_ref[...], tab_ref[:, cols], preferred_element_type=jnp.float32
            )


def decimate_dft(samples, filter_taps, chunk=8192, block_cols=1024):
    channels, windows, row_length = samples.shape
    block_size = min(128, row_length // DECIM)
    rows = channels * windows
    points = row_length // DECIM
    c1, s1, c2, s2 = dft_factors(points, NBINS)
    hi_count = c1.shape[0]
    halves = NBINS // block_cols
    dec_steps = row_length // chunk

    def raw_map(i):
        return (0, 0, jnp.minimum(i, dec_steps - 1))

    def factor_map(i):
        return (0, jnp.maximum(i - dec_steps, 0) % halves)

    def out_map(i):
        return (0, jnp.maximum(i - dec_steps, 0))

    return pl.pallas_call(
        functools.partial(fused_kernel, dec_steps=dec_steps, halves=halves, sub_cols=256),
        grid=(dec_steps + 2 * halves,),
        in_specs=[
            pl.BlockSpec(memory_space=pltpu.SMEM),
            pl.BlockSpec((channels, windows, chunk), raw_map),
            pl.BlockSpec((hi_count, block_cols), factor_map),
            pl.BlockSpec((hi_count, block_cols), factor_map),
            pl.BlockSpec((LO, block_cols), factor_map),
            pl.BlockSpec((LO, block_cols), factor_map),
        ],
        out_specs=pl.BlockSpec((rows, block_cols), out_map),
        out_shape=jax.ShapeDtypeStruct((rows, 2 * NBINS), jnp.float32),
        scratch_shapes=[
            pltpu.VMEM((rows, block_size), jnp.float32),
            pltpu.VMEM((DECIM * block_size, 2 * block_size), jnp.bfloat16),
            pltpu.VMEM((rows, points), jnp.bfloat16),
            pltpu.VMEM((points, block_cols), jnp.bfloat16),
        ],
    )(filter_taps, samples, c1, s1, c2, s2)


def whiten(spectrum, slices, group):
    rows = spectrum.shape[0]
    real_part = spectrum[:, :NBINS]
    imag_part = spectrum[:, NBINS:]
    magnitude = jnp.sqrt(real_part * real_part + imag_part * imag_part)
    smooth = jnp.dot(magnitude, smoother(NBINS, SMOOTH), precision=lax.Precision.HIGH)
    floor_level = water_level * jnp.mean(smooth, axis=1, keepdims=True) + epsilon
    factor = 1.0 / (smooth + floor_level)
    whitened = (spectrum * jnp.concatenate([factor, factor], axis=1)).astype(jnp.bfloat16)
    whitened = jnp.transpose(whitened.reshape(rows, 2, slices, group), (2, 1, 3, 0))
    return whitened.reshape(slices, 2 * group, rows)


def on_device(raw_samples, filter_taps, tile_pairs, tile_owners):
    wide_count = lax.axis_size("wide")
    narrow_count = lax.axis_size("narrow")
    devices = wide_count * narrow_count
    chan_dev, window_total, _ = raw_samples.shape
    assert chan_dev == BLK
    group = NBINS // devices
    rows = chan_dev * window_total

    whitened = whiten(decimate_dft(raw_samples, filter_taps), devices, group)
    spectra = lax.all_to_all(whitened, ("wide", "narrow"), 0, 0, tiled=True)

    source = jnp.take(spectra, tile_pairs[:, 0], axis=0)
    target = jnp.take(spectra, tile_pairs[:, 1], axis=0)
    tiles = tile_pairs.shape[0]
    source = source.reshape(tiles, 2, group, BLK, window_total)
    target = target.reshape(tiles, 2, group, BLK, window_total)
    src_real, src_imag = source[:, 0], source[:, 1]
    dst_real, dst_imag = target[:, 0], target[:, 1]

    def mm(a, b):
        return jnp.einsum("tbiw,tbjw->tbij", a, b, preferred_element_type=jnp.float32)

    real_sum = mm(src_real, dst_real) + mm(src_imag, dst_imag)
    imag_sum = mm(src_real, dst_imag) - mm(src_imag, dst_real)
    cross = jnp.stack([real_sum, imag_sum], axis=1)
    pair_share = BLK * BLK // wide_count
    cross = cross.reshape(tiles, 2 * group, BLK * BLK // pair_share, pair_share)
    cross = jnp.transpose(cross, (0, 2, 3, 1))

    slot_ids = jnp.arange(SLOTS, dtype=jnp.int32)
    owner_ids = jnp.arange(narrow_count, dtype=jnp.int32)
    owned_all = tile_owners[None, :] == owner_ids[:, None]
    rank_all = jnp.cumsum(owned_all.astype(jnp.int32), axis=1) - 1
    select_all = (owned_all[:, None, :] & (rank_all[:, None, :] == slot_ids[None, :, None])).astype(
        jnp.float32
    )
    send = jnp.einsum("nst,twqv->wnsqv", select_all, cross, precision=lax.Precision.HIGHEST)
    send = send.reshape(devices, SLOTS * pair_share * 2 * group)
    arrived = lax.all_to_all(send, ("wide", "narrow"), 0, 0, tiled=True)
    arrived = arrived.reshape(devices, SLOTS * pair_share, 2, group)
    arrived = jnp.transpose(arrived, (1, 2, 0, 3)).reshape(SLOTS * pair_share, 2, NBINS)
    stacked = lag_transform(arrived, NFFT, LAGS, window_total)
    return stacked.reshape(SLOTS, pair_share, LAGS)


def solution(mesh):
    in_specs = (P(("wide", "narrow"), None, None), P(), P(), P())
    out_specs = P("narrow", "wide", None)
    return jax.shard_map(
        on_device, mesh=mesh, in_specs=in_specs, out_specs=out_specs, check_vma=False
    )
```

```python
import functools
import math

import numpy as np

import jax
import jax.numpy as jnp
from jax import lax
from jax.experimental import pallas as pl
from jax.experimental.pallas import tpu as pltpu
from jax.sharding import PartitionSpec as P

NFFT = 4096
DECIM = 4
NBINS = 1024
SMOOTH = 63
LAGS = 512
BLK = 8
SLOTS = 8
TAPS = 64

water_level = 0.2
epsilon = 1e-06


def fir_table(filter_taps, block_size):
    taps = filter_taps.astype(jnp.bfloat16)
    span = filter_taps.shape[0] // DECIM
    cols = 2 * block_size
    width = cols + 1
    phase = taps.reshape(span, DECIM)[:, ::-1].T
    padded = jnp.pad(phase, ((0, 0), (0, width - span)))
    shifted = jnp.tile(padded, (1, block_size))[:, : block_size * cols]
    shifted = shifted.reshape(DECIM, block_size, cols)
    return jnp.transpose(shifted, (1, 0, 2)).reshape(DECIM * block_size, cols)


def decim_kernel(x_ref, t_ref, o_ref, carry_ref):
    @pl.when(pl.program_id(0) == 0)
    def _():
        carry_ref[...] = jnp.zeros_like(carry_ref)

    table = t_ref[...]
    channels, windows, width = x_ref.shape
    segment = table.shape[0]
    block = table.shape[1] // 2
    for g in range(width // segment):
        x = x_ref[:, :, g * segment : (g + 1) * segment].reshape(channels * windows, segment)
        both = jnp.dot(x, table, preferred_element_type=jnp.float32)
        o_ref[:, g * block : (g + 1) * block] = (both[:, :block] + carry_ref[...]).astype(
            jnp.bfloat16
        )
        carry_ref[...] = both[:, block:]


def decimate(samples, filter_taps, chunk=8192):
    channels, windows, row_length = samples.shape
    block_size = min(128, row_length // DECIM)
    table = fir_table(filter_taps, block_size)
    rows = channels * windows
    return pl.pallas_call(
        decim_kernel,
        grid=(row_length // chunk,),
        in_specs=[
            pl.BlockSpec((channels, windows, chunk), lambda j: (0, 0, j)),
            pl.BlockSpec(table.shape, lambda j: (0, 0)),
        ],
        out_specs=pl.BlockSpec((rows, chunk // DECIM), lambda j: (0, j)),
        out_shape=jax.ShapeDtypeStruct((rows, row_length // DECIM), jnp.bfloat16),
        scratch_shapes=[pltpu.VMEM((rows, block_size), jnp.float32)],
    )(samples, table)


def trig(index, modulus):
    angle = (index % modulus).astype(jnp.float32) * (2.0 * math.pi / modulus)
    return jnp.cos(angle), jnp.sin(angle)


LO = 128


def dft_factors(point_count, bin_count):
    frequency = 1 + np.arange(bin_count, dtype=np.int64)[None, :]
    hi = np.arange(point_count // LO, dtype=np.int64)[:, None]
    lo = np.arange(LO, dtype=np.int64)[:, None]
    angle_hi = (frequency * hi * LO % point_count) * (2.0 * np.pi / point_count)
    angle_lo = (frequency * lo % point_count) * (2.0 * np.pi / point_count)
    c1, s1 = np.cos(angle_hi), np.sin(angle_hi)
    c2, s2 = np.cos(angle_lo), np.sin(angle_lo)
    return [jnp.asarray(t.astype(np.float32)) for t in (c1, s1, c2, s2)]


def dft_kernel(c1_ref, s1_ref, c2_ref, s2_ref, dec_ref, out_ref, tab_ref, *, halves):
    real = pl.program_id(0) < halves
    c1 = c1_ref[...]
    s1 = s1_ref[...]
    p = jnp.where(real, c1, -s1)
    q = jnp.where(real, -s1, -c1)
    c2 = c2_ref[...]
    s2 = s2_ref[...]
    for hi in range(p.shape[0]):
        value = p[hi : hi + 1, :] * c2 + q[hi : hi + 1, :] * s2
        tab_ref[hi * LO : (hi + 1) * LO, :] = value.astype(jnp.bfloat16)
    out_ref[...] = jnp.dot(dec_ref[...], tab_ref[...], preferred_element_type=jnp.float32)


def dft(decimated, block_cols=512):
    rows, points = decimated.shape
    c1, s1, c2, s2 = dft_factors(points, NBINS)
    hi_count = c1.shape[0]
    halves = NBINS // block_cols
    return pl.pallas_call(
        functools.partial(dft_kernel, halves=halves),
        grid=(2 * halves,),
        in_specs=[
            pl.BlockSpec((hi_count, block_cols), lambda i: (0, i % halves)),
            pl.BlockSpec((hi_count, block_cols), lambda i: (0, i % halves)),
            pl.BlockSpec((LO, block_cols), lambda i: (0, i % halves)),
            pl.BlockSpec((LO, block_cols), lambda i: (0, i % halves)),
            pl.BlockSpec((rows, points), lambda i: (0, 0)),
        ],
        out_specs=pl.BlockSpec((rows, block_cols), lambda i: (0, i)),
        out_shape=jax.ShapeDtypeStruct((rows, 2 * NBINS), jnp.float32),
        scratch_shapes=[pltpu.VMEM((points, block_cols), jnp.bfloat16)],
    )(c1, s1, c2, s2, decimated)


def lag_transform(cross, point_count, lag_count, window_count):
    split = 64
    pairs, _, bin_count = cross.shape
    frequency = 1 + jnp.arange(bin_count, dtype=jnp.int32)
    hi = jnp.arange(lag_count // split, dtype=jnp.int32)[:, None]
    lo = jnp.arange(split, dtype=jnp.int32)[None, :]
    ca, sa = trig(frequency[None, :] * (point_count - lag_count // 2 + split * hi), point_count)
    cb, sb = trig(frequency[:, None] * lo, point_count)
    weight = 1.0 / math.sqrt(window_count * bin_count)
    xr = cross[:, 0][:, None, :]
    xi = cross[:, 1][:, None, :]
    u = xr * ca[None] - xi * sa[None]
    v = xr * sa[None] + xi * ca[None]
    uv = jnp.concatenate([u, v], axis=2).reshape(pairs * (lag_count // split), 2 * bin_count)
    table = jnp.concatenate([cb, -sb], axis=0) * weight
    out = jnp.dot(uv, table, precision=lax.Precision.HIGHEST)
    return out.reshape(pairs, lag_count)


def smoother(bin_count, span_width):
    bin_index = jnp.arange(bin_count, dtype=jnp.int32)
    nearby = (jnp.abs(bin_index[:, None] - bin_index[None, :]) <= (span_width - 1) // 2).astype(
        jnp.float32
    )
    return nearby / jnp.sum(nearby, axis=0, keepdims=True)


def fused_kernel(taps_ref, x_ref, c1_ref, s1_ref, c2_ref, s2_ref, out_ref, carry_ref, fir_ref, dec_ref,
                 tab_ref, *, dec_steps, halves):
    i = pl.program_id(0)

    @pl.when(i == 0)
    def _():
        carry_ref[...] = jnp.zeros_like(carry_ref)
        shape = fir_ref.shape
        row = lax.broadcasted_iota(jnp.int32, shape, 0)
        phase = row % DECIM
        offset = lax.broadcasted_iota(jnp.int32, shape, 1) - row // DECIM
        table = jnp.zeros(shape, jnp.float32)
        for m in range(taps_ref.shape[0] // DECIM):
            value = jnp.full(shape, taps_ref[DECIM * m], jnp.float32)
            for b in range(DECIM - 1):
                value = jnp.where(phase == b, taps_ref[DECIM * m + DECIM - 1 - b], value)
            table = jnp.where(offset == m, value, table)
        fir_ref[...] = table.astype(jnp.bfloat16)

    @pl.when(i < dec_steps)
    def _():
        table = fir_ref[...]
        channels, windows, width = x_ref.shape
        segment = table.shape[0]
        block = table.shape[1] // 2
        per_step = width // segment
        for g in range(per_step):
            x = x_ref[:, :, g * segment : (g + 1) * segment].reshape(channels * windows, segment)
            both = jnp.dot(x, table, preferred_element_type=jnp.float32)
            col = pl.multiple_of((i * per_step + g) * block, block)
            dec_ref[:, pl.ds(col, block)] = (both[:, :block] + carry_ref[...]).astype(jnp.bfloat16)
            carry_ref[...] = both[:, block:]

    @pl.when(i >= dec_steps)
    def _():
        real = i - dec_steps < halves
        c1 = c1_ref[...]
        s1 = s1_ref[...]
        p = jnp.where(real, c1, -s1)
        q = jnp.where(real, -s1, -c1)
        c2 = c2_ref[...]
        s2 = s2_ref[...]
        for hi in range(p.shape[0]):
            value = p[hi : hi + 1, :] * c2 + q[hi : hi + 1, :] * s2
            tab_ref[hi * LO : (hi + 1) * LO, :] = value.astype(jnp.bfloat16)
        out_ref[...] = jnp.dot(dec_ref[...], tab_ref[...], preferred_element_type=jnp.float32)


def decimate_dft(samples, filter_taps, chunk=8192, block_cols=512):
    channels, windows, row_length = samples.shape
    block_size = min(128, row_length // DECIM)
    rows = channels * windows
    points = row_length // DECIM
    c1, s1, c2, s2 = dft_factors(points, NBINS)
    hi_count = c1.shape[0]
    halves = NBINS // block_cols
    dec_steps = row_length // chunk

    def raw_map(i):
        return (0, 0, jnp.minimum(i, dec_steps - 1))

    def factor_map(i):
        return (0, jnp.maximum(i - dec_steps, 0) % halves)

    def out_map(i):
        return (0, jnp.maximum(i - dec_steps, 0))

    return pl.pallas_call(
        functools.partial(fused_kernel, dec_steps=dec_steps, halves=halves),
        grid=(dec_steps + 2 * halves,),
        in_specs=[
            pl.BlockSpec(memory_space=pltpu.SMEM),
            pl.BlockSpec((channels, windows, chunk), raw_map),
            pl.BlockSpec((hi_count, block_cols), factor_map),
            pl.BlockSpec((hi_count, block_cols), factor_map),
            pl.BlockSpec((LO, block_cols), factor_map),
            pl.BlockSpec((LO, block_cols), factor_map),
        ],
        out_specs=pl.BlockSpec((rows, block_cols), out_map),
        out_shape=jax.ShapeDtypeStruct((rows, 2 * NBINS), jnp.float32),
        scratch_shapes=[
            pltpu.VMEM((rows, block_size), jnp.float32),
            pltpu.VMEM((DECIM * block_size, 2 * block_size), jnp.bfloat16),
            pltpu.VMEM((rows, points), jnp.bfloat16),
            pltpu.VMEM((points, block_cols), jnp.bfloat16),
        ],
    )(filter_taps, samples, c1, s1, c2, s2)


def whiten(spectrum, slices, group):
    rows = spectrum.shape[0]
    real_part = spectrum[:, :NBINS]
    imag_part = spectrum[:, NBINS:]
    magnitude = jnp.sqrt(real_part * real_part + imag_part * imag_part)
    smooth = jnp.dot(magnitude, smoother(NBINS, SMOOTH), precision=lax.Precision.HIGH)
    floor_level = water_level * jnp.mean(smooth, axis=1, keepdims=True) + epsilon
    factor = 1.0 / (smooth + floor_level)
    whitened = (spectrum * jnp.concatenate([factor, factor], axis=1)).astype(jnp.bfloat16)
    whitened = jnp.transpose(whitened.reshape(rows, 2, slices, group), (2, 1, 3, 0))
    return whitened.reshape(slices, 2 * group, rows)


def on_device(raw_samples, filter_taps, tile_pairs, tile_owners):
    wide_count = lax.axis_size("wide")
    narrow_count = lax.axis_size("narrow")
    devices = wide_count * narrow_count
    chan_dev, window_total, _ = raw_samples.shape
    assert chan_dev == BLK
    group = NBINS // devices
    rows = chan_dev * window_total

    whitened = whiten(decimate_dft(raw_samples, filter_taps), devices, group)
    spectra = lax.all_to_all(whitened, ("wide", "narrow"), 0, 0, tiled=True)

    tiles = tile_pairs.shape[0]
    blocks = jnp.take(spectra, jnp.transpose(tile_pairs).reshape(-1), axis=0)
    blocks = blocks.reshape(2, tiles, 2, group, BLK, window_total)
    source, target = blocks[0], blocks[1]
    src_both = jnp.concatenate([source[:, 0], source[:, 1]], axis=-1)
    dst_real_imag = jnp.concatenate([target[:, 0], target[:, 1]], axis=-1)
    dst_imag_real = jnp.concatenate([target[:, 1], -target[:, 0]], axis=-1)

    def mm(a, b):
        return jnp.einsum("tbiw,tbjw->tbij", a, b, preferred_element_type=jnp.float32)

    real_sum = mm(src_both, dst_real_imag)
    imag_sum = mm(src_both, dst_imag_real)
    cross = jnp.stack([real_sum, imag_sum], axis=1)
    pair_share = BLK * BLK // wide_count
    cross = cross.reshape(tiles, 2 * group, BLK * BLK // pair_share, pair_share)
    cross = jnp.transpose(cross, (0, 2, 3, 1))

    slot_ids = jnp.arange(SLOTS, dtype=jnp.int32)
    owner_ids = jnp.arange(narrow_count, dtype=jnp.int32)
    owned_all = tile_owners[None, :] == owner_ids[:, None]
    rank_all = jnp.cumsum(owned_all.astype(jnp.int32), axis=1) - 1
    select_all = (owned_all[:, None, :] & (rank_all[:, None, :] == slot_ids[None, :, None])).astype(
        jnp.float32
    )
    send = jnp.einsum("nst,twqv->wnsqv", select_all, cross, precision=lax.Precision.HIGHEST)
    send = send.reshape(devices, SLOTS * pair_share * 2 * group)
    arrived = lax.all_to_all(send, ("wide", "narrow"), 0, 0, tiled=True)
    arrived = arrived.reshape(devices, SLOTS * pair_share, 2, group)
    arrived = jnp.transpose(arrived, (1, 2, 0, 3)).reshape(SLOTS * pair_share, 2, NBINS)
    stacked = lag_transform(arrived, NFFT, LAGS, window_total)
    return stacked.reshape(SLOTS, pair_share, LAGS)


def solution(mesh):
    in_specs = (P(("wide", "narrow"), None, None), P(), P(), P())
    out_specs = P("narrow", "wide", None)
    return jax.shard_map(
        on_device, mesh=mesh, in_specs=in_specs, out_specs=out_specs, check_vma=False
    )
```

```python
import functools
import math

import numpy as np

import jax
import jax.numpy as jnp
from jax import lax
from jax.experimental import pallas as pl
from jax.experimental.pallas import tpu as pltpu
from jax.sharding import PartitionSpec as P

NFFT = 4096
DECIM = 4
NBINS = 1024
SMOOTH = 63
LAGS = 512
BLK = 8
SLOTS = 8
TAPS = 64

water_level = 0.2
epsilon = 1e-06


def fir_table(filter_taps, block_size):
    taps = filter_taps.astype(jnp.bfloat16)
    span = filter_taps.shape[0] // DECIM
    cols = 2 * block_size
    width = cols + 1
    phase = taps.reshape(span, DECIM)[:, ::-1].T
    padded = jnp.pad(phase, ((0, 0), (0, width - span)))
    shifted = jnp.tile(padded, (1, block_size))[:, : block_size * cols]
    shifted = shifted.reshape(DECIM, block_size, cols)
    return jnp.transpose(shifted, (1, 0, 2)).reshape(DECIM * block_size, cols)


def decim_kernel(x_ref, t_ref, o_ref, carry_ref):
    @pl.when(pl.program_id(0) == 0)
    def _():
        carry_ref[...] = jnp.zeros_like(carry_ref)

    table = t_ref[...]
    channels, windows, width = x_ref.shape
    segment = table.shape[0]
    block = table.shape[1] // 2
    for g in range(width // segment):
        x = x_ref[:, :, g * segment : (g + 1) * segment].reshape(channels * windows, segment)
        both = jnp.dot(x, table, preferred_element_type=jnp.float32)
        o_ref[:, g * block : (g + 1) * block] = (both[:, :block] + carry_ref[...]).astype(
            jnp.bfloat16
        )
        carry_ref[...] = both[:, block:]


def decimate(samples, filter_taps, chunk=8192):
    channels, windows, row_length = samples.shape
    block_size = min(128, row_length // DECIM)
    table = fir_table(filter_taps, block_size)
    rows = channels * windows
    return pl.pallas_call(
        decim_kernel,
        grid=(row_length // chunk,),
        in_specs=[
            pl.BlockSpec((channels, windows, chunk), lambda j: (0, 0, j)),
            pl.BlockSpec(table.shape, lambda j: (0, 0)),
        ],
        out_specs=pl.BlockSpec((rows, chunk // DECIM), lambda j: (0, j)),
        out_shape=jax.ShapeDtypeStruct((rows, row_length // DECIM), jnp.bfloat16),
        scratch_shapes=[pltpu.VMEM((rows, block_size), jnp.float32)],
    )(samples, table)


def trig(index, modulus):
    angle = (index % modulus).astype(jnp.float32) * (2.0 * math.pi / modulus)
    return jnp.cos(angle), jnp.sin(angle)


LO = 128


def dft_factors(point_count, bin_count):
    frequency = 1 + np.arange(bin_count, dtype=np.int64)[None, :]
    hi = np.arange(point_count // LO, dtype=np.int64)[:, None]
    lo = np.arange(LO, dtype=np.int64)[:, None]
    angle_hi = (frequency * hi * LO % point_count) * (2.0 * np.pi / point_count)
    angle_lo = (frequency * lo % point_count) * (2.0 * np.pi / point_count)
    c1, s1 = np.cos(angle_hi), np.sin(angle_hi)
    c2, s2 = np.cos(angle_lo), np.sin(angle_lo)
    return [jnp.asarray(t.astype(np.float32)) for t in (c1, s1, c2, s2)]


def dft_kernel(c1_ref, s1_ref, c2_ref, s2_ref, dec_ref, out_ref, tab_ref, *, halves):
    real = pl.program_id(0) < halves
    c1 = c1_ref[...]
    s1 = s1_ref[...]
    p = jnp.where(real, c1, -s1)
    q = jnp.where(real, -s1, -c1)
    c2 = c2_ref[...]
    s2 = s2_ref[...]
    for hi in range(p.shape[0]):
        value = p[hi : hi + 1, :] * c2 + q[hi : hi + 1, :] * s2
        tab_ref[hi * LO : (hi + 1) * LO, :] = value.astype(jnp.bfloat16)
    out_ref[...] = jnp.dot(dec_ref[...], tab_ref[...], preferred_element_type=jnp.float32)


def dft(decimated, block_cols=512):
    rows, points = decimated.shape
    c1, s1, c2, s2 = dft_factors(points, NBINS)
    hi_count = c1.shape[0]
    halves = NBINS // block_cols
    return pl.pallas_call(
        functools.partial(dft_kernel, halves=halves),
        grid=(2 * halves,),
        in_specs=[
            pl.BlockSpec((hi_count, block_cols), lambda i: (0, i % halves)),
            pl.BlockSpec((hi_count, block_cols), lambda i: (0, i % halves)),
            pl.BlockSpec((LO, block_cols), lambda i: (0, i % halves)),
            pl.BlockSpec((LO, block_cols), lambda i: (0, i % halves)),
            pl.BlockSpec((rows, points), lambda i: (0, 0)),
        ],
        out_specs=pl.BlockSpec((rows, block_cols), lambda i: (0, i)),
        out_shape=jax.ShapeDtypeStruct((rows, 2 * NBINS), jnp.float32),
        scratch_shapes=[pltpu.VMEM((points, block_cols), jnp.bfloat16)],
    )(c1, s1, c2, s2, decimated)


def lag_transform(cross, point_count, lag_count, window_count):
    split = 64
    pairs, _, bin_count = cross.shape
    frequency = 1 + jnp.arange(bin_count, dtype=jnp.int32)
    hi = jnp.arange(lag_count // split, dtype=jnp.int32)[:, None]
    lo = jnp.arange(split, dtype=jnp.int32)[None, :]
    ca, sa = trig(frequency[None, :] * (point_count - lag_count // 2 + split * hi), point_count)
    cb, sb = trig(frequency[:, None] * lo, point_count)
    weight = 1.0 / math.sqrt(window_count * bin_count)
    xr = cross[:, 0][:, None, :]
    xi = cross[:, 1][:, None, :]
    u = xr * ca[None] - xi * sa[None]
    v = xr * sa[None] + xi * ca[None]
    uv = jnp.concatenate([u, v], axis=2).reshape(pairs * (lag_count // split), 2 * bin_count)
    table = jnp.concatenate([cb, -sb], axis=0) * weight
    out = jnp.dot(uv, table, precision=lax.Precision.HIGHEST)
    return out.reshape(pairs, lag_count)


def smoother(bin_count, span_width):
    bin_index = jnp.arange(bin_count, dtype=jnp.int32)
    nearby = (jnp.abs(bin_index[:, None] - bin_index[None, :]) <= (span_width - 1) // 2).astype(
        jnp.float32
    )
    return nearby / jnp.sum(nearby, axis=0, keepdims=True)


def fused_kernel(taps_ref, x_ref, c1_ref, s1_ref, c2_ref, s2_ref, out_ref, carry_ref, fir_ref, dec_ref,
                 tab_ref, *, dec_steps, halves):
    i = pl.program_id(0)

    @pl.when(i == 0)
    def _():
        carry_ref[...] = jnp.zeros_like(carry_ref)
        shape = fir_ref.shape
        row = lax.broadcasted_iota(jnp.int32, shape, 0)
        phase = row % DECIM
        offset = lax.broadcasted_iota(jnp.int32, shape, 1) - row // DECIM
        table = jnp.zeros(shape, jnp.float32)
        for m in range(taps_ref.shape[0] // DECIM):
            value = jnp.full(shape, taps_ref[DECIM * m], jnp.float32)
            for b in range(DECIM - 1):
                value = jnp.where(phase == b, taps_ref[DECIM * m + DECIM - 1 - b], value)
            table = jnp.where(offset == m, value, table)
        fir_ref[...] = table.astype(jnp.bfloat16)

    @pl.when(i < dec_steps)
    def _():
        table = fir_ref[...]
        channels, windows, width = x_ref.shape
        segment = table.shape[0]
        block = table.shape[1] // 2
        per_step = width // segment
        for g in range(per_step):
            x = x_ref[:, :, g * segment : (g + 1) * segment].reshape(channels * windows, segment)
            both = jnp.dot(x, table, preferred_element_type=jnp.float32)
            col = pl.multiple_of((i * per_step + g) * block, block)
            dec_ref[:, pl.ds(col, block)] = (both[:, :block] + carry_ref[...]).astype(jnp.bfloat16)
            carry_ref[...] = both[:, block:]

    @pl.when(i >= dec_steps)
    def _():
        real = i - dec_steps < halves
        c1 = c1_ref[...]
        s1 = s1_ref[...]
        p = jnp.where(real, c1, -s1)
        q = jnp.where(real, -s1, -c1)
        c2 = c2_ref[...]
        s2 = s2_ref[...]
        for hi in range(p.shape[0]):
            value = p[hi : hi + 1, :] * c2 + q[hi : hi + 1, :] * s2
            tab_ref[hi * LO : (hi + 1) * LO, :] = value.astype(jnp.bfloat16)
        out_ref[...] = jnp.dot(dec_ref[...], tab_ref[...], preferred_element_type=jnp.float32)


def decimate_dft(samples, filter_taps, chunk=8192, block_cols=512):
    channels, windows, row_length = samples.shape
    block_size = min(128, row_length // DECIM)
    rows = channels * windows
    points = row_length // DECIM
    c1, s1, c2, s2 = dft_factors(points, NBINS)
    hi_count = c1.shape[0]
    halves = NBINS // block_cols
    dec_steps = row_length // chunk

    def raw_map(i):
        return (0, 0, jnp.minimum(i, dec_steps - 1))

    def factor_map(i):
        return (0, jnp.maximum(i - dec_steps, 0) % halves)

    def out_map(i):
        return (0, jnp.maximum(i - dec_steps, 0))

    return pl.pallas_call(
        functools.partial(fused_kernel, dec_steps=dec_steps, halves=halves),
        grid=(dec_steps + 2 * halves,),
        in_specs=[
            pl.BlockSpec(memory_space=pltpu.SMEM),
            pl.BlockSpec((channels, windows, chunk), raw_map),
            pl.BlockSpec((hi_count, block_cols), factor_map),
            pl.BlockSpec((hi_count, block_cols), factor_map),
            pl.BlockSpec((LO, block_cols), factor_map),
            pl.BlockSpec((LO, block_cols), factor_map),
        ],
        out_specs=pl.BlockSpec((rows, block_cols), out_map),
        out_shape=jax.ShapeDtypeStruct((rows, 2 * NBINS), jnp.float32),
        scratch_shapes=[
            pltpu.VMEM((rows, block_size), jnp.float32),
            pltpu.VMEM((DECIM * block_size, 2 * block_size), jnp.bfloat16),
            pltpu.VMEM((rows, points), jnp.bfloat16),
            pltpu.VMEM((points, block_cols), jnp.bfloat16),
        ],
    )(filter_taps, samples, c1, s1, c2, s2)


def whiten(spectrum, slices, group):
    rows = spectrum.shape[0]
    real_part = spectrum[:, :NBINS]
    imag_part = spectrum[:, NBINS:]
    magnitude = jnp.sqrt(real_part * real_part + imag_part * imag_part)
    smooth = jnp.dot(magnitude, smoother(NBINS, SMOOTH), precision=lax.Precision.HIGH)
    floor_level = water_level * jnp.mean(smooth, axis=1, keepdims=True) + epsilon
    factor = 1.0 / (smooth + floor_level)
    whitened = (spectrum * jnp.concatenate([factor, factor], axis=1)).astype(jnp.bfloat16)
    whitened = jnp.transpose(whitened.reshape(rows, 2, slices, group), (2, 1, 3, 0))
    return whitened.reshape(slices, 2 * group, rows)


def on_device(raw_samples, filter_taps, tile_pairs, tile_owners):
    wide_count = lax.axis_size("wide")
    narrow_count = lax.axis_size("narrow")
    devices = wide_count * narrow_count
    chan_dev, window_total, _ = raw_samples.shape
    assert chan_dev == BLK
    group = NBINS // devices
    rows = chan_dev * window_total

    whitened = whiten(decimate_dft(raw_samples, filter_taps), devices, group)
    spectra = lax.all_to_all(whitened, ("wide", "narrow"), 0, 0, tiled=True)

    tiles = tile_pairs.shape[0]
    blocks = jnp.take(spectra, jnp.transpose(tile_pairs).reshape(-1), axis=0)
    blocks = blocks.reshape(2, tiles, 2, group, BLK, window_total)
    source, target = blocks[0], blocks[1]
    src_both = jnp.concatenate([source[:, 0], source[:, 1]], axis=-1)
    dst_real_imag = jnp.concatenate([target[:, 0], target[:, 1]], axis=-1)
    dst_imag_real = jnp.concatenate([target[:, 1], -target[:, 0]], axis=-1)

    def mm(a, b):
        return jnp.einsum("tbiw,tbjw->tijb", a, b, preferred_element_type=jnp.float32)

    real_sum = mm(src_both, dst_real_imag)
    imag_sum = mm(src_both, dst_imag_real)
    cross = jnp.stack([real_sum, imag_sum], axis=3)
    pair_share = BLK * BLK // wide_count
    cross = cross.reshape(tiles, BLK * BLK // pair_share, pair_share, 2 * group)

    slot_ids = jnp.arange(SLOTS, dtype=jnp.int32)
    owner_ids = jnp.arange(narrow_count, dtype=jnp.int32)
    owned_all = tile_owners[None, :] == owner_ids[:, None]
    rank_all = jnp.cumsum(owned_all.astype(jnp.int32), axis=1) - 1
    select_all = (owned_all[:, None, :] & (rank_all[:, None, :] == slot_ids[None, :, None])).astype(
        jnp.float32
    )
    send = jnp.einsum("nst,twqv->wnsqv", select_all, cross, precision=lax.Precision.HIGHEST)
    send = send.reshape(devices, SLOTS * pair_share * 2 * group)
    arrived = lax.all_to_all(send, ("wide", "narrow"), 0, 0, tiled=True)
    arrived = arrived.reshape(devices, SLOTS * pair_share, 2, group)
    arrived = jnp.transpose(arrived, (1, 2, 0, 3)).reshape(SLOTS * pair_share, 2, NBINS)
    stacked = lag_transform(arrived, NFFT, LAGS, window_total)
    return stacked.reshape(SLOTS, pair_share, LAGS)


def solution(mesh):
    in_specs = (P(("wide", "narrow"), None, None), P(), P(), P())
    out_specs = P("narrow", "wide", None)
    return jax.shard_map(
        on_device, mesh=mesh, in_specs=in_specs, out_specs=out_specs, check_vma=False
    )
```

```python
import functools
import math

import numpy as np

import jax
import jax.numpy as jnp
from jax import lax
from jax.experimental import pallas as pl
from jax.experimental.pallas import tpu as pltpu
from jax.sharding import PartitionSpec as P

NFFT = 4096
DECIM = 4
NBINS = 1024
SMOOTH = 63
LAGS = 512
BLK = 8
SLOTS = 8
TAPS = 64

water_level = 0.2
epsilon = 1e-06


def fir_table(filter_taps, block_size):
    taps = filter_taps.astype(jnp.bfloat16)
    span = filter_taps.shape[0] // DECIM
    cols = 2 * block_size
    width = cols + 1
    phase = taps.reshape(span, DECIM)[:, ::-1].T
    padded = jnp.pad(phase, ((0, 0), (0, width - span)))
    shifted = jnp.tile(padded, (1, block_size))[:, : block_size * cols]
    shifted = shifted.reshape(DECIM, block_size, cols)
    return jnp.transpose(shifted, (1, 0, 2)).reshape(DECIM * block_size, cols)


def decim_kernel(x_ref, t_ref, o_ref, carry_ref):
    @pl.when(pl.program_id(0) == 0)
    def _():
        carry_ref[...] = jnp.zeros_like(carry_ref)

    table = t_ref[...]
    channels, windows, width = x_ref.shape
    segment = table.shape[0]
    block = table.shape[1] // 2
    for g in range(width // segment):
        x = x_ref[:, :, g * segment : (g + 1) * segment].reshape(channels * windows, segment)
        both = jnp.dot(x, table, preferred_element_type=jnp.float32)
        o_ref[:, g * block : (g + 1) * block] = (both[:, :block] + carry_ref[...]).astype(
            jnp.bfloat16
        )
        carry_ref[...] = both[:, block:]


def decimate(samples, filter_taps, chunk=8192):
    channels, windows, row_length = samples.shape
    block_size = min(128, row_length // DECIM)
    table = fir_table(filter_taps, block_size)
    rows = channels * windows
    return pl.pallas_call(
        decim_kernel,
        grid=(row_length // chunk,),
        in_specs=[
            pl.BlockSpec((channels, windows, chunk), lambda j: (0, 0, j)),
            pl.BlockSpec(table.shape, lambda j: (0, 0)),
        ],
        out_specs=pl.BlockSpec((rows, chunk // DECIM), lambda j: (0, j)),
        out_shape=jax.ShapeDtypeStruct((rows, row_length // DECIM), jnp.bfloat16),
        scratch_shapes=[pltpu.VMEM((rows, block_size), jnp.float32)],
    )(samples, table)


def trig(index, modulus):
    angle = (index % modulus).astype(jnp.float32) * (2.0 * math.pi / modulus)
    return jnp.cos(angle), jnp.sin(angle)


LO = 128


def dft_factors(point_count, bin_count):
    frequency = 1 + np.arange(bin_count, dtype=np.int64)[None, :]
    hi = np.arange(point_count // LO, dtype=np.int64)[:, None]
    lo = np.arange(LO, dtype=np.int64)[:, None]
    angle_hi = (frequency * hi * LO % point_count) * (2.0 * np.pi / point_count)
    angle_lo = (frequency * lo % point_count) * (2.0 * np.pi / point_count)
    c1, s1 = np.cos(angle_hi), np.sin(angle_hi)
    c2, s2 = np.cos(angle_lo), np.sin(angle_lo)
    return [jnp.asarray(t.astype(np.float32)) for t in (c1, s1, c2, s2)]


def dft_kernel(c1_ref, s1_ref, c2_ref, s2_ref, dec_ref, out_ref, tab_ref, *, halves):
    real = pl.program_id(0) < halves
    c1 = c1_ref[...]
    s1 = s1_ref[...]
    p = jnp.where(real, c1, -s1)
    q = jnp.where(real, -s1, -c1)
    c2 = c2_ref[...]
    s2 = s2_ref[...]
    for hi in range(p.shape[0]):
        value = p[hi : hi + 1, :] * c2 + q[hi : hi + 1, :] * s2
        tab_ref[hi * LO : (hi + 1) * LO, :] = value.astype(jnp.bfloat16)
    out_ref[...] = jnp.dot(dec_ref[...], tab_ref[...], preferred_element_type=jnp.float32)


def dft(decimated, block_cols=512):
    rows, points = decimated.shape
    c1, s1, c2, s2 = dft_factors(points, NBINS)
    hi_count = c1.shape[0]
    halves = NBINS // block_cols
    return pl.pallas_call(
        functools.partial(dft_kernel, halves=halves),
        grid=(2 * halves,),
        in_specs=[
            pl.BlockSpec((hi_count, block_cols), lambda i: (0, i % halves)),
            pl.BlockSpec((hi_count, block_cols), lambda i: (0, i % halves)),
            pl.BlockSpec((LO, block_cols), lambda i: (0, i % halves)),
            pl.BlockSpec((LO, block_cols), lambda i: (0, i % halves)),
            pl.BlockSpec((rows, points), lambda i: (0, 0)),
        ],
        out_specs=pl.BlockSpec((rows, block_cols), lambda i: (0, i)),
        out_shape=jax.ShapeDtypeStruct((rows, 2 * NBINS), jnp.float32),
        scratch_shapes=[pltpu.VMEM((points, block_cols), jnp.bfloat16)],
    )(c1, s1, c2, s2, decimated)


def lag_transform(cross, point_count, lag_count, window_count):
    split = 64
    pairs, _, bin_count = cross.shape
    frequency = 1 + jnp.arange(bin_count, dtype=jnp.int32)
    hi = jnp.arange(lag_count // split, dtype=jnp.int32)[:, None]
    lo = jnp.arange(split, dtype=jnp.int32)[None, :]
    ca, sa = trig(frequency[None, :] * (point_count - lag_count // 2 + split * hi), point_count)
    cb, sb = trig(frequency[:, None] * lo, point_count)
    weight = 1.0 / math.sqrt(window_count * bin_count)
    xr = cross[:, 0][:, None, :]
    xi = cross[:, 1][:, None, :]
    u = xr * ca[None] - xi * sa[None]
    v = xr * sa[None] + xi * ca[None]
    uv = jnp.concatenate([u, v], axis=2).reshape(pairs * (lag_count // split), 2 * bin_count)
    table = jnp.concatenate([cb, -sb], axis=0) * weight
    out = jnp.dot(uv, table, precision=lax.Precision.HIGH)
    return out.reshape(pairs, lag_count)


def smoother(bin_count, span_width):
    bin_index = jnp.arange(bin_count, dtype=jnp.int32)
    nearby = (jnp.abs(bin_index[:, None] - bin_index[None, :]) <= (span_width - 1) // 2).astype(
        jnp.float32
    )
    return nearby / jnp.sum(nearby, axis=0, keepdims=True)


def fused_kernel(taps_ref, x_ref, c1_ref, s1_ref, c2_ref, s2_ref, out_ref, carry_ref, fir_ref, dec_ref,
                 tab_ref, *, dec_steps, halves):
    i = pl.program_id(0)

    @pl.when(i == 0)
    def _():
        carry_ref[...] = jnp.zeros_like(carry_ref)
        shape = fir_ref.shape
        row = lax.broadcasted_iota(jnp.int32, shape, 0)
        phase = row % DECIM
        offset = lax.broadcasted_iota(jnp.int32, shape, 1) - row // DECIM
        table = jnp.zeros(shape, jnp.float32)
        for m in range(taps_ref.shape[0] // DECIM):
            value = jnp.full(shape, taps_ref[DECIM * m], jnp.float32)
            for b in range(DECIM - 1):
                value = jnp.where(phase == b, taps_ref[DECIM * m + DECIM - 1 - b], value)
            table = jnp.where(offset == m, value, table)
        fir_ref[...] = table.astype(jnp.bfloat16)

    @pl.when(i < dec_steps)
    def _():
        table = fir_ref[...]
        channels, windows, width = x_ref.shape
        segment = table.shape[0]
        block = table.shape[1] // 2
        per_step = width // segment
        for g in range(per_step):
            x = x_ref[:, :, g * segment : (g + 1) * segment].reshape(channels * windows, segment)
            both = jnp.dot(x, table, preferred_element_type=jnp.float32)
            col = pl.multiple_of((i * per_step + g) * block, block)
            dec_ref[:, pl.ds(col, block)] = (both[:, :block] + carry_ref[...]).astype(jnp.bfloat16)
            carry_ref[...] = both[:, block:]

    @pl.when(i >= dec_steps)
    def _():
        real = i - dec_steps < halves
        c1 = c1_ref[...]
        s1 = s1_ref[...]
        p = jnp.where(real, c1, -s1)
        q = jnp.where(real, -s1, -c1)
        c2 = c2_ref[...]
        s2 = s2_ref[...]
        for hi in range(p.shape[0]):
            value = p[hi : hi + 1, :] * c2 + q[hi : hi + 1, :] * s2
            tab_ref[hi * LO : (hi + 1) * LO, :] = value.astype(jnp.bfloat16)
        out_ref[...] = jnp.dot(dec_ref[...], tab_ref[...], preferred_element_type=jnp.float32)


def decimate_dft(samples, filter_taps, chunk=8192, block_cols=512):
    channels, windows, row_length = samples.shape
    block_size = min(128, row_length // DECIM)
    rows = channels * windows
    points = row_length // DECIM
    c1, s1, c2, s2 = dft_factors(points, NBINS)
    hi_count = c1.shape[0]
    halves = NBINS // block_cols
    dec_steps = row_length // chunk

    def raw_map(i):
        return (0, 0, jnp.minimum(i, dec_steps - 1))

    def factor_map(i):
        return (0, jnp.maximum(i - dec_steps, 0) % halves)

    def out_map(i):
        return (0, jnp.maximum(i - dec_steps, 0))

    return pl.pallas_call(
        functools.partial(fused_kernel, dec_steps=dec_steps, halves=halves),
        grid=(dec_steps + 2 * halves,),
        in_specs=[
            pl.BlockSpec(memory_space=pltpu.SMEM),
            pl.BlockSpec((channels, windows, chunk), raw_map),
            pl.BlockSpec((hi_count, block_cols), factor_map),
            pl.BlockSpec((hi_count, block_cols), factor_map),
            pl.BlockSpec((LO, block_cols), factor_map),
            pl.BlockSpec((LO, block_cols), factor_map),
        ],
        out_specs=pl.BlockSpec((rows, block_cols), out_map),
        out_shape=jax.ShapeDtypeStruct((rows, 2 * NBINS), jnp.float32),
        scratch_shapes=[
            pltpu.VMEM((rows, block_size), jnp.float32),
            pltpu.VMEM((DECIM * block_size, 2 * block_size), jnp.bfloat16),
            pltpu.VMEM((rows, points), jnp.bfloat16),
            pltpu.VMEM((points, block_cols), jnp.bfloat16),
        ],
    )(filter_taps, samples, c1, s1, c2, s2)


def whiten(spectrum, slices, group):
    rows = spectrum.shape[0]
    real_part = spectrum[:, :NBINS]
    imag_part = spectrum[:, NBINS:]
    magnitude = jnp.sqrt(real_part * real_part + imag_part * imag_part)
    smooth = jnp.dot(magnitude, smoother(NBINS, SMOOTH), precision=lax.Precision.HIGH)
    floor_level = water_level * jnp.mean(smooth, axis=1, keepdims=True) + epsilon
    factor = 1.0 / (smooth + floor_level)
    whitened = (spectrum * jnp.concatenate([factor, factor], axis=1)).astype(jnp.bfloat16)
    whitened = jnp.transpose(whitened.reshape(rows, 2, slices, group), (2, 1, 3, 0))
    return whitened.reshape(slices, 2 * group, rows)


def on_device(raw_samples, filter_taps, tile_pairs, tile_owners):
    wide_count = lax.axis_size("wide")
    narrow_count = lax.axis_size("narrow")
    devices = wide_count * narrow_count
    chan_dev, window_total, _ = raw_samples.shape
    assert chan_dev == BLK
    group = NBINS // devices
    rows = chan_dev * window_total

    whitened = whiten(decimate_dft(raw_samples, filter_taps), devices, group)
    spectra = lax.all_to_all(whitened, ("wide", "narrow"), 0, 0, tiled=True)

    tiles = tile_pairs.shape[0]
    blocks = jnp.take(spectra, jnp.transpose(tile_pairs).reshape(-1), axis=0)
    blocks = blocks.reshape(2, tiles, 2, group, BLK, window_total)
    source, target = blocks[0], blocks[1]
    src_both = jnp.concatenate([source[:, 0], source[:, 1]], axis=-1)
    dst_real_imag = jnp.concatenate([target[:, 0], target[:, 1]], axis=-1)
    dst_imag_real = jnp.concatenate([target[:, 1], -target[:, 0]], axis=-1)

    def mm(a, b):
        return jnp.einsum("tbiw,tbjw->tbij", a, b, preferred_element_type=jnp.float32)

    real_sum = mm(src_both, dst_real_imag)
    imag_sum = mm(src_both, dst_imag_real)
    cross = jnp.stack([real_sum, imag_sum], axis=1)
    pair_share = BLK * BLK // wide_count
    cross = cross.reshape(tiles, 2 * group, BLK * BLK // pair_share, pair_share)
    cross = jnp.transpose(cross, (0, 2, 3, 1))

    slot_ids = jnp.arange(SLOTS, dtype=jnp.int32)
    owner_ids = jnp.arange(narrow_count, dtype=jnp.int32)
    owned_all = tile_owners[None, :] == owner_ids[:, None]
    rank_all = jnp.cumsum(owned_all.astype(jnp.int32), axis=1) - 1
    select_all = (owned_all[:, None, :] & (rank_all[:, None, :] == slot_ids[None, :, None])).astype(
        jnp.float32
    )
    send = jnp.einsum("nst,twqv->wnsqv", select_all, cross, precision=lax.Precision.HIGHEST)
    send = send.reshape(devices, SLOTS * pair_share * 2 * group)
    arrived = lax.all_to_all(send, ("wide", "narrow"), 0, 0, tiled=True)
    arrived = arrived.reshape(devices, SLOTS * pair_share, 2, group)
    arrived = jnp.transpose(arrived, (1, 2, 0, 3)).reshape(SLOTS * pair_share, 2, NBINS)
    stacked = lag_transform(arrived, NFFT, LAGS, window_total)
    return stacked.reshape(SLOTS, pair_share, LAGS)


def solution(mesh):
    in_specs = (P(("wide", "narrow"), None, None), P(), P(), P())
    out_specs = P("narrow", "wide", None)
    return jax.shard_map(
        on_device, mesh=mesh, in_specs=in_specs, out_specs=out_specs, check_vma=False
    )
```

```python
import functools
import math

import numpy as np

import jax
import jax.numpy as jnp
from jax import lax
from jax.experimental import pallas as pl
from jax.experimental.pallas import tpu as pltpu
from jax.sharding import PartitionSpec as P

NFFT = 4096
DECIM = 4
NBINS = 1024
SMOOTH = 63
LAGS = 512
BLK = 8
SLOTS = 8
TAPS = 64

water_level = 0.2
epsilon = 1e-06


def fir_table(filter_taps, block_size):
    taps = filter_taps.astype(jnp.bfloat16)
    span = filter_taps.shape[0] // DECIM
    cols = 2 * block_size
    width = cols + 1
    phase = taps.reshape(span, DECIM)[:, ::-1].T
    padded = jnp.pad(phase, ((0, 0), (0, width - span)))
    shifted = jnp.tile(padded, (1, block_size))[:, : block_size * cols]
    shifted = shifted.reshape(DECIM, block_size, cols)
    return jnp.transpose(shifted, (1, 0, 2)).reshape(DECIM * block_size, cols)


def decim_kernel(x_ref, t_ref, o_ref, carry_ref):
    @pl.when(pl.program_id(0) == 0)
    def _():
        carry_ref[...] = jnp.zeros_like(carry_ref)

    table = t_ref[...]
    channels, windows, width = x_ref.shape
    segment = table.shape[0]
    block = table.shape[1] // 2
    for g in range(width // segment):
        x = x_ref[:, :, g * segment : (g + 1) * segment].reshape(channels * windows, segment)
        both = jnp.dot(x, table, preferred_element_type=jnp.float32)
        o_ref[:, g * block : (g + 1) * block] = (both[:, :block] + carry_ref[...]).astype(
            jnp.bfloat16
        )
        carry_ref[...] = both[:, block:]


def decimate(samples, filter_taps, chunk=8192):
    channels, windows, row_length = samples.shape
    block_size = min(128, row_length // DECIM)
    table = fir_table(filter_taps, block_size)
    rows = channels * windows
    return pl.pallas_call(
        decim_kernel,
        grid=(row_length // chunk,),
        in_specs=[
            pl.BlockSpec((channels, windows, chunk), lambda j: (0, 0, j)),
            pl.BlockSpec(table.shape, lambda j: (0, 0)),
        ],
        out_specs=pl.BlockSpec((rows, chunk // DECIM), lambda j: (0, j)),
        out_shape=jax.ShapeDtypeStruct((rows, row_length // DECIM), jnp.bfloat16),
        scratch_shapes=[pltpu.VMEM((rows, block_size), jnp.float32)],
    )(samples, table)


def trig(index, modulus):
    angle = (index % modulus).astype(jnp.float32) * (2.0 * math.pi / modulus)
    return jnp.cos(angle), jnp.sin(angle)


LO = 128


def dft_factors(point_count, bin_count):
    frequency = 1 + np.arange(bin_count, dtype=np.int64)[None, :]
    hi = np.arange(point_count // LO, dtype=np.int64)[:, None]
    lo = np.arange(LO, dtype=np.int64)[:, None]
    angle_hi = (frequency * hi * LO % point_count) * (2.0 * np.pi / point_count)
    angle_lo = (frequency * lo % point_count) * (2.0 * np.pi / point_count)
    c1, s1 = np.cos(angle_hi), np.sin(angle_hi)
    c2, s2 = np.cos(angle_lo), np.sin(angle_lo)
    return [jnp.asarray(t.astype(np.float32)) for t in (c1, s1, c2, s2)]


def dft_kernel(c1_ref, s1_ref, c2_ref, s2_ref, dec_ref, out_ref, tab_ref, *, halves):
    real = pl.program_id(0) < halves
    c1 = c1_ref[...]
    s1 = s1_ref[...]
    p = jnp.where(real, c1, -s1)
    q = jnp.where(real, -s1, -c1)
    c2 = c2_ref[...]
    s2 = s2_ref[...]
    for hi in range(p.shape[0]):
        value = p[hi : hi + 1, :] * c2 + q[hi : hi + 1, :] * s2
        tab_ref[hi * LO : (hi + 1) * LO, :] = value.astype(jnp.bfloat16)
    out_ref[...] = jnp.dot(dec_ref[...], tab_ref[...], preferred_element_type=jnp.float32)


def dft(decimated, block_cols=512):
    rows, points = decimated.shape
    c1, s1, c2, s2 = dft_factors(points, NBINS)
    hi_count = c1.shape[0]
    halves = NBINS // block_cols
    return pl.pallas_call(
        functools.partial(dft_kernel, halves=halves),
        grid=(2 * halves,),
        in_specs=[
            pl.BlockSpec((hi_count, block_cols), lambda i: (0, i % halves)),
            pl.BlockSpec((hi_count, block_cols), lambda i: (0, i % halves)),
            pl.BlockSpec((LO, block_cols), lambda i: (0, i % halves)),
            pl.BlockSpec((LO, block_cols), lambda i: (0, i % halves)),
            pl.BlockSpec((rows, points), lambda i: (0, 0)),
        ],
        out_specs=pl.BlockSpec((rows, block_cols), lambda i: (0, i)),
        out_shape=jax.ShapeDtypeStruct((rows, 2 * NBINS), jnp.float32),
        scratch_shapes=[pltpu.VMEM((points, block_cols), jnp.bfloat16)],
    )(c1, s1, c2, s2, decimated)


def lag_transform(cross, point_count, lag_count, window_count):
    split = 64
    pairs, _, bin_count = cross.shape
    frequency = 1 + jnp.arange(bin_count, dtype=jnp.int32)
    hi = jnp.arange(lag_count // split, dtype=jnp.int32)[:, None]
    lo = jnp.arange(split, dtype=jnp.int32)[None, :]
    ca, sa = trig(frequency[None, :] * (point_count - lag_count // 2 + split * hi), point_count)
    cb, sb = trig(frequency[:, None] * lo, point_count)
    weight = 1.0 / math.sqrt(window_count * bin_count)
    xr = cross[:, 0][:, None, :]
    xi = cross[:, 1][:, None, :]
    u = xr * ca[None] - xi * sa[None]
    v = xr * sa[None] + xi * ca[None]
    uv = jnp.concatenate([u, v], axis=2).reshape(pairs * (lag_count // split), 2 * bin_count)
    table = jnp.concatenate([cb, -sb], axis=0) * weight
    out = jnp.dot(uv, table, precision=lax.Precision.HIGH)
    return out.reshape(pairs, lag_count)


def smoother(bin_count, span_width):
    bin_index = jnp.arange(bin_count, dtype=jnp.int32)
    nearby = (jnp.abs(bin_index[:, None] - bin_index[None, :]) <= (span_width - 1) // 2).astype(
        jnp.float32
    )
    return nearby / jnp.sum(nearby, axis=0, keepdims=True)


def fused_kernel(taps_ref, x_ref, c1_ref, s1_ref, c2_ref, s2_ref, out_ref, carry_ref, fir_ref, dec_ref,
                 tab_ref, *, dec_steps, halves):
    i = pl.program_id(0)

    @pl.when(i == 0)
    def _():
        carry_ref[...] = jnp.zeros_like(carry_ref)
        shape = fir_ref.shape
        row = lax.broadcasted_iota(jnp.int32, shape, 0)
        phase = row % DECIM
        offset = lax.broadcasted_iota(jnp.int32, shape, 1) - row // DECIM
        table = jnp.zeros(shape, jnp.float32)
        for m in range(taps_ref.shape[0] // DECIM):
            value = jnp.full(shape, taps_ref[DECIM * m], jnp.float32)
            for b in range(DECIM - 1):
                value = jnp.where(phase == b, taps_ref[DECIM * m + DECIM - 1 - b], value)
            table = jnp.where(offset == m, value, table)
        fir_ref[...] = table.astype(jnp.bfloat16)

    @pl.when(i < dec_steps)
    def _():
        table = fir_ref[...]
        channels, windows, width = x_ref.shape
        segment = table.shape[0]
        block = table.shape[1] // 2
        per_step = width // segment
        for g in range(per_step):
            x = x_ref[:, :, g * segment : (g + 1) * segment].reshape(channels * windows, segment)
            both = jnp.dot(x, table, preferred_element_type=jnp.float32)
            col = pl.multiple_of((i * per_step + g) * block, block)
            dec_ref[:, pl.ds(col, block)] = (both[:, :block] + carry_ref[...]).astype(jnp.bfloat16)
            carry_ref[...] = both[:, block:]

    @pl.when(i >= dec_steps)
    def _():
        real = i - dec_steps < halves
        c1 = c1_ref[...]
        s1 = s1_ref[...]
        p = jnp.where(real, c1, -s1)
        q = jnp.where(real, -s1, -c1)
        c2 = c2_ref[...]
        s2 = s2_ref[...]
        for hi in range(p.shape[0]):
            value = p[hi : hi + 1, :] * c2 + q[hi : hi + 1, :] * s2
            tab_ref[hi * LO : (hi + 1) * LO, :] = value.astype(jnp.bfloat16)
        out_ref[...] = jnp.dot(dec_ref[...], tab_ref[...], preferred_element_type=jnp.float32)


def decimate_dft(samples, filter_taps, chunk=8192, block_cols=512):
    channels, windows, row_length = samples.shape
    block_size = min(128, row_length // DECIM)
    rows = channels * windows
    points = row_length // DECIM
    c1, s1, c2, s2 = dft_factors(points, NBINS)
    hi_count = c1.shape[0]
    halves = NBINS // block_cols
    dec_steps = row_length // chunk

    def raw_map(i):
        return (0, 0, jnp.minimum(i, dec_steps - 1))

    def factor_map(i):
        return (0, jnp.maximum(i - dec_steps, 0) % halves)

    def out_map(i):
        return (0, jnp.maximum(i - dec_steps, 0))

    return pl.pallas_call(
        functools.partial(fused_kernel, dec_steps=dec_steps, halves=halves),
        grid=(dec_steps + 2 * halves,),
        in_specs=[
            pl.BlockSpec(memory_space=pltpu.SMEM),
            pl.BlockSpec((channels, windows, chunk), raw_map),
            pl.BlockSpec((hi_count, block_cols), factor_map),
            pl.BlockSpec((hi_count, block_cols), factor_map),
            pl.BlockSpec((LO, block_cols), factor_map),
            pl.BlockSpec((LO, block_cols), factor_map),
        ],
        out_specs=pl.BlockSpec((rows, block_cols), out_map),
        out_shape=jax.ShapeDtypeStruct((rows, 2 * NBINS), jnp.float32),
        scratch_shapes=[
            pltpu.VMEM((rows, block_size), jnp.float32),
            pltpu.VMEM((DECIM * block_size, 2 * block_size), jnp.bfloat16),
            pltpu.VMEM((rows, points), jnp.bfloat16),
            pltpu.VMEM((points, block_cols), jnp.bfloat16),
        ],
    )(filter_taps, samples, c1, s1, c2, s2)


def whiten(spectrum, slices, group):
    rows = spectrum.shape[0]
    real_part = spectrum[:, :NBINS]
    imag_part = spectrum[:, NBINS:]
    magnitude = jnp.sqrt(real_part * real_part + imag_part * imag_part)
    smooth = jnp.dot(magnitude, smoother(NBINS, SMOOTH), precision=lax.Precision.HIGH)
    floor_level = water_level * jnp.mean(smooth, axis=1, keepdims=True) + epsilon
    factor = 1.0 / (smooth + floor_level)
    whitened = (spectrum * jnp.concatenate([factor, factor], axis=1)).astype(jnp.bfloat16)
    whitened = jnp.transpose(whitened.reshape(rows, 2, slices, group), (2, 1, 3, 0))
    return whitened.reshape(slices, 2 * group, rows)


def on_device(raw_samples, filter_taps, tile_pairs, tile_owners):
    wide_count = lax.axis_size("wide")
    narrow_count = lax.axis_size("narrow")
    devices = wide_count * narrow_count
    chan_dev, window_total, _ = raw_samples.shape
    assert chan_dev == BLK
    group = NBINS // devices
    rows = chan_dev * window_total

    whitened = whiten(decimate_dft(raw_samples, filter_taps), devices, group)
    spectra = lax.all_to_all(whitened, ("wide", "narrow"), 0, 0, tiled=True)

    tiles = tile_pairs.shape[0]
    blocks = jnp.take(spectra, jnp.transpose(tile_pairs).reshape(-1), axis=0)
    blocks = blocks.reshape(2, tiles, 2, group, BLK, window_total)
    source, target = blocks[0], blocks[1]
    src_both = jnp.concatenate([source[:, 0], source[:, 1]], axis=-1)
    dst_real_imag = jnp.concatenate([target[:, 0], target[:, 1]], axis=-1)
    dst_imag_real = jnp.concatenate([target[:, 1], -target[:, 0]], axis=-1)

    def mm(a, b):
        return jnp.einsum("tbiw,tbjw->tbij", a, b, preferred_element_type=jnp.float32)

    real_sum = mm(src_both, dst_real_imag)
    imag_sum = mm(src_both, dst_imag_real)
    cross = jnp.stack([real_sum, imag_sum], axis=1)
    pair_share = BLK * BLK // wide_count
    cross = cross.reshape(tiles, 2 * group, BLK * BLK // pair_share, pair_share)
    cross = jnp.transpose(cross, (0, 2, 3, 1))

    slot_ids = jnp.arange(SLOTS, dtype=jnp.int32)
    owner_ids = jnp.arange(narrow_count, dtype=jnp.int32)
    owned_all = tile_owners[None, :] == owner_ids[:, None]
    rank_all = jnp.cumsum(owned_all.astype(jnp.int32), axis=1) - 1
    select_all = (owned_all[:, None, :] & (rank_all[:, None, :] == slot_ids[None, :, None])).astype(
        jnp.float32
    )
    send = jnp.einsum("nst,twqv->wnsqv", select_all, cross, precision=lax.Precision.HIGH)
    send = send.reshape(devices, SLOTS * pair_share * 2 * group)
    arrived = lax.all_to_all(send, ("wide", "narrow"), 0, 0, tiled=True)
    arrived = arrived.reshape(devices, SLOTS * pair_share, 2, group)
    arrived = jnp.transpose(arrived, (1, 2, 0, 3)).reshape(SLOTS * pair_share, 2, NBINS)
    stacked = lag_transform(arrived, NFFT, LAGS, window_total)
    return stacked.reshape(SLOTS, pair_share, LAGS)


def solution(mesh):
    in_specs = (P(("wide", "narrow"), None, None), P(), P(), P())
    out_specs = P("narrow", "wide", None)
    return jax.shard_map(
        on_device, mesh=mesh, in_specs=in_specs, out_specs=out_specs, check_vma=False
    )
```

```python
import functools
import math

import numpy as np

import jax
import jax.numpy as jnp
from jax import lax
from jax.experimental import pallas as pl
from jax.experimental.pallas import tpu as pltpu
from jax.sharding import PartitionSpec as P

NFFT = 4096
DECIM = 4
NBINS = 1024
SMOOTH = 63
LAGS = 512
BLK = 8
SLOTS = 8
TAPS = 64

water_level = 0.2
epsilon = 1e-06


def fir_table(filter_taps, block_size):
    taps = filter_taps.astype(jnp.bfloat16)
    span = filter_taps.shape[0] // DECIM
    cols = 2 * block_size
    width = cols + 1
    phase = taps.reshape(span, DECIM)[:, ::-1].T
    padded = jnp.pad(phase, ((0, 0), (0, width - span)))
    shifted = jnp.tile(padded, (1, block_size))[:, : block_size * cols]
    shifted = shifted.reshape(DECIM, block_size, cols)
    return jnp.transpose(shifted, (1, 0, 2)).reshape(DECIM * block_size, cols)


def decim_kernel(x_ref, t_ref, o_ref, carry_ref):
    @pl.when(pl.program_id(0) == 0)
    def _():
        carry_ref[...] = jnp.zeros_like(carry_ref)

    table = t_ref[...]
    channels, windows, width = x_ref.shape
    segment = table.shape[0]
    block = table.shape[1] // 2
    for g in range(width // segment):
        x = x_ref[:, :, g * segment : (g + 1) * segment].reshape(channels * windows, segment)
        both = jnp.dot(x, table, preferred_element_type=jnp.float32)
        o_ref[:, g * block : (g + 1) * block] = (both[:, :block] + carry_ref[...]).astype(
            jnp.bfloat16
        )
        carry_ref[...] = both[:, block:]


def decimate(samples, filter_taps, chunk=8192):
    channels, windows, row_length = samples.shape
    block_size = min(128, row_length // DECIM)
    table = fir_table(filter_taps, block_size)
    rows = channels * windows
    return pl.pallas_call(
        decim_kernel,
        grid=(row_length // chunk,),
        in_specs=[
            pl.BlockSpec((channels, windows, chunk), lambda j: (0, 0, j)),
            pl.BlockSpec(table.shape, lambda j: (0, 0)),
        ],
        out_specs=pl.BlockSpec((rows, chunk // DECIM), lambda j: (0, j)),
        out_shape=jax.ShapeDtypeStruct((rows, row_length // DECIM), jnp.bfloat16),
        scratch_shapes=[pltpu.VMEM((rows, block_size), jnp.float32)],
    )(samples, table)


def trig(index, modulus):
    angle = (index % modulus).astype(jnp.float32) * (2.0 * math.pi / modulus)
    return jnp.cos(angle), jnp.sin(angle)


LO = 128


def dft_factors(point_count, bin_count):
    frequency = 1 + np.arange(bin_count, dtype=np.int64)[None, :]
    hi = np.arange(point_count // LO, dtype=np.int64)[:, None]
    lo = np.arange(LO, dtype=np.int64)[:, None]
    angle_hi = (frequency * hi * LO % point_count) * (2.0 * np.pi / point_count)
    angle_lo = (frequency * lo % point_count) * (2.0 * np.pi / point_count)
    c1, s1 = np.cos(angle_hi), np.sin(angle_hi)
    c2, s2 = np.cos(angle_lo), np.sin(angle_lo)
    return [jnp.asarray(t.astype(np.float32)) for t in (c1, s1, c2, s2)]


def dft_kernel(c1_ref, s1_ref, c2_ref, s2_ref, dec_ref, out_ref, tab_ref, *, halves):
    real = pl.program_id(0) < halves
    c1 = c1_ref[...]
    s1 = s1_ref[...]
    p = jnp.where(real, c1, -s1)
    q = jnp.where(real, -s1, -c1)
    c2 = c2_ref[...]
    s2 = s2_ref[...]
    for hi in range(p.shape[0]):
        value = p[hi : hi + 1, :] * c2 + q[hi : hi + 1, :] * s2
        tab_ref[hi * LO : (hi + 1) * LO, :] = value.astype(jnp.bfloat16)
    out_ref[...] = jnp.dot(dec_ref[...], tab_ref[...], preferred_element_type=jnp.float32)


def dft(decimated, block_cols=512):
    rows, points = decimated.shape
    c1, s1, c2, s2 = dft_factors(points, NBINS)
    hi_count = c1.shape[0]
    halves = NBINS // block_cols
    return pl.pallas_call(
        functools.partial(dft_kernel, halves=halves),
        grid=(2 * halves,),
        in_specs=[
            pl.BlockSpec((hi_count, block_cols), lambda i: (0, i % halves)),
            pl.BlockSpec((hi_count, block_cols), lambda i: (0, i % halves)),
            pl.BlockSpec((LO, block_cols), lambda i: (0, i % halves)),
            pl.BlockSpec((LO, block_cols), lambda i: (0, i % halves)),
            pl.BlockSpec((rows, points), lambda i: (0, 0)),
        ],
        out_specs=pl.BlockSpec((rows, block_cols), lambda i: (0, i)),
        out_shape=jax.ShapeDtypeStruct((rows, 2 * NBINS), jnp.float32),
        scratch_shapes=[pltpu.VMEM((points, block_cols), jnp.bfloat16)],
    )(c1, s1, c2, s2, decimated)


def lag_transform(cross, point_count, lag_count, window_count):
    split = 64
    pairs, _, bin_count = cross.shape
    frequency = 1 + jnp.arange(bin_count, dtype=jnp.int32)
    hi = jnp.arange(lag_count // split, dtype=jnp.int32)[:, None]
    lo = jnp.arange(split, dtype=jnp.int32)[None, :]
    ca, sa = trig(frequency[None, :] * (point_count - lag_count // 2 + split * hi), point_count)
    cb, sb = trig(frequency[:, None] * lo, point_count)
    weight = 1.0 / math.sqrt(window_count * bin_count)
    xr = cross[:, 0][:, None, :]
    xi = cross[:, 1][:, None, :]
    u = xr * ca[None] - xi * sa[None]
    v = xr * sa[None] + xi * ca[None]
    uv = jnp.concatenate([u, v], axis=2).reshape(pairs * (lag_count // split), 2 * bin_count)
    table = jnp.concatenate([cb, -sb], axis=0) * weight
    out = jnp.dot(uv, table, precision=lax.Precision.HIGH)
    return out.reshape(pairs, lag_count)


def smoother(bin_count, span_width):
    bin_index = jnp.arange(bin_count, dtype=jnp.int32)
    nearby = (jnp.abs(bin_index[:, None] - bin_index[None, :]) <= (span_width - 1) // 2).astype(
        jnp.float32
    )
    return nearby / jnp.sum(nearby, axis=0, keepdims=True)


def fused_kernel(taps_ref, x_ref, c1_ref, s1_ref, c2_ref, s2_ref, out_ref, carry_ref, fir_ref, dec_ref,
                 tab_ref, *, dec_steps, halves):
    i = pl.program_id(0)

    @pl.when(i == 0)
    def _():
        carry_ref[...] = jnp.zeros_like(carry_ref)
        shape = fir_ref.shape
        row = lax.broadcasted_iota(jnp.int32, shape, 0)
        phase = row % DECIM
        offset = lax.broadcasted_iota(jnp.int32, shape, 1) - row // DECIM
        table = jnp.zeros(shape, jnp.float32)
        for m in range(taps_ref.shape[0] // DECIM):
            value = jnp.full(shape, taps_ref[DECIM * m], jnp.float32)
            for b in range(DECIM - 1):
                value = jnp.where(phase == b, taps_ref[DECIM * m + DECIM - 1 - b], value)
            table = jnp.where(offset == m, value, table)
        fir_ref[...] = table.astype(jnp.bfloat16)

    @pl.when(i < dec_steps)
    def _():
        table = fir_ref[...]
        channels, windows, width = x_ref.shape
        segment = table.shape[0]
        block = table.shape[1] // 2
        per_step = width // segment
        for g in range(per_step):
            x = x_ref[:, :, g * segment : (g + 1) * segment].reshape(channels * windows, segment)
            both = jnp.dot(x, table, preferred_element_type=jnp.float32)
            col = pl.multiple_of((i * per_step + g) * block, block)
            dec_ref[:, pl.ds(col, block)] = (both[:, :block] + carry_ref[...]).astype(jnp.bfloat16)
            carry_ref[...] = both[:, block:]

    @pl.when(i >= dec_steps)
    def _():
        real = i - dec_steps < halves
        c1 = c1_ref[...]
        s1 = s1_ref[...]
        p = jnp.where(real, c1, -s1)
        q = jnp.where(real, -s1, -c1)
        c2 = c2_ref[...]
        s2 = s2_ref[...]
        for hi in range(p.shape[0]):
            value = p[hi : hi + 1, :] * c2 + q[hi : hi + 1, :] * s2
            tab_ref[hi * LO : (hi + 1) * LO, :] = value.astype(jnp.bfloat16)
        out_ref[...] = jnp.dot(dec_ref[...], tab_ref[...], preferred_element_type=jnp.float32)


def decimate_dft(samples, filter_taps, chunk=8192, block_cols=1024):
    channels, windows, row_length = samples.shape
    block_size = min(128, row_length // DECIM)
    rows = channels * windows
    points = row_length // DECIM
    c1, s1, c2, s2 = dft_factors(points, NBINS)
    hi_count = c1.shape[0]
    halves = NBINS // block_cols
    dec_steps = row_length // chunk

    def raw_map(i):
        return (0, 0, jnp.minimum(i, dec_steps - 1))

    def factor_map(i):
        return (0, jnp.maximum(i - dec_steps, 0) % halves)

    def out_map(i):
        return (0, jnp.maximum(i - dec_steps, 0))

    return pl.pallas_call(
        functools.partial(fused_kernel, dec_steps=dec_steps, halves=halves),
        grid=(dec_steps + 2 * halves,),
        in_specs=[
            pl.BlockSpec(memory_space=pltpu.SMEM),
            pl.BlockSpec((channels, windows, chunk), raw_map),
            pl.BlockSpec((hi_count, block_cols), factor_map),
            pl.BlockSpec((hi_count, block_cols), factor_map),
            pl.BlockSpec((LO, block_cols), factor_map),
            pl.BlockSpec((LO, block_cols), factor_map),
        ],
        out_specs=pl.BlockSpec((rows, block_cols), out_map),
        out_shape=jax.ShapeDtypeStruct((rows, 2 * NBINS), jnp.float32),
        scratch_shapes=[
            pltpu.VMEM((rows, block_size), jnp.float32),
            pltpu.VMEM((DECIM * block_size, 2 * block_size), jnp.bfloat16),
            pltpu.VMEM((rows, points), jnp.bfloat16),
            pltpu.VMEM((points, block_cols), jnp.bfloat16),
        ],
    )(filter_taps, samples, c1, s1, c2, s2)


def whiten(spectrum, slices, group):
    rows = spectrum.shape[0]
    real_part = spectrum[:, :NBINS]
    imag_part = spectrum[:, NBINS:]
    magnitude = jnp.sqrt(real_part * real_part + imag_part * imag_part)
    smooth = jnp.dot(magnitude, smoother(NBINS, SMOOTH), precision=lax.Precision.HIGH)
    floor_level = water_level * jnp.mean(smooth, axis=1, keepdims=True) + epsilon
    factor = 1.0 / (smooth + floor_level)
    whitened = (spectrum * jnp.concatenate([factor, factor], axis=1)).astype(jnp.bfloat16)
    whitened = jnp.transpose(whitened.reshape(rows, 2, slices, group), (2, 1, 3, 0))
    return whitened.reshape(slices, 2 * group, rows)


def on_device(raw_samples, filter_taps, tile_pairs, tile_owners):
    wide_count = lax.axis_size("wide")
    narrow_count = lax.axis_size("narrow")
    devices = wide_count * narrow_count
    chan_dev, window_total, _ = raw_samples.shape
    assert chan_dev == BLK
    group = NBINS // devices
    rows = chan_dev * window_total

    whitened = whiten(decimate_dft(raw_samples, filter_taps), devices, group)
    spectra = lax.all_to_all(whitened, ("wide", "narrow"), 0, 0, tiled=True)

    tiles = tile_pairs.shape[0]
    blocks = jnp.take(spectra, jnp.transpose(tile_pairs).reshape(-1), axis=0)
    blocks = blocks.reshape(2, tiles, 2, group, BLK, window_total)
    source, target = blocks[0], blocks[1]
    src_both = jnp.concatenate([source[:, 0], source[:, 1]], axis=-1)
    dst_real_imag = jnp.concatenate([target[:, 0], target[:, 1]], axis=-1)
    dst_imag_real = jnp.concatenate([target[:, 1], -target[:, 0]], axis=-1)

    def mm(a, b):
        return jnp.einsum("tbiw,tbjw->tbij", a, b, preferred_element_type=jnp.float32)

    real_sum = mm(src_both, dst_real_imag)
    imag_sum = mm(src_both, dst_imag_real)
    cross = jnp.stack([real_sum, imag_sum], axis=1)
    pair_share = BLK * BLK // wide_count
    cross = cross.reshape(tiles, 2 * group, BLK * BLK // pair_share, pair_share)
    cross = jnp.transpose(cross, (0, 2, 3, 1))

    slot_ids = jnp.arange(SLOTS, dtype=jnp.int32)
    owner_ids = jnp.arange(narrow_count, dtype=jnp.int32)
    owned_all = tile_owners[None, :] == owner_ids[:, None]
    rank_all = jnp.cumsum(owned_all.astype(jnp.int32), axis=1) - 1
    select_all = (owned_all[:, None, :] & (rank_all[:, None, :] == slot_ids[None, :, None])).astype(
        jnp.float32
    )
    send = jnp.einsum("nst,twqv->wnsqv", select_all, cross, precision=lax.Precision.HIGHEST)
    send = send.reshape(devices, SLOTS * pair_share * 2 * group)
    arrived = lax.all_to_all(send, ("wide", "narrow"), 0, 0, tiled=True)
    arrived = arrived.reshape(devices, SLOTS * pair_share, 2, group)
    arrived = jnp.transpose(arrived, (1, 2, 0, 3)).reshape(SLOTS * pair_share, 2, NBINS)
    stacked = lag_transform(arrived, NFFT, LAGS, window_total)
    return stacked.reshape(SLOTS, pair_share, LAGS)


def solution(mesh):
    in_specs = (P(("wide", "narrow"), None, None), P(), P(), P())
    out_specs = P("narrow", "wide", None)
    return jax.shard_map(
        on_device, mesh=mesh, in_specs=in_specs, out_specs=out_specs, check_vma=False
    )
```
